32 devices in a mesh: groups: 2 (over x), ctx: 8 (over z, y), dp: 2 (over core).
Axes of the slice: x: 2, y: 2, z: 4, core: 2. Of those that a mesh axis runs over, the one named last changes fastest.
Arguments:
- hidden_in: bfloat16 [4, 2048, 4608], P(('groups', 'dp'), 'ctx'), parts along dimension 0, may hold values from -6 to 6
- norm_gain: float32 [4608], replicated, may hold values from 0.1 to 1.9
- key_weight: bfloat16 [4608, 1024], P(('ctx', 'dp')), may hold values from -0.09375 to 0.09375
- value_weight: bfloat16 [4608, 1024], P(('ctx', 'dp')), may hold values from -0.09375 to 0.09375
- queries: bfloat16 [4, 2048, 2048], P(('groups', 'dp'), 'ctx'), parts along dimension 0, may hold values from -64 to 64
- out_grad: bfloat16 [4, 2048, 2048], P(('groups', 'dp'), 'ctx'), parts along dimension 0, may hold values from -96 to 96
Outputs:
- hidden_grad: bfloat16 [4, 2048, 4608], P(('groups', 'dp'), 'ctx'), parts along dimension 0
- query_gradient: bfloat16 [4, 2048, 2048], P(('groups', 'dp'), 'ctx'), parts along dimension 0
- key_weight_grad: float32 [9216, 1024], P(('groups', 'ctx', 'dp')), parts along dimension 0
- value_weight_grad: float32 [9216, 1024], P(('groups', 'ctx', 'dp')), parts along dimension 0
- gain_grad: float32 [9216], P(('groups', 'ctx', 'dp')), parts along dimension 0
The draws below stay inside these ranges and needn't reach their ends.
There are 2 independent parts, one for each index of `groups`. The reference program is written for one: setup_inputs(seed, part) draws one part's arguments, and reference() takes and returns one part's arrays. A program takes and returns all parts, laid end to end along the dimension named above; an argument that names none is the same for every part. Nothing has to cross between parts.
All inputs are finite; a program needn't handle non-finite values.
Results may differ from the reference program's by a relative error of at most 0.023.
The reference program's roundings to bfloat16 on the way count: a program that leaves them out, or rounds other values in their place, can miss the bound.
Values may be sent and summed in bfloat16 or wider, within the bound.
No kernel may reach another device: no remote copies, remote signals or barrier semaphores. Data moves between devices by JAX's collectives and lax.ppermute only.
A program may use at most 192 MiB of HBM per device.

```python
import jax
import jax.numpy as jnp
from jax import lax

D = 4608
HEADS = 16
KV_HEADS = 8
HEAD_DIM = 128
TOK_DEV = 256
QW = 2048
KVW = 1024
WINDOW = 256
LEN = 2048
SEQS = 2
N_CTX = 8


def draw_queries(key, part):
    base_key = jax.random.fold_in(jax.random.fold_in(key, 17), 0)
    drawn = jnp.clip(jax.random.normal(base_key, (SEQS, LEN, HEADS, HEAD_DIM), jnp.float32), -6.0, 6.0)
    return drawn.reshape(SEQS, LEN, HEADS * HEAD_DIM).astype(jnp.bfloat16)


def spiked(array, own_key, source, target, shards_of, factor):
    owner, partner = [(jnp.arange(array.shape[axis_at]) // (array.shape[axis_at] // shards_of)).reshape([-1 if axis == axis_at else 1 for axis in range(array.ndim)]) for axis_at in (source, target)]
    chosen = jax.random.permutation(own_key, shards_of)[partner]
    strong = (owner == chosen) | (owner == (partner + shards_of // 2) % shards_of)
    return jnp.where(strong, factor * array, array)


def steps_of(rng, shape, cuts, smallest, largest):
    loudness, own = 1.0, jax.random.fold_in(rng, 6)
    for dim, shards_of in cuts:
        draws = jnp.exp(jax.random.uniform(jax.random.fold_in(own, dim), (shards_of,), jnp.float32, smallest / len(cuts), largest / len(cuts)))
        loudness = loudness * jnp.repeat(draws, shape[dim] // shards_of).reshape([-1 if axis == dim else 1 for axis in range(len(shape))])
    return loudness


def scatter_about(rng, shape, deviation, bound, cuts=(), kind=jnp.bfloat16):
    entries = deviation * jax.random.normal(rng, shape, jnp.float32)
    if cuts:
        entries = entries * steps_of(rng, shape, cuts, -0.22, 0.18)
    return jnp.clip(entries, -bound, bound).astype(kind)


def heavy_noise(key, shape, scale, limit, cuts, heavy, held_as=jnp.bfloat16):
    array = scale * jax.random.normal(key, shape, jnp.float32)
    if cuts:
        array = array * steps_of(key, shape, cuts, -0.22, 0.18)
    return jnp.clip(spiked(array, jax.random.fold_in(key, 3), *heavy), -limit, limit).astype(held_as)


def setup_inputs(seed: int = 0, part: int = 0) -> dict:
    splits = jax.random.split(jax.random.key(seed), 7)
    own_keys = jax.random.split(jax.random.fold_in(splits[6], part), 7)
    return {
        "hidden_in": heavy_noise(own_keys[0], (SEQS, LEN, D), 1.0, 6.0, ((0, 2), (1, 8)), (1, 2, 8, 2.0)),
        "norm_gain": jnp.clip(1.0 + 0.18 * jax.random.normal(splits[1], (D,), jnp.float32), 0.1, 1.9),
        "key_weight": scatter_about(splits[2], (D, KVW), D ** -0.5, 0.09375, ((0, 16),)),
        "value_weight": scatter_about(splits[3], (D, KVW), D ** -0.5, 0.09375, ((0, 16),)),
        "queries": draw_queries(jax.random.fold_in(jax.random.fold_in(splits[6], part), 71), part),
        "out_grad": scatter_about(own_keys[5], (SEQS, LEN, QW), 16.0, 96.0, ((0, 2), (1, 8))),
    }


score_scale = 1.0 / 12.0
grad_scale = 1.0 / 64.0
norm_eps = 1e-06
rope_base = 10000.0
masked_score = -1e+30

def round_low(values_in):
    return lax.optimization_barrier(values_in.astype(jnp.bfloat16)).astype(jnp.float32)

def rotation(positions):
    half_dim = HEAD_DIM // 2
    frequency = rope_base ** (-jnp.arange(half_dim, dtype=jnp.float32) / half_dim)
    angles = positions.astype(jnp.float32)[:, None] * frequency[None, :]
    return (jnp.cos(angles)[:, None, :], jnp.sin(angles)[:, None, :])

def rotate(tensor, cosine_table, sine_table):
    half_dim = HEAD_DIM // 2
    front_half = tensor[..., :half_dim]
    back_half = tensor[..., half_dim:]
    return jnp.concatenate([front_half * cosine_table - back_half * sine_table, back_half * cosine_table + front_half * sine_table], axis=-1)

def rotate_back(tensor, cosine_table, sine_table):
    half_dim = HEAD_DIM // 2
    front_half = tensor[..., :half_dim]
    back_half = tensor[..., half_dim:]
    return jnp.concatenate([front_half * cosine_table + back_half * sine_table, back_half * cosine_table - front_half * sine_table], axis=-1)

def tile_masks(has_prev):
    row_index = jnp.arange(TOK_DEV)[:, None]
    col_index = jnp.arange(TOK_DEV)[None, :]
    near_mask = (col_index <= row_index) & (row_index - col_index < WINDOW)
    far_mask = (col_index > row_index + TOK_DEV - WINDOW) & has_prev
    return (near_mask, far_mask)

def block_backward(query_block, grad_block, nearby_keys, near_values, distant_keys, far_values, has_prev):
    group_size = HEADS // KV_HEADS
    query_head_split = query_block.astype(jnp.float32).reshape(TOK_DEV, KV_HEADS, group_size, HEAD_DIM)
    gradient_heads = grad_block.astype(jnp.float32).reshape(TOK_DEV, KV_HEADS, group_size, HEAD_DIM)
    near_mask, far_mask = tile_masks(has_prev)

    def pair_products(leftover_heads, key_row_block):
        return jnp.einsum('qbak,wbk->baqw', leftover_heads, key_row_block.astype(jnp.float32))
    near_scores = jnp.where(near_mask, pair_products(query_head_split, nearby_keys) * score_scale, masked_score)
    far_scores = jnp.where(far_mask, pair_products(query_head_split, distant_keys) * score_scale, masked_score)
    row_top = jnp.maximum(lax.optimization_barrier(jnp.max(near_scores, -1)), lax.optimization_barrier(jnp.max(far_scores, -1)))[..., None]
    near_exp = jnp.where(near_mask, jnp.exp(near_scores - row_top), 0.0)
    far_exp = jnp.where(far_mask, jnp.exp(far_scores - row_top), 0.0)
    row_total = (lax.optimization_barrier(jnp.sum(near_exp, -1)) + lax.optimization_barrier(jnp.sum(far_exp, -1)))[..., None]
    near_probs = near_exp / row_total
    far_probs = far_exp / row_total
    near_dprobs = pair_products(gradient_heads, near_values)
    far_dprobs = pair_products(gradient_heads, far_values)
    weighted = (lax.optimization_barrier(jnp.sum(near_probs * near_dprobs, -1)) + lax.optimization_barrier(jnp.sum(far_probs * far_dprobs, -1)))[..., None]
    nearby_score_gradient = round_low(near_probs * (near_dprobs - weighted) * score_scale)
    distant_score_gradient = round_low(far_probs * (far_dprobs - weighted) * score_scale)
    nearby_reduced = round_low(near_probs)
    distant_reduced = round_low(far_probs)
    query_gradient = jnp.einsum('xqwc,cxi->wxqi', nearby_score_gradient, nearby_keys.astype(jnp.float32)) + jnp.einsum('xqwc,cxi->wxqi', distant_score_gradient, distant_keys.astype(jnp.float32))
    nearby_key = jnp.einsum('woia,iwon->awn', nearby_score_gradient, query_head_split)
    distant_key = jnp.einsum('woia,iwon->awn', distant_score_gradient, query_head_split)
    nearby_value = jnp.einsum('woia,iwon->awn', nearby_reduced, gradient_heads)
    distant_value = jnp.einsum('woia,iwon->awn', distant_reduced, gradient_heads)
    query_out = query_gradient.reshape(TOK_DEV, HEADS * HEAD_DIM).astype(jnp.bfloat16)
    return (query_out, nearby_key, nearby_value, distant_key, distant_value)

def reference(hidden_in, norm_gain, key_weight, value_weight, queries, out_grad):
    kv_width = KV_HEADS * HEAD_DIM
    block_count = SEQS * N_CTX
    inputs = hidden_in.astype(jnp.float32)
    inverse = lax.rsqrt(lax.optimization_barrier(jnp.mean(inputs * inputs, axis=-1, keepdims=True)) + norm_eps)
    normed = (inputs * inverse * norm_gain).astype(jnp.bfloat16)
    flat_normed = normed.reshape(SEQS * LEN, D)
    keys_raw = jnp.dot(flat_normed, key_weight, preferred_element_type=jnp.float32).reshape(SEQS, LEN, KV_HEADS, HEAD_DIM)
    values = jnp.dot(flat_normed, value_weight, preferred_element_type=jnp.float32).astype(jnp.bfloat16)
    values = values.reshape(SEQS, N_CTX, TOK_DEV, KV_HEADS, HEAD_DIM)
    cosine_table, sine_table = rotation(jnp.arange(LEN))
    keys = rotate(keys_raw, cosine_table, sine_table).astype(jnp.bfloat16).reshape(SEQS, N_CTX, TOK_DEV, KV_HEADS, HEAD_DIM)
    prev_keys = jnp.concatenate([jnp.zeros_like(keys[:, :1]), keys[:, :-1]], axis=1)
    prev_values = jnp.concatenate([jnp.zeros_like(values[:, :1]), values[:, :-1]], axis=1)
    has_prev = jnp.broadcast_to(jnp.arange(N_CTX)[None, :] > 0, (SEQS, N_CTX)).reshape(block_count)
    block_shape = (block_count, TOK_DEV, KV_HEADS, HEAD_DIM)

    def one_block(pieces):
        return block_backward(*pieces)
    query_blocks, nearby_key, nearby_value, distant_key, distant_value = lax.map(one_block, (queries.reshape(block_count, TOK_DEV, HEADS * HEAD_DIM), out_grad.reshape(block_count, TOK_DEV, HEADS * HEAD_DIM), keys.reshape(block_shape), values.reshape(block_shape), prev_keys.reshape(block_shape), prev_values.reshape(block_shape), has_prev))

    def arrive(far_part):
        lowered = round_low(far_part.reshape(SEQS, N_CTX, TOK_DEV, KV_HEADS, HEAD_DIM))
        return jnp.concatenate([lowered[:, 1:], jnp.zeros_like(lowered[:, :1])], axis=1)
    key_grad = nearby_key.reshape(SEQS, N_CTX, TOK_DEV, KV_HEADS, HEAD_DIM) + arrive(distant_key)
    value_grad = nearby_value.reshape(SEQS, N_CTX, TOK_DEV, KV_HEADS, HEAD_DIM) + arrive(distant_value)
    key_grad_raw = rotate_back(key_grad.reshape(SEQS, LEN, KV_HEADS, HEAD_DIM), cosine_table, sine_table)
    key_grad_raw = key_grad_raw.astype(jnp.bfloat16).reshape(SEQS * LEN, kv_width)
    value_low = value_grad.astype(jnp.bfloat16).reshape(SEQS * LEN, kv_width)

    def add_block(running, pieces):
        normed_block, key_block, value_block = pieces
        key_term = round_low(jnp.dot(normed_block.T, key_block, preferred_element_type=jnp.float32) * grad_scale)
        value_term = round_low(jnp.dot(normed_block.T, value_block, preferred_element_type=jnp.float32) * grad_scale)
        return ((running[0] + key_term, running[1] + value_term), None)
    start_sums = (jnp.zeros((D, kv_width), jnp.float32), jnp.zeros((D, kv_width), jnp.float32))
    weight_sums, unused = lax.scan(add_block, start_sums, (flat_normed.reshape(block_count, TOK_DEV, D), key_grad_raw.reshape(block_count, TOK_DEV, kv_width), value_low.reshape(block_count, TOK_DEV, kv_width)))
    normed_grad = jnp.dot(key_grad_raw, key_weight.T, preferred_element_type=jnp.float32)
    normed_grad = normed_grad + jnp.dot(value_low, value_weight.T, preferred_element_type=jnp.float32)
    normed_grad = normed_grad.reshape(SEQS, LEN, D)
    scaled = normed_grad * norm_gain
    cubed = inverse * inverse * inverse
    hidden_grad = (inverse * scaled - inputs * cubed * lax.optimization_barrier(jnp.mean(scaled * inputs, axis=-1, keepdims=True))).astype(jnp.bfloat16)
    gain_grad = lax.optimization_barrier(jnp.sum((normed_grad * inputs * inverse).reshape(SEQS * LEN, D), axis=0)) * grad_scale
    query_gradient = query_blocks.reshape(SEQS, LEN, HEADS * HEAD_DIM)
    return (hidden_grad, query_gradient, weight_sums[0], weight_sums[1], gain_grad)
```

```python
import jax
import jax.numpy as jnp
from jax import lax
from jax.sharding import PartitionSpec as P

HEADS = 16
KV_HEADS = 8
HEAD_DIM = 128
WINDOW = 256


score_scale = 1.0 / 12.0
grad_scale = 1.0 / 64.0
norm_eps = 1e-06
rope_base = 10000.0
masked_score = -1e30


def from_behind(value, axis, steps):
    count = lax.axis_size(axis)
    initial, last = (max(0, -steps), min(count, count - steps))
    return lax.ppermute(value, axis, [(source, source + steps) for source in range(initial, last)])


def rotation(positions):
    half_dim = HEAD_DIM // 2
    frequency = rope_base ** (-jnp.arange(half_dim, dtype=jnp.float32) / half_dim)
    angles = positions.astype(jnp.float32)[:, None] * frequency[None, :]
    return (jnp.cos(angles)[:, None, :], jnp.sin(angles)[:, None, :])


def rotate(tensor, cosine_table, sine_table):
    half_dim = HEAD_DIM // 2
    front_half = tensor[..., :half_dim]
    back_half = tensor[..., half_dim:]
    return jnp.concatenate(
        [
            front_half * cosine_table - back_half * sine_table,
            back_half * cosine_table + front_half * sine_table,
        ],
        axis=-1,
    )


def rotate_back(tensor, cosine_table, sine_table):
    half_dim = HEAD_DIM // 2
    front_half = tensor[..., :half_dim]
    back_half = tensor[..., half_dim:]
    return jnp.concatenate(
        [
            front_half * cosine_table + back_half * sine_table,
            back_half * cosine_table - front_half * sine_table,
        ],
        axis=-1,
    )


def block_backward(
    query_block, grad_block, nearby_keys, near_values, distant_keys, far_values, has_prev
):
    tok_rows = query_block.shape[0]
    group_size = HEADS // KV_HEADS
    query_head_split = query_block.reshape(tok_rows, KV_HEADS, group_size, HEAD_DIM)
    gradient_heads = grad_block.reshape(tok_rows, KV_HEADS, group_size, HEAD_DIM)
    row_index = jnp.arange(tok_rows)[:, None]
    col_index = jnp.arange(tok_rows)[None, :]
    near_mask = (col_index <= row_index) & (row_index - col_index < WINDOW)
    far_mask = (col_index > row_index + tok_rows - WINDOW) & has_prev

    def pair_products(leftover_heads, key_row_block):
        return jnp.einsum(
            "qbak,wbk->baqw", leftover_heads, key_row_block, preferred_element_type=jnp.float32
        )

    near_scores = jnp.where(
        near_mask, pair_products(query_head_split, nearby_keys) * score_scale, masked_score
    )
    far_scores = jnp.where(
        far_mask, pair_products(query_head_split, distant_keys) * score_scale, masked_score
    )
    row_top = jnp.maximum(jnp.max(near_scores, -1), jnp.max(far_scores, -1))[..., None]
    near_exp = jnp.where(near_mask, jnp.exp(near_scores - row_top), 0.0)
    far_exp = jnp.where(far_mask, jnp.exp(far_scores - row_top), 0.0)
    row_total = (jnp.sum(near_exp, -1) + jnp.sum(far_exp, -1))[..., None]
    near_probs = near_exp / row_total
    far_probs = far_exp / row_total
    near_dprobs = pair_products(gradient_heads, near_values)
    far_dprobs = pair_products(gradient_heads, far_values)
    weighted = (jnp.sum(near_probs * near_dprobs, -1) + jnp.sum(far_probs * far_dprobs, -1))[
        ..., None
    ]
    nearby_score_gradient = (near_probs * (near_dprobs - weighted) * score_scale).astype(
        jnp.bfloat16
    )
    distant_score_gradient = (far_probs * (far_dprobs - weighted) * score_scale).astype(
        jnp.bfloat16
    )
    nearby_reduced = near_probs.astype(jnp.bfloat16)
    distant_reduced = far_probs.astype(jnp.bfloat16)
    query_gradient = jnp.einsum(
        "xqwc,cxi->wxqi", nearby_score_gradient, nearby_keys, preferred_element_type=jnp.float32
    )
    query_gradient = query_gradient + jnp.einsum(
        "xqwc,cxi->wxqi", distant_score_gradient, distant_keys, preferred_element_type=jnp.float32
    )
    nearby_key = jnp.einsum(
        "woia,iwon->awn",
        nearby_score_gradient,
        query_head_split,
        preferred_element_type=jnp.float32,
    )
    distant_key = jnp.einsum(
        "woia,iwon->awn",
        distant_score_gradient,
        query_head_split,
        preferred_element_type=jnp.float32,
    )
    nearby_value = jnp.einsum(
        "woia,iwon->awn", nearby_reduced, gradient_heads, preferred_element_type=jnp.float32
    )
    distant_value = jnp.einsum(
        "woia,iwon->awn", distant_reduced, gradient_heads, preferred_element_type=jnp.float32
    )
    query_out = query_gradient.reshape(tok_rows, HEADS * HEAD_DIM).astype(jnp.bfloat16)
    return (query_out, nearby_key, nearby_value, distant_key, distant_value)


def body(hidden_in, norm_gain, key_weight, value_weight, queries, out_grad):
    tok_rows = hidden_in.shape[1]
    key_width = key_weight.shape[1]
    inputs = hidden_in[0].astype(jnp.float32)
    inverse = lax.rsqrt(jnp.mean(inputs * inputs, axis=-1, keepdims=True) + norm_eps)
    normed = (inputs * inverse * norm_gain).astype(jnp.bfloat16)
    n_ctx = lax.axis_size("ctx")
    n_dp = lax.axis_size("dp")
    model_width = normed.shape[1]
    shard_rows = model_width // (n_ctx * n_dp)

    def to_dp_major(rows):
        lead = rows.shape[:-1]
        split = rows.reshape(lead + (n_ctx, n_dp, shard_rows))
        return jnp.swapaxes(split, -3, -2).reshape(lead + (model_width,))

    def from_dp_major(rows):
        lead = rows.shape[:-1]
        split = rows.reshape(lead + (n_dp, n_ctx, shard_rows))
        return jnp.swapaxes(split, -3, -2).reshape(lead + (model_width,))

    def gather_rows(weight):
        by_ctx = lax.all_gather(weight, "ctx", axis=0, tiled=True)
        return lax.all_gather(by_ctx, "dp", axis=0, tiled=True)

    full_key, full_value = gather_rows(key_weight), gather_rows(value_weight)
    normed_perm = to_dp_major(normed)
    key_raw = jnp.dot(normed_perm, full_key, preferred_element_type=jnp.float32)
    value_rows = jnp.dot(normed_perm, full_value, preferred_element_type=jnp.float32).astype(
        jnp.bfloat16
    )
    ctx_index = lax.axis_index("ctx")
    positions = ctx_index * tok_rows + jnp.arange(tok_rows, dtype=jnp.int32)
    cosine_table, sine_table = rotation(positions)
    key_row_block = rotate(key_raw.reshape(tok_rows, KV_HEADS, HEAD_DIM), cosine_table, sine_table)
    key_row_block = key_row_block.astype(jnp.bfloat16).reshape(tok_rows, key_width)
    prev_key, prev_value = from_behind((key_row_block, value_rows), "ctx", 1)
    head_shape = (tok_rows, KV_HEADS, HEAD_DIM)
    query_gradient, nearby_key, nearby_value, distant_key, distant_value = block_backward(
        queries[0],
        out_grad[0],
        key_row_block.reshape(head_shape),
        value_rows.reshape(head_shape),
        prev_key.reshape(head_shape),
        prev_value.reshape(head_shape),
        ctx_index > 0,
    )
    incoming_key, incoming_value = from_behind(
        (distant_key.astype(jnp.bfloat16), distant_value.astype(jnp.bfloat16)), "ctx", -1
    )
    key_grad = nearby_key + incoming_key.astype(jnp.float32)
    value_grad = nearby_value + incoming_value.astype(jnp.float32)
    key_grad_raw = (
        rotate_back(key_grad, cosine_table, sine_table)
        .astype(jnp.bfloat16)
        .reshape(tok_rows, key_width)
    )
    value_low = value_grad.astype(jnp.bfloat16).reshape(tok_rows, key_width)
    key_part = jnp.einsum(
        "td,tk->dk", normed_perm, key_grad_raw, preferred_element_type=jnp.float32
    )
    value_part = jnp.einsum(
        "td,tk->dk", normed_perm, value_low, preferred_element_type=jnp.float32
    )
    terms = (jnp.concatenate([key_part, value_part], axis=1) * grad_scale).astype(jnp.bfloat16)
    terms = lax.psum_scatter(terms, "dp", scatter_dimension=0, tiled=True)
    stacked = lax.psum_scatter(terms, "ctx", scatter_dimension=0, tiled=True).astype(jnp.float32)
    key_weight_grad = stacked[:, :key_width]
    value_weight_grad = stacked[:, key_width:]
    normed_grad = jnp.einsum(
        "tk,dk->td", key_grad_raw, full_key, preferred_element_type=jnp.float32
    )
    normed_grad = normed_grad + jnp.einsum(
        "tk,dk->td", value_low, full_value, preferred_element_type=jnp.float32
    )
    normed_grad = from_dp_major(normed_grad)
    scaled = normed_grad * norm_gain
    cubed = inverse * inverse * inverse
    hidden_grad = (
        inverse * scaled - inputs * cubed * jnp.mean(scaled * inputs, axis=-1, keepdims=True)
    ).astype(jnp.bfloat16)
    gain_term = jnp.sum(normed_grad * inputs * inverse, axis=0) * grad_scale
    gain_term = lax.psum_scatter(to_dp_major(gain_term), "dp", scatter_dimension=0, tiled=True)
    gain_grad = lax.psum_scatter(gain_term, "ctx", scatter_dimension=0, tiled=True)
    return (hidden_grad[None], query_gradient[None], key_weight_grad, value_weight_grad, gain_grad)


def solution(mesh):
    return jax.shard_map(
        body,
        mesh=mesh,
        in_specs=(
            P(("groups", "dp"), "ctx", None),
            P(),
            P(("ctx", "dp"), None),
            P(("ctx", "dp"), None),
            P(("groups", "dp"), "ctx", None),
            P(("groups", "dp"), "ctx", None),
        ),
        out_specs=(
            P(("groups", "dp"), "ctx", None),
            P(("groups", "dp"), "ctx", None),
            P(("groups", "ctx", "dp"), None),
            P(("groups", "ctx", "dp"), None),
            P(("groups", "ctx", "dp")),
        ),
        check_vma=False,
    )
```

```python
import jax
import jax.numpy as jnp
from jax import lax
from jax.sharding import PartitionSpec as P

HEADS = 16
KV_HEADS = 8
HEAD_DIM = 128
WINDOW = 256


score_scale = 1.0 / 12.0
grad_scale = 1.0 / 64.0
norm_eps = 1e-06
rope_base = 10000.0
masked_score = -1e30


def from_behind(value, axis, steps):
    count = lax.axis_size(axis)
    initial, last = (max(0, -steps), min(count, count - steps))
    return lax.ppermute(value, axis, [(source, source + steps) for source in range(initial, last)])


def rotation(positions):
    half_dim = HEAD_DIM // 2
    frequency = rope_base ** (-jnp.arange(half_dim, dtype=jnp.float32) / half_dim)
    angles = positions.astype(jnp.float32)[:, None] * frequency[None, :]
    return (jnp.cos(angles)[:, None, :], jnp.sin(angles)[:, None, :])


def rotate(tensor, cosine_table, sine_table):
    half_dim = HEAD_DIM // 2
    front_half = tensor[..., :half_dim]
    back_half = tensor[..., half_dim:]
    return jnp.concatenate(
        [
            front_half * cosine_table - back_half * sine_table,
            back_half * cosine_table + front_half * sine_table,
        ],
        axis=-1,
    )


def rotate_back(tensor, cosine_table, sine_table):
    half_dim = HEAD_DIM // 2
    front_half = tensor[..., :half_dim]
    back_half = tensor[..., half_dim:]
    return jnp.concatenate(
        [
            front_half * cosine_table + back_half * sine_table,
            back_half * cosine_table - front_half * sine_table,
        ],
        axis=-1,
    )


def block_backward(
    query_block, grad_block, nearby_keys, near_values, distant_keys, far_values, has_prev
):
    tok_rows = query_block.shape[0]
    group_size = HEADS // KV_HEADS
    query_head_split = query_block.reshape(tok_rows, KV_HEADS, group_size, HEAD_DIM)
    gradient_heads = grad_block.reshape(tok_rows, KV_HEADS, group_size, HEAD_DIM)
    row_index = jnp.arange(tok_rows)[:, None]
    col_index = jnp.arange(tok_rows)[None, :]
    near_mask = (col_index <= row_index) & (row_index - col_index < WINDOW)
    far_mask = (col_index > row_index + tok_rows - WINDOW) & has_prev

    def pair_products(leftover_heads, key_row_block):
        return jnp.einsum(
            "qbak,wbk->baqw", leftover_heads, key_row_block, preferred_element_type=jnp.float32
        )

    near_scores = jnp.where(
        near_mask, pair_products(query_head_split, nearby_keys) * score_scale, masked_score
    )
    far_scores = jnp.where(
        far_mask, pair_products(query_head_split, distant_keys) * score_scale, masked_score
    )
    row_top = jnp.maximum(jnp.max(near_scores, -1), jnp.max(far_scores, -1))[..., None]
    near_exp = jnp.where(near_mask, jnp.exp(near_scores - row_top), 0.0)
    far_exp = jnp.where(far_mask, jnp.exp(far_scores - row_top), 0.0)
    row_total = (jnp.sum(near_exp, -1) + jnp.sum(far_exp, -1))[..., None]
    near_probs = near_exp / row_total
    far_probs = far_exp / row_total
    near_dprobs = pair_products(gradient_heads, near_values)
    far_dprobs = pair_products(gradient_heads, far_values)
    weighted = (jnp.sum(near_probs * near_dprobs, -1) + jnp.sum(far_probs * far_dprobs, -1))[
        ..., None
    ]
    nearby_score_gradient = (near_probs * (near_dprobs - weighted) * score_scale).astype(
        jnp.bfloat16
    )
    distant_score_gradient = (far_probs * (far_dprobs - weighted) * score_scale).astype(
        jnp.bfloat16
    )
    nearby_reduced = near_probs.astype(jnp.bfloat16)
    distant_reduced = far_probs.astype(jnp.bfloat16)
    query_gradient = jnp.einsum(
        "xqwc,cxi->wxqi", nearby_score_gradient, nearby_keys, preferred_element_type=jnp.float32
    )
    query_gradient = query_gradient + jnp.einsum(
        "xqwc,cxi->wxqi", distant_score_gradient, distant_keys, preferred_element_type=jnp.float32
    )
    nearby_key = jnp.einsum(
        "woia,iwon->awn",
        nearby_score_gradient,
        query_head_split,
        preferred_element_type=jnp.float32,
    )
    distant_key = jnp.einsum(
        "woia,iwon->awn",
        distant_score_gradient,
        query_head_split,
        preferred_element_type=jnp.float32,
    )
    nearby_value = jnp.einsum(
        "woia,iwon->awn", nearby_reduced, gradient_heads, preferred_element_type=jnp.float32
    )
    distant_value = jnp.einsum(
        "woia,iwon->awn", distant_reduced, gradient_heads, preferred_element_type=jnp.float32
    )
    query_out = query_gradient.reshape(tok_rows, HEADS * HEAD_DIM).astype(jnp.bfloat16)
    return (query_out, nearby_key, nearby_value, distant_key, distant_value)


def body(hidden_in, norm_gain, key_weight, value_weight, queries, out_grad):
    tok_rows = hidden_in.shape[1]
    key_width = key_weight.shape[1]
    inputs = hidden_in[0].astype(jnp.float32)
    inverse = lax.rsqrt(jnp.mean(inputs * inputs, axis=-1, keepdims=True) + norm_eps)
    normed = (inputs * inverse * norm_gain).astype(jnp.bfloat16)
    n_groups = lax.axis_size("groups")
    group_index = lax.axis_index("groups")

    def gather_rows(weight):
        pieces = weight.reshape(n_groups, weight.shape[0] // n_groups, weight.shape[1])
        return lax.all_gather(pieces[group_index], ("ctx", "dp", "groups"), axis=0, tiled=True)

    full_key, full_value = gather_rows(key_weight), gather_rows(value_weight)
    key_raw = jnp.dot(normed, full_key, preferred_element_type=jnp.float32)
    value_rows = jnp.dot(normed, full_value, preferred_element_type=jnp.float32).astype(
        jnp.bfloat16
    )
    ctx_index = lax.axis_index("ctx")
    positions = ctx_index * tok_rows + jnp.arange(tok_rows, dtype=jnp.int32)
    cosine_table, sine_table = rotation(positions)
    key_row_block = rotate(key_raw.reshape(tok_rows, KV_HEADS, HEAD_DIM), cosine_table, sine_table)
    key_row_block = key_row_block.astype(jnp.bfloat16).reshape(tok_rows, key_width)
    prev_key, prev_value = from_behind((key_row_block, value_rows), "ctx", 1)
    head_shape = (tok_rows, KV_HEADS, HEAD_DIM)
    query_gradient, nearby_key, nearby_value, distant_key, distant_value = block_backward(
        queries[0],
        out_grad[0],
        key_row_block.reshape(head_shape),
        value_rows.reshape(head_shape),
        prev_key.reshape(head_shape),
        prev_value.reshape(head_shape),
        ctx_index > 0,
    )
    incoming_key, incoming_value = from_behind(
        (distant_key.astype(jnp.bfloat16), distant_value.astype(jnp.bfloat16)), "ctx", -1
    )
    key_grad = nearby_key + incoming_key.astype(jnp.float32)
    value_grad = nearby_value + incoming_value.astype(jnp.float32)
    key_grad_raw = (
        rotate_back(key_grad, cosine_table, sine_table)
        .astype(jnp.bfloat16)
        .reshape(tok_rows, key_width)
    )
    value_low = value_grad.astype(jnp.bfloat16).reshape(tok_rows, key_width)
    n_blocks = lax.axis_size("ctx") * lax.axis_size("dp")
    shard_rows = normed.shape[1] // n_blocks
    normed_cols = jnp.swapaxes(normed.reshape(tok_rows, n_blocks, shard_rows), 0, 1)
    normed_cols = lax.all_to_all(normed_cols, ("ctx", "dp"), 0, 0, tiled=True)
    grads_low = lax.all_gather(
        jnp.concatenate([key_grad_raw, value_low], axis=1), ("ctx", "dp"), axis=0
    )
    block_terms = jnp.einsum(
        "btd,btk->bdk", normed_cols, grads_low, preferred_element_type=jnp.float32
    )
    stacked = (block_terms * grad_scale).astype(jnp.bfloat16).astype(jnp.float32).sum(0)
    key_weight_grad = stacked[:, :key_width]
    value_weight_grad = stacked[:, key_width:]
    normed_grad = jnp.einsum(
        "tk,dk->td", key_grad_raw, full_key, preferred_element_type=jnp.float32
    )
    normed_grad = normed_grad + jnp.einsum(
        "tk,dk->td", value_low, full_value, preferred_element_type=jnp.float32
    )
    scaled = normed_grad * norm_gain
    cubed = inverse * inverse * inverse
    hidden_grad = (
        inverse * scaled - inputs * cubed * jnp.mean(scaled * inputs, axis=-1, keepdims=True)
    ).astype(jnp.bfloat16)
    gain_term = jnp.sum(normed_grad * inputs * inverse, axis=0) * grad_scale
    gain_grad = lax.psum_scatter(gain_term, ("ctx", "dp"), scatter_dimension=0, tiled=True)
    return (hidden_grad[None], query_gradient[None], key_weight_grad, value_weight_grad, gain_grad)


def solution(mesh):
    return jax.shard_map(
        body,
        mesh=mesh,
        in_specs=(
            P(("groups", "dp"), "ctx", None),
            P(),
            P(("ctx", "dp"), None),
            P(("ctx", "dp"), None),
            P(("groups", "dp"), "ctx", None),
            P(("groups", "dp"), "ctx", None),
        ),
        out_specs=(
            P(("groups", "dp"), "ctx", None),
            P(("groups", "dp"), "ctx", None),
            P(("groups", "ctx", "dp"), None),
            P(("groups", "ctx", "dp"), None),
            P(("groups", "ctx", "dp")),
        ),
        check_vma=False,
    )
```

```python
import jax
import jax.numpy as jnp
from jax import lax
from jax.sharding import PartitionSpec as P

HEADS = 16
KV_HEADS = 8
HEAD_DIM = 128
WINDOW = 256


score_scale = 1.0 / 12.0
grad_scale = 1.0 / 64.0
norm_eps = 1e-06
rope_base = 10000.0
masked_score = -1e30


def from_behind(value, axis, steps):
    count = lax.axis_size(axis)
    initial, last = (max(0, -steps), min(count, count - steps))
    return lax.ppermute(value, axis, [(source, source + steps) for source in range(initial, last)])


def rotation(positions):
    half_dim = HEAD_DIM // 2
    frequency = rope_base ** (-jnp.arange(half_dim, dtype=jnp.float32) / half_dim)
    angles = positions.astype(jnp.float32)[:, None] * frequency[None, :]
    return (jnp.cos(angles)[:, None, :], jnp.sin(angles)[:, None, :])


def rotate(tensor, cosine_table, sine_table):
    half_dim = HEAD_DIM // 2
    front_half = tensor[..., :half_dim]
    back_half = tensor[..., half_dim:]
    return jnp.concatenate(
        [
            front_half * cosine_table - back_half * sine_table,
            back_half * cosine_table + front_half * sine_table,
        ],
        axis=-1,
    )


def rotate_back(tensor, cosine_table, sine_table):
    half_dim = HEAD_DIM // 2
    front_half = tensor[..., :half_dim]
    back_half = tensor[..., half_dim:]
    return jnp.concatenate(
        [
            front_half * cosine_table + back_half * sine_table,
            back_half * cosine_table - front_half * sine_table,
        ],
        axis=-1,
    )


def block_backward(
    query_block, grad_block, nearby_keys, near_values, distant_keys, far_values, has_prev
):
    tok_rows = query_block.shape[0]
    group_size = HEADS // KV_HEADS
    query_head_split = query_block.reshape(tok_rows, KV_HEADS, group_size, HEAD_DIM)
    gradient_heads = grad_block.reshape(tok_rows, KV_HEADS, group_size, HEAD_DIM)
    row_index = jnp.arange(tok_rows)[:, None]
    col_index = jnp.arange(tok_rows)[None, :]
    near_mask = (col_index <= row_index) & (row_index - col_index < WINDOW)
    far_mask = (col_index > row_index + tok_rows - WINDOW) & has_prev

    def pair_products(leftover_heads, key_row_block):
        return jnp.einsum(
            "qbak,wbk->baqw", leftover_heads, key_row_block, preferred_element_type=jnp.float32
        )

    near_scores = jnp.where(
        near_mask, pair_products(query_head_split, nearby_keys) * score_scale, masked_score
    )
    far_scores = jnp.where(
        far_mask, pair_products(query_head_split, distant_keys) * score_scale, masked_score
    )
    row_top = jnp.maximum(jnp.max(near_scores, -1), jnp.max(far_scores, -1))[..., None]
    near_exp = jnp.where(near_mask, jnp.exp(near_scores - row_top), 0.0)
    far_exp = jnp.where(far_mask, jnp.exp(far_scores - row_top), 0.0)
    row_total = (jnp.sum(near_exp, -1) + jnp.sum(far_exp, -1))[..., None]
    near_probs = near_exp / row_total
    far_probs = far_exp / row_total
    near_dprobs = pair_products(gradient_heads, near_values)
    far_dprobs = pair_products(gradient_heads, far_values)
    weighted = (jnp.sum(near_probs * near_dprobs, -1) + jnp.sum(far_probs * far_dprobs, -1))[
        ..., None
    ]
    nearby_score_gradient = (near_probs * (near_dprobs - weighted) * score_scale).astype(
        jnp.bfloat16
    )
    distant_score_gradient = (far_probs * (far_dprobs - weighted) * score_scale).astype(
        jnp.bfloat16
    )
    nearby_reduced = near_probs.astype(jnp.bfloat16)
    distant_reduced = far_probs.astype(jnp.bfloat16)
    query_gradient = jnp.einsum(
        "xqwc,cxi->wxqi", nearby_score_gradient, nearby_keys, preferred_element_type=jnp.float32
    )
    query_gradient = query_gradient + jnp.einsum(
        "xqwc,cxi->wxqi", distant_score_gradient, distant_keys, preferred_element_type=jnp.float32
    )
    nearby_key = jnp.einsum(
        "woia,iwon->awn",
        nearby_score_gradient,
        query_head_split,
        preferred_element_type=jnp.float32,
    )
    distant_key = jnp.einsum(
        "woia,iwon->awn",
        distant_score_gradient,
        query_head_split,
        preferred_element_type=jnp.float32,
    )
    nearby_value = jnp.einsum(
        "woia,iwon->awn", nearby_reduced, gradient_heads, preferred_element_type=jnp.float32
    )
    distant_value = jnp.einsum(
        "woia,iwon->awn", distant_reduced, gradient_heads, preferred_element_type=jnp.float32
    )
    query_out = query_gradient.reshape(tok_rows, HEADS * HEAD_DIM).astype(jnp.bfloat16)
    return (query_out, nearby_key, nearby_value, distant_key, distant_value)


def body(hidden_in, norm_gain, key_weight, value_weight, queries, out_grad):
    tok_rows = hidden_in.shape[1]
    key_width = key_weight.shape[1]
    inputs = hidden_in[0].astype(jnp.float32)
    inverse = lax.rsqrt(jnp.mean(inputs * inputs, axis=-1, keepdims=True) + norm_eps)
    normed = (inputs * inverse * norm_gain).astype(jnp.bfloat16)
    n_groups = lax.axis_size("groups")
    group_index = lax.axis_index("groups")

    def gather_rows(weight):
        pieces = weight.reshape(n_groups, weight.shape[0] // n_groups, weight.shape[1])
        return lax.all_gather(pieces[group_index], ("ctx", "dp", "groups"), axis=0, tiled=True)

    def exchange_gather(piece, axes):
        count = 1
        for axis in axes:
            count = count * lax.axis_size(axis)
        copies = jnp.broadcast_to(piece[None], (count,) + piece.shape)
        return lax.all_to_all(copies, axes, 0, 0, tiled=True)

    def exchange_rows(weight):
        pieces = weight.reshape(n_groups, weight.shape[0] // n_groups, weight.shape[1])
        gathered = exchange_gather(pieces[group_index], ("ctx", "dp", "groups"))
        return gathered.reshape(-1, weight.shape[1])

    full_key, full_value = gather_rows(key_weight), exchange_rows(value_weight)
    key_raw = jnp.dot(normed, full_key, preferred_element_type=jnp.float32)
    value_rows = jnp.dot(normed, full_value, preferred_element_type=jnp.float32).astype(
        jnp.bfloat16
    )
    ctx_index = lax.axis_index("ctx")
    positions = ctx_index * tok_rows + jnp.arange(tok_rows, dtype=jnp.int32)
    cosine_table, sine_table = rotation(positions)
    key_row_block = rotate(key_raw.reshape(tok_rows, KV_HEADS, HEAD_DIM), cosine_table, sine_table)
    key_row_block = key_row_block.astype(jnp.bfloat16).reshape(tok_rows, key_width)
    prev_key, prev_value = from_behind((key_row_block, value_rows), "ctx", 1)
    head_shape = (tok_rows, KV_HEADS, HEAD_DIM)
    query_gradient, nearby_key, nearby_value, distant_key, distant_value = block_backward(
        queries[0],
        out_grad[0],
        key_row_block.reshape(head_shape),
        value_rows.reshape(head_shape),
        prev_key.reshape(head_shape),
        prev_value.reshape(head_shape),
        ctx_index > 0,
    )
    incoming_key, incoming_value = from_behind(
        (distant_key.astype(jnp.bfloat16), distant_value.astype(jnp.bfloat16)), "ctx", -1
    )
    key_grad = nearby_key + incoming_key.astype(jnp.float32)
    value_grad = nearby_value + incoming_value.astype(jnp.float32)
    key_grad_raw = (
        rotate_back(key_grad, cosine_table, sine_table)
        .astype(jnp.bfloat16)
        .reshape(tok_rows, key_width)
    )
    value_low = value_grad.astype(jnp.bfloat16).reshape(tok_rows, key_width)
    n_blocks = lax.axis_size("ctx") * lax.axis_size("dp")
    shard_rows = normed.shape[1] // n_blocks
    normed_cols = jnp.swapaxes(normed.reshape(tok_rows, n_blocks, shard_rows), 0, 1)
    normed_cols = lax.all_to_all(normed_cols, ("ctx", "dp"), 0, 0, tiled=True)
    key_grads_low = lax.all_gather(key_grad_raw, ("ctx", "dp"), axis=0)
    value_grads_low = exchange_gather(value_low, ("ctx", "dp"))

    def weight_grad_rows(grads_low):
        block_terms = jnp.einsum(
            "btd,btk->bdk", normed_cols, grads_low, preferred_element_type=jnp.float32
        )
        return (block_terms * grad_scale).astype(jnp.bfloat16).astype(jnp.float32).sum(0)

    stacked = jnp.concatenate(
        [weight_grad_rows(key_grads_low), weight_grad_rows(value_grads_low)], axis=1
    )
    key_weight_grad = stacked[:, :key_width]
    value_weight_grad = stacked[:, key_width:]
    normed_grad = jnp.einsum(
        "tk,dk->td", key_grad_raw, full_key, preferred_element_type=jnp.float32
    )
    normed_grad = normed_grad + jnp.einsum(
        "tk,dk->td", value_low, full_value, preferred_element_type=jnp.float32
    )
    scaled = normed_grad * norm_gain
    cubed = inverse * inverse * inverse
    hidden_grad = (
        inverse * scaled - inputs * cubed * jnp.mean(scaled * inputs, axis=-1, keepdims=True)
    ).astype(jnp.bfloat16)
    gain_term = jnp.sum(normed_grad * inputs * inverse, axis=0) * grad_scale
    gain_pieces = lax.all_to_all(
        gain_term.reshape(n_blocks, shard_rows), ("ctx", "dp"), 0, 0, tiled=True
    )
    gain_grad = jnp.sum(gain_pieces, axis=0)
    return (hidden_grad[None], query_gradient[None], key_weight_grad, value_weight_grad, gain_grad)


def solution(mesh):
    return jax.shard_map(
        body,
        mesh=mesh,
        in_specs=(
            P(("groups", "dp"), "ctx", None),
            P(),
            P(("ctx", "dp"), None),
            P(("ctx", "dp"), None),
            P(("groups", "dp"), "ctx", None),
            P(("groups", "dp"), "ctx", None),
        ),
        out_specs=(
            P(("groups", "dp"), "ctx", None),
            P(("groups", "dp"), "ctx", None),
            P(("groups", "ctx", "dp"), None),
            P(("groups", "ctx", "dp"), None),
            P(("groups", "ctx", "dp")),
        ),
        check_vma=False,
    )
```

```python
import jax
import jax.numpy as jnp
from jax import lax
from jax.sharding import PartitionSpec as P

HEADS = 16
KV_HEADS = 8
HEAD_DIM = 128
WINDOW = 256


score_scale = 1.0 / 12.0
grad_scale = 1.0 / 64.0
norm_eps = 1e-06
rope_base = 10000.0
masked_score = -1e30


def from_behind(value, axis, steps):
    count = lax.axis_size(axis)
    initial, last = (max(0, -steps), min(count, count - steps))
    return lax.ppermute(value, axis, [(source, source + steps) for source in range(initial, last)])


def rotation(positions):
    half_dim = HEAD_DIM // 2
    frequency = rope_base ** (-jnp.arange(half_dim, dtype=jnp.float32) / half_dim)
    angles = positions.astype(jnp.float32)[:, None] * frequency[None, :]
    return (jnp.cos(angles)[:, None, :], jnp.sin(angles)[:, None, :])


def rotate(tensor, cosine_table, sine_table):
    half_dim = HEAD_DIM // 2
    front_half = tensor[..., :half_dim]
    back_half = tensor[..., half_dim:]
    return jnp.concatenate(
        [
            front_half * cosine_table - back_half * sine_table,
            back_half * cosine_table + front_half * sine_table,
        ],
        axis=-1,
    )


def rotate_back(tensor, cosine_table, sine_table):
    half_dim = HEAD_DIM // 2
    front_half = tensor[..., :half_dim]
    back_half = tensor[..., half_dim:]
    return jnp.concatenate(
        [
            front_half * cosine_table + back_half * sine_table,
            back_half * cosine_table - front_half * sine_table,
        ],
        axis=-1,
    )


def block_backward(
    query_block, grad_block, nearby_keys, near_values, distant_keys, far_values, has_prev
):
    tok_rows = query_block.shape[0]
    group_size = HEADS // KV_HEADS
    query_head_split = query_block.reshape(tok_rows, KV_HEADS, group_size, HEAD_DIM)
    gradient_heads = grad_block.reshape(tok_rows, KV_HEADS, group_size, HEAD_DIM)
    row_index = jnp.arange(tok_rows)[:, None]
    col_index = jnp.arange(tok_rows)[None, :]
    near_mask = (col_index <= row_index) & (row_index - col_index < WINDOW)
    far_mask = (col_index > row_index + tok_rows - WINDOW) & has_prev

    def pair_products(leftover_heads, key_row_block):
        return jnp.einsum(
            "qbak,wbk->baqw", leftover_heads, key_row_block, preferred_element_type=jnp.float32
        )

    near_scores = jnp.where(
        near_mask, pair_products(query_head_split, nearby_keys) * score_scale, masked_score
    )
    far_scores = jnp.where(
        far_mask, pair_products(query_head_split, distant_keys) * score_scale, masked_score
    )
    row_top = jnp.maximum(jnp.max(near_scores, -1), jnp.max(far_scores, -1))[..., None]
    near_exp = jnp.where(near_mask, jnp.exp(near_scores - row_top), 0.0)
    far_exp = jnp.where(far_mask, jnp.exp(far_scores - row_top), 0.0)
    row_total = (jnp.sum(near_exp, -1) + jnp.sum(far_exp, -1))[..., None]
    near_probs = near_exp / row_total
    far_probs = far_exp / row_total
    near_dprobs = pair_products(gradient_heads, near_values)
    far_dprobs = pair_products(gradient_heads, far_values)
    weighted = (jnp.sum(near_probs * near_dprobs, -1) + jnp.sum(far_probs * far_dprobs, -1))[
        ..., None
    ]
    nearby_score_gradient = (near_probs * (near_dprobs - weighted) * score_scale).astype(
        jnp.bfloat16
    )
    distant_score_gradient = (far_probs * (far_dprobs - weighted) * score_scale).astype(
        jnp.bfloat16
    )
    nearby_reduced = near_probs.astype(jnp.bfloat16)
    distant_reduced = far_probs.astype(jnp.bfloat16)
    query_gradient = jnp.einsum(
        "xqwc,cxi->wxqi", nearby_score_gradient, nearby_keys, preferred_element_type=jnp.float32
    )
    query_gradient = query_gradient + jnp.einsum(
        "xqwc,cxi->wxqi", distant_score_gradient, distant_keys, preferred_element_type=jnp.float32
    )
    nearby_key = jnp.einsum(
        "woia,iwon->awn",
        nearby_score_gradient,
        query_head_split,
        preferred_element_type=jnp.float32,
    )
    distant_key = jnp.einsum(
        "woia,iwon->awn",
        distant_score_gradient,
        query_head_split,
        preferred_element_type=jnp.float32,
    )
    nearby_value = jnp.einsum(
        "woia,iwon->awn", nearby_reduced, gradient_heads, preferred_element_type=jnp.float32
    )
    distant_value = jnp.einsum(
        "woia,iwon->awn", distant_reduced, gradient_heads, preferred_element_type=jnp.float32
    )
    query_out = query_gradient.reshape(tok_rows, HEADS * HEAD_DIM).astype(jnp.bfloat16)
    return (query_out, nearby_key, nearby_value, distant_key, distant_value)


def ring_order(n_ctx, n_dp):
    if n_ctx % 2 == 0:
        half = n_ctx // 2
        chips = [2 * a for a in range(half)] + [2 * a + 1 for a in reversed(range(half))]
    else:
        chips = list(range(n_ctx))
    return [chip * n_dp + core for chip in chips for core in range(n_dp)]


def ring_gather(piece, axes, ring):
    count = len(ring)
    ahead = [(ring[i], ring[(i + 1) % count]) for i in range(count)]
    behind = [(ring[i], ring[(i - 1) % count]) for i in range(count)]
    n_ahead = count // 2
    from_left, from_right = [], []
    moving = piece
    for _ in range(n_ahead):
        moving = lax.ppermute(moving, axes, ahead)
        from_left.append(moving)
    moving = piece
    for _ in range(count - 1 - n_ahead):
        moving = lax.ppermute(moving, axes, behind)
        from_right.append(moving)
    return jnp.stack([piece] + from_right + from_left[::-1])


def body(hidden_in, norm_gain, key_weight, value_weight, queries, out_grad):
    tok_rows = hidden_in.shape[1]
    key_width = key_weight.shape[1]
    inputs = hidden_in[0].astype(jnp.float32)
    inverse = lax.rsqrt(jnp.mean(inputs * inputs, axis=-1, keepdims=True) + norm_eps)
    normed = (inputs * inverse * norm_gain).astype(jnp.bfloat16)
    n_ctx = lax.axis_size("ctx")
    n_dp = lax.axis_size("dp")
    n_blocks = n_ctx * n_dp
    shard_rows = normed.shape[1] // n_blocks
    ring = ring_order(n_ctx, n_dp)
    ring_pos = [0] * n_blocks
    for place, member in enumerate(ring):
        ring_pos[member] = place
    my_place = jnp.array(ring_pos, jnp.int32)[lax.axis_index("ctx") * n_dp + lax.axis_index("dp")]
    offsets = jnp.arange(n_blocks, dtype=jnp.int32)
    source_of = jnp.array(ring, jnp.int32)[(my_place + offsets) % n_blocks]
    offset_of = (jnp.array(ring_pos, jnp.int32) - my_place) % n_blocks
    weights = ring_gather(
        jnp.concatenate([key_weight, value_weight], axis=1), ("ctx", "dp"), ring
    )
    full_key, full_value = weights[..., :key_width], weights[..., key_width:]
    normed_blocks = jnp.take(normed.reshape(tok_rows, n_blocks, shard_rows), source_of, axis=1)
    key_raw = jnp.einsum(
        "tjr,jrk->tk", normed_blocks, full_key, preferred_element_type=jnp.float32
    )
    value_rows = jnp.einsum(
        "tjr,jrk->tk", normed_blocks, full_value, preferred_element_type=jnp.float32
    ).astype(jnp.bfloat16)
    ctx_index = lax.axis_index("ctx")
    positions = ctx_index * tok_rows + jnp.arange(tok_rows, dtype=jnp.int32)
    cosine_table, sine_table = rotation(positions)
    key_row_block = rotate(key_raw.reshape(tok_rows, KV_HEADS, HEAD_DIM), cosine_table, sine_table)
    key_row_block = key_row_block.astype(jnp.bfloat16).reshape(tok_rows, key_width)
    prev_key, prev_value = from_behind((key_row_block, value_rows), "ctx", 1)
    head_shape = (tok_rows, KV_HEADS, HEAD_DIM)
    query_gradient, nearby_key, nearby_value, distant_key, distant_value = block_backward(
        queries[0],
        out_grad[0],
        key_row_block.reshape(head_shape),
        value_rows.reshape(head_shape),
        prev_key.reshape(head_shape),
        prev_value.reshape(head_shape),
        ctx_index > 0,
    )
    incoming_key, incoming_value = from_behind(
        (distant_key.astype(jnp.bfloat16), distant_value.astype(jnp.bfloat16)), "ctx", -1
    )
    key_grad = nearby_key + incoming_key.astype(jnp.float32)
    value_grad = nearby_value + incoming_value.astype(jnp.float32)
    key_grad_raw = (
        rotate_back(key_grad, cosine_table, sine_table)
        .astype(jnp.bfloat16)
        .reshape(tok_rows, key_width)
    )
    value_low = value_grad.astype(jnp.bfloat16).reshape(tok_rows, key_width)
    normed_cols = jnp.swapaxes(normed.reshape(tok_rows, n_blocks, shard_rows), 0, 1)
    normed_cols = lax.all_to_all(normed_cols, ("ctx", "dp"), 0, 0, tiled=True)
    normed_cols = jnp.take(normed_cols, source_of, axis=0)
    grads_low = ring_gather(
        jnp.concatenate([key_grad_raw, value_low], axis=1), ("ctx", "dp"), ring
    )
    block_terms = jnp.einsum(
        "btd,btk->bdk", normed_cols, grads_low, preferred_element_type=jnp.float32
    )
    stacked = (block_terms * grad_scale).astype(jnp.bfloat16).astype(jnp.float32).sum(0)
    key_weight_grad = stacked[:, :key_width]
    value_weight_grad = stacked[:, key_width:]
    normed_grad = jnp.einsum(
        "tk,jrk->tjr", key_grad_raw, full_key, preferred_element_type=jnp.float32
    )
    normed_grad = normed_grad + jnp.einsum(
        "tk,jrk->tjr", value_low, full_value, preferred_element_type=jnp.float32
    )
    normed_grad = jnp.take(normed_grad, offset_of, axis=1).reshape(tok_rows, -1)
    scaled = normed_grad * norm_gain
    cubed = inverse * inverse * inverse
    hidden_grad = (
        inverse * scaled - inputs * cubed * jnp.mean(scaled * inputs, axis=-1, keepdims=True)
    ).astype(jnp.bfloat16)
    gain_term = jnp.sum(normed_grad * inputs * inverse, axis=0) * grad_scale
    gain_pieces = lax.all_to_all(
        gain_term.reshape(n_blocks, shard_rows), ("ctx", "dp"), 0, 0, tiled=True
    )
    gain_grad = jnp.sum(gain_pieces, axis=0)
    return (hidden_grad[None], query_gradient[None], key_weight_grad, value_weight_grad, gain_grad)


def solution(mesh):
    return jax.shard_map(
        body,
        mesh=mesh,
        in_specs=(
            P(("groups", "dp"), "ctx", None),
            P(),
            P(("ctx", "dp"), None),
            P(("ctx", "dp"), None),
            P(("groups", "dp"), "ctx", None),
            P(("groups", "dp"), "ctx", None),
        ),
        out_specs=(
            P(("groups", "dp"), "ctx", None),
            P(("groups", "dp"), "ctx", None),
            P(("groups", "ctx", "dp"), None),
            P(("groups", "ctx", "dp"), None),
            P(("groups", "ctx", "dp")),
        ),
        check_vma=False,
    )
```

```python
import jax
import jax.numpy as jnp
from jax import lax
from jax.sharding import PartitionSpec as P

HEADS = 16
KV_HEADS = 8
HEAD_DIM = 128
WINDOW = 256


score_scale = 1.0 / 12.0
grad_scale = 1.0 / 64.0
norm_eps = 1e-06
rope_base = 10000.0
masked_score = -1e30


def from_behind(value, axis, steps):
    count = lax.axis_size(axis)
    initial, last = (max(0, -steps), min(count, count - steps))
    return lax.ppermute(value, axis, [(source, source + steps) for source in range(initial, last)])


def rotation(positions):
    half_dim = HEAD_DIM // 2
    frequency = rope_base ** (-jnp.arange(half_dim, dtype=jnp.float32) / half_dim)
    angles = positions.astype(jnp.float32)[:, None] * frequency[None, :]
    return (jnp.cos(angles)[:, None, :], jnp.sin(angles)[:, None, :])


def rotate(tensor, cosine_table, sine_table):
    half_dim = HEAD_DIM // 2
    front_half = tensor[..., :half_dim]
    back_half = tensor[..., half_dim:]
    return jnp.concatenate(
        [
            front_half * cosine_table - back_half * sine_table,
            back_half * cosine_table + front_half * sine_table,
        ],
        axis=-1,
    )


def rotate_back(tensor, cosine_table, sine_table):
    half_dim = HEAD_DIM // 2
    front_half = tensor[..., :half_dim]
    back_half = tensor[..., half_dim:]
    return jnp.concatenate(
        [
            front_half * cosine_table + back_half * sine_table,
            back_half * cosine_table - front_half * sine_table,
        ],
        axis=-1,
    )


def block_backward(
    query_block, grad_block, nearby_keys, near_values, distant_keys, far_values, has_prev
):
    tok_rows = query_block.shape[0]
    group_size = HEADS // KV_HEADS
    query_head_split = query_block.reshape(tok_rows, KV_HEADS, group_size, HEAD_DIM)
    gradient_heads = grad_block.reshape(tok_rows, KV_HEADS, group_size, HEAD_DIM)
    row_index = jnp.arange(tok_rows)[:, None]
    col_index = jnp.arange(tok_rows)[None, :]
    near_mask = (col_index <= row_index) & (row_index - col_index < WINDOW)
    far_mask = (col_index > row_index + tok_rows - WINDOW) & has_prev

    def pair_products(leftover_heads, key_row_block):
        return jnp.einsum(
            "qbak,wbk->baqw", leftover_heads, key_row_block, preferred_element_type=jnp.float32
        )

    near_scores = jnp.where(
        near_mask, pair_products(query_head_split, nearby_keys) * score_scale, masked_score
    )
    far_scores = jnp.where(
        far_mask, pair_products(query_head_split, distant_keys) * score_scale, masked_score
    )
    row_top = jnp.maximum(jnp.max(near_scores, -1), jnp.max(far_scores, -1))[..., None]
    near_exp = jnp.where(near_mask, jnp.exp(near_scores - row_top), 0.0)
    far_exp = jnp.where(far_mask, jnp.exp(far_scores - row_top), 0.0)
    row_total = (jnp.sum(near_exp, -1) + jnp.sum(far_exp, -1))[..., None]
    near_probs = near_exp / row_total
    far_probs = far_exp / row_total
    near_dprobs = pair_products(gradient_heads, near_values)
    far_dprobs = pair_products(gradient_heads, far_values)
    weighted = (jnp.sum(near_probs * near_dprobs, -1) + jnp.sum(far_probs * far_dprobs, -1))[
        ..., None
    ]
    nearby_score_gradient = (near_probs * (near_dprobs - weighted) * score_scale).astype(
        jnp.bfloat16
    )
    distant_score_gradient = (far_probs * (far_dprobs - weighted) * score_scale).astype(
        jnp.bfloat16
    )
    nearby_reduced = near_probs.astype(jnp.bfloat16)
    distant_reduced = far_probs.astype(jnp.bfloat16)
    query_gradient = jnp.einsum(
        "xqwc,cxi->wxqi", nearby_score_gradient, nearby_keys, preferred_element_type=jnp.float32
    )
    query_gradient = query_gradient + jnp.einsum(
        "xqwc,cxi->wxqi", distant_score_gradient, distant_keys, preferred_element_type=jnp.float32
    )
    nearby_key = jnp.einsum(
        "woia,iwon->awn",
        nearby_score_gradient,
        query_head_split,
        preferred_element_type=jnp.float32,
    )
    distant_key = jnp.einsum(
        "woia,iwon->awn",
        distant_score_gradient,
        query_head_split,
        preferred_element_type=jnp.float32,
    )
    nearby_value = jnp.einsum(
        "woia,iwon->awn", nearby_reduced, gradient_heads, preferred_element_type=jnp.float32
    )
    distant_value = jnp.einsum(
        "woia,iwon->awn", distant_reduced, gradient_heads, preferred_element_type=jnp.float32
    )
    query_out = query_gradient.reshape(tok_rows, HEADS * HEAD_DIM).astype(jnp.bfloat16)
    return (query_out, nearby_key, nearby_value, distant_key, distant_value)


def ring_order(n_ctx, n_dp):
    if n_ctx % 2 == 0:
        half = n_ctx // 2
        chips = [2 * a for a in range(half)] + [2 * a + 1 for a in reversed(range(half))]
    else:
        chips = list(range(n_ctx))
    return [chip * n_dp + core for chip in chips for core in range(n_dp)]


def ring_gather(piece, axes, ring):
    count = len(ring)
    ahead = [(ring[i], ring[(i + 1) % count]) for i in range(count)]
    behind = [(ring[i], ring[(i - 1) % count]) for i in range(count)]
    n_ahead = count // 2
    from_left, from_right = [], []
    moving = piece
    for _ in range(n_ahead):
        moving = lax.ppermute(moving, axes, ahead)
        from_left.append(moving)
    moving = piece
    for _ in range(count - 1 - n_ahead):
        moving = lax.ppermute(moving, axes, behind)
        from_right.append(moving)
    return [piece] + from_right + from_left[::-1]


def body(hidden_in, norm_gain, key_weight, value_weight, queries, out_grad):
    tok_rows = hidden_in.shape[1]
    key_width = key_weight.shape[1]
    inputs = hidden_in[0].astype(jnp.float32)
    inverse = lax.rsqrt(jnp.mean(inputs * inputs, axis=-1, keepdims=True) + norm_eps)
    normed = (inputs * inverse * norm_gain).astype(jnp.bfloat16)
    n_ctx = lax.axis_size("ctx")
    n_dp = lax.axis_size("dp")
    n_blocks = n_ctx * n_dp
    shard_rows = normed.shape[1] // n_blocks
    ring = ring_order(n_ctx, n_dp)
    ring_pos = [0] * n_blocks
    for place, member in enumerate(ring):
        ring_pos[member] = place
    my_place = jnp.array(ring_pos, jnp.int32)[lax.axis_index("ctx") * n_dp + lax.axis_index("dp")]
    offsets = jnp.arange(n_blocks, dtype=jnp.int32)
    source_of = jnp.array(ring, jnp.int32)[(my_place + offsets) % n_blocks]
    offset_of = (jnp.array(ring_pos, jnp.int32) - my_place) % n_blocks
    weights = ring_gather(
        jnp.concatenate([key_weight, value_weight], axis=1), ("ctx", "dp"), ring
    )
    normed_local = jnp.swapaxes(normed.reshape(tok_rows, n_blocks, shard_rows), 0, 1)
    normed_blocks = jnp.take(normed_local, source_of, axis=0)
    projected = jnp.dot(normed_blocks[0], weights[0], preferred_element_type=jnp.float32)
    for place in range(1, n_blocks):
        projected = projected + jnp.dot(
            normed_blocks[place], weights[place], preferred_element_type=jnp.float32
        )
    key_raw = projected[:, :key_width]
    value_rows = projected[:, key_width:].astype(jnp.bfloat16)
    ctx_index = lax.axis_index("ctx")
    positions = ctx_index * tok_rows + jnp.arange(tok_rows, dtype=jnp.int32)
    cosine_table, sine_table = rotation(positions)
    key_row_block = rotate(key_raw.reshape(tok_rows, KV_HEADS, HEAD_DIM), cosine_table, sine_table)
    key_row_block = key_row_block.astype(jnp.bfloat16).reshape(tok_rows, key_width)
    prev_key, prev_value = from_behind((key_row_block, value_rows), "ctx", 1)
    head_shape = (tok_rows, KV_HEADS, HEAD_DIM)
    query_gradient, nearby_key, nearby_value, distant_key, distant_value = block_backward(
        queries[0],
        out_grad[0],
        key_row_block.reshape(head_shape),
        value_rows.reshape(head_shape),
        prev_key.reshape(head_shape),
        prev_value.reshape(head_shape),
        ctx_index > 0,
    )
    incoming_key, incoming_value = from_behind(
        (distant_key.astype(jnp.bfloat16), distant_value.astype(jnp.bfloat16)), "ctx", -1
    )
    key_grad = nearby_key + incoming_key.astype(jnp.float32)
    value_grad = nearby_value + incoming_value.astype(jnp.float32)
    key_grad_raw = (
        rotate_back(key_grad, cosine_table, sine_table)
        .astype(jnp.bfloat16)
        .reshape(tok_rows, key_width)
    )
    value_low = value_grad.astype(jnp.bfloat16).reshape(tok_rows, key_width)
    normed_cols = lax.all_to_all(normed_local, ("ctx", "dp"), 0, 0, tiled=True)
    normed_cols = jnp.take(normed_cols, source_of, axis=0)
    grads_cat = jnp.concatenate([key_grad_raw, value_low], axis=1)
    grads_low = ring_gather(grads_cat, ("ctx", "dp"), ring)

    def block_term(place):
        term = jnp.einsum(
            "td,tk->dk", normed_cols[place], grads_low[place], preferred_element_type=jnp.float32
        )
        return (term * grad_scale).astype(jnp.bfloat16).astype(jnp.float32)

    stacked = block_term(0)
    for place in range(1, n_blocks):
        stacked = stacked + block_term(place)
    key_weight_grad = stacked[:, :key_width]
    value_weight_grad = stacked[:, key_width:]
    normed_grad = jnp.stack(
        [
            jnp.einsum("tk,rk->tr", grads_cat, piece, preferred_element_type=jnp.float32)
            for piece in weights
        ]
    )
    normed_grad = jnp.swapaxes(jnp.take(normed_grad, offset_of, axis=0), 0, 1)
    normed_grad = normed_grad.reshape(tok_rows, -1)
    scaled = normed_grad * norm_gain
    cubed = inverse * inverse * inverse
    hidden_grad = (
        inverse * scaled - inputs * cubed * jnp.mean(scaled * inputs, axis=-1, keepdims=True)
    ).astype(jnp.bfloat16)
    gain_term = jnp.sum(normed_grad * inputs * inverse, axis=0) * grad_scale
    gain_pieces = lax.all_to_all(
        gain_term.reshape(n_blocks, shard_rows), ("ctx", "dp"), 0, 0, tiled=True
    )
    gain_grad = jnp.sum(gain_pieces, axis=0)
    return (hidden_grad[None], query_gradient[None], key_weight_grad, value_weight_grad, gain_grad)


def solution(mesh):
    return jax.shard_map(
        body,
        mesh=mesh,
        in_specs=(
            P(("groups", "dp"), "ctx", None),
            P(),
            P(("ctx", "dp"), None),
            P(("ctx", "dp"), None),
            P(("groups", "dp"), "ctx", None),
            P(("groups", "dp"), "ctx", None),
        ),
        out_specs=(
            P(("groups", "dp"), "ctx", None),
            P(("groups", "dp"), "ctx", None),
            P(("groups", "ctx", "dp"), None),
            P(("groups", "ctx", "dp"), None),
            P(("groups", "ctx", "dp")),
        ),
        check_vma=False,
    )
```

```python
import jax
import jax.numpy as jnp
from jax import lax
from jax.sharding import PartitionSpec as P

HEADS = 16
KV_HEADS = 8
HEAD_DIM = 128
WINDOW = 256


score_scale = 1.0 / 12.0
grad_scale = 1.0 / 64.0
norm_eps = 1e-06
rope_base = 10000.0
masked_score = -1e30


def from_behind(value, axis, steps):
    count = lax.axis_size(axis)
    initial, last = (max(0, -steps), min(count, count - steps))
    return lax.ppermute(value, axis, [(source, source + steps) for source in range(initial, last)])


def rotation(positions):
    half_dim = HEAD_DIM // 2
    frequency = rope_base ** (-jnp.arange(half_dim, dtype=jnp.float32) / half_dim)
    angles = positions.astype(jnp.float32)[:, None] * frequency[None, :]
    return (jnp.cos(angles)[:, None, :], jnp.sin(angles)[:, None, :])


def rotate(tensor, cosine_table, sine_table):
    half_dim = HEAD_DIM // 2
    front_half = tensor[..., :half_dim]
    back_half = tensor[..., half_dim:]
    return jnp.concatenate(
        [
            front_half * cosine_table - back_half * sine_table,
            back_half * cosine_table + front_half * sine_table,
        ],
        axis=-1,
    )


def rotate_back(tensor, cosine_table, sine_table):
    half_dim = HEAD_DIM // 2
    front_half = tensor[..., :half_dim]
    back_half = tensor[..., half_dim:]
    return jnp.concatenate(
        [
            front_half * cosine_table + back_half * sine_table,
            back_half * cosine_table - front_half * sine_table,
        ],
        axis=-1,
    )


def block_backward(
    query_block, grad_block, nearby_keys, near_values, distant_keys, far_values, has_prev
):
    tok_rows = query_block.shape[0]
    group_size = HEADS // KV_HEADS
    query_head_split = query_block.reshape(tok_rows, KV_HEADS, group_size, HEAD_DIM)
    gradient_heads = grad_block.reshape(tok_rows, KV_HEADS, group_size, HEAD_DIM)
    row_index = jnp.arange(tok_rows)[:, None]
    col_index = jnp.arange(tok_rows)[None, :]
    near_mask = (col_index <= row_index) & (row_index - col_index < WINDOW)
    far_mask = (col_index > row_index + tok_rows - WINDOW) & has_prev

    def pair_products(leftover_heads, key_row_block):
        return jnp.einsum(
            "qbak,wbk->baqw", leftover_heads, key_row_block, preferred_element_type=jnp.float32
        )

    near_scores = jnp.where(
        near_mask, pair_products(query_head_split, nearby_keys) * score_scale, masked_score
    )
    far_scores = jnp.where(
        far_mask, pair_products(query_head_split, distant_keys) * score_scale, masked_score
    )
    row_top = jnp.maximum(jnp.max(near_scores, -1), jnp.max(far_scores, -1))[..., None]
    near_exp = jnp.where(near_mask, jnp.exp(near_scores - row_top), 0.0)
    far_exp = jnp.where(far_mask, jnp.exp(far_scores - row_top), 0.0)
    row_total = (jnp.sum(near_exp, -1) + jnp.sum(far_exp, -1))[..., None]
    near_probs = near_exp / row_total
    far_probs = far_exp / row_total
    near_dprobs = pair_products(gradient_heads, near_values)
    far_dprobs = pair_products(gradient_heads, far_values)
    weighted = (jnp.sum(near_probs * near_dprobs, -1) + jnp.sum(far_probs * far_dprobs, -1))[
        ..., None
    ]
    nearby_score_gradient = (near_probs * (near_dprobs - weighted) * score_scale).astype(
        jnp.bfloat16
    )
    distant_score_gradient = (far_probs * (far_dprobs - weighted) * score_scale).astype(
        jnp.bfloat16
    )
    nearby_reduced = near_probs.astype(jnp.bfloat16)
    distant_reduced = far_probs.astype(jnp.bfloat16)
    query_gradient = jnp.einsum(
        "xqwc,cxi->wxqi", nearby_score_gradient, nearby_keys, preferred_element_type=jnp.float32
    )
    query_gradient = query_gradient + jnp.einsum(
        "xqwc,cxi->wxqi", distant_score_gradient, distant_keys, preferred_element_type=jnp.float32
    )
    nearby_key = jnp.einsum(
        "woia,iwon->awn",
        nearby_score_gradient,
        query_head_split,
        preferred_element_type=jnp.float32,
    )
    distant_key = jnp.einsum(
        "woia,iwon->awn",
        distant_score_gradient,
        query_head_split,
        preferred_element_type=jnp.float32,
    )
    nearby_value = jnp.einsum(
        "woia,iwon->awn", nearby_reduced, gradient_heads, preferred_element_type=jnp.float32
    )
    distant_value = jnp.einsum(
        "woia,iwon->awn", distant_reduced, gradient_heads, preferred_element_type=jnp.float32
    )
    query_out = query_gradient.reshape(tok_rows, HEADS * HEAD_DIM).astype(jnp.bfloat16)
    return (query_out, nearby_key, nearby_value, distant_key, distant_value)


def ring_order(n_ctx, n_dp):
    if n_ctx % 2 == 0:
        half = n_ctx // 2
        chips = [2 * a for a in range(half)] + [2 * a + 1 for a in reversed(range(half))]
    else:
        chips = list(range(n_ctx))
    return [chip * n_dp + core for chip in chips for core in range(n_dp)]


def ring_gather(piece, axes, ring):
    count = len(ring)
    ahead = [(ring[i], ring[(i + 1) % count]) for i in range(count)]
    behind = [(ring[i], ring[(i - 1) % count]) for i in range(count)]
    n_ahead = count // 2
    from_left, from_right = [], []
    moving = piece
    for _ in range(n_ahead):
        moving = lax.ppermute(moving, axes, ahead)
        from_left.append(moving)
    moving = piece
    for _ in range(count - 1 - n_ahead):
        moving = lax.ppermute(moving, axes, behind)
        from_right.append(moving)
    return [piece] + from_right + from_left[::-1]


def body(hidden_in, norm_gain, key_weight, value_weight, queries, out_grad):
    tok_rows = hidden_in.shape[1]
    key_width = key_weight.shape[1]
    inputs = hidden_in[0].astype(jnp.float32)
    inverse = lax.rsqrt(jnp.mean(inputs * inputs, axis=-1, keepdims=True) + norm_eps)
    normed = (inputs * inverse * norm_gain).astype(jnp.bfloat16)
    n_ctx = lax.axis_size("ctx")
    n_dp = lax.axis_size("dp")
    n_blocks = n_ctx * n_dp
    shard_rows = normed.shape[1] // n_blocks
    core = lax.axis_index("dp")
    first_core = core == 0
    chip_ring = ring_order(n_ctx, 1)
    chip_place = [0] * n_ctx
    for place, member in enumerate(chip_ring):
        chip_place[member] = place
    my_chip_place = jnp.array(chip_place, jnp.int32)[lax.axis_index("ctx")]
    chip_offsets = jnp.arange(n_ctx, dtype=jnp.int32)
    chips_by_offset = jnp.array(chip_ring, jnp.int32)[(my_chip_place + chip_offsets) % n_ctx]
    source_of = (chips_by_offset[:, None] * n_dp + jnp.stack([core, 1 - core])[None, :]).reshape(-1)
    all_blocks = jnp.arange(n_blocks, dtype=jnp.int32)
    block_chip_place = jnp.array(chip_place, jnp.int32)[all_blocks // n_dp]
    offset_of = 2 * ((block_chip_place - my_chip_place) % n_ctx) + (all_blocks % n_dp != core)
    swap_pairs = [(0, 1), (1, 0)]

    def gather_halves(rows):
        half = rows.shape[1] // 2
        other = lax.ppermute(rows, "dp", swap_pairs)
        pair = jnp.stack([rows, other])
        mine_local = lax.dynamic_slice_in_dim(pair, core * half, half, axis=2)
        theirs_local = lax.dynamic_slice_in_dim(pair, (1 - core) * half, half, axis=2)
        chip_pieces = ring_gather(mine_local, ("ctx",), chip_ring)
        mine, theirs = [], []
        for place, piece in enumerate(chip_pieces):
            mine.extend([piece[0], piece[1]])
            if place == 0:
                theirs.extend([theirs_local[0], theirs_local[1]])
            else:
                arrived = lax.ppermute(piece, "dp", swap_pairs)
                theirs.extend([arrived[1], arrived[0]])
        return mine, theirs

    def pick(flag, when_true, when_false):
        return jnp.where(flag, when_true, when_false)

    weights_mine, weights_theirs = gather_halves(
        jnp.concatenate([key_weight, value_weight], axis=1)
    )
    normed_local = jnp.swapaxes(normed.reshape(tok_rows, n_blocks, shard_rows), 0, 1)
    normed_blocks = jnp.take(normed_local, source_of, axis=0)

    def project(pieces):
        total = jnp.dot(normed_blocks[0], pieces[0], preferred_element_type=jnp.float32)
        for place in range(1, n_blocks):
            total = total + jnp.dot(
                normed_blocks[place], pieces[place], preferred_element_type=jnp.float32
            )
        return total

    projected_mine, projected_theirs = project(weights_mine), project(weights_theirs)
    key_raw = pick(first_core, projected_mine, projected_theirs)
    value_rows = pick(first_core, projected_theirs, projected_mine).astype(jnp.bfloat16)
    ctx_index = lax.axis_index("ctx")
    positions = ctx_index * tok_rows + jnp.arange(tok_rows, dtype=jnp.int32)
    cosine_table, sine_table = rotation(positions)
    key_row_block = rotate(key_raw.reshape(tok_rows, KV_HEADS, HEAD_DIM), cosine_table, sine_table)
    key_row_block = key_row_block.astype(jnp.bfloat16).reshape(tok_rows, key_width)
    prev_key, prev_value = from_behind((key_row_block, value_rows), "ctx", 1)
    head_shape = (tok_rows, KV_HEADS, HEAD_DIM)
    query_gradient, nearby_key, nearby_value, distant_key, distant_value = block_backward(
        queries[0],
        out_grad[0],
        key_row_block.reshape(head_shape),
        value_rows.reshape(head_shape),
        prev_key.reshape(head_shape),
        prev_value.reshape(head_shape),
        ctx_index > 0,
    )
    incoming_key, incoming_value = from_behind(
        (distant_key.astype(jnp.bfloat16), distant_value.astype(jnp.bfloat16)), "ctx", -1
    )
    key_grad = nearby_key + incoming_key.astype(jnp.float32)
    value_grad = nearby_value + incoming_value.astype(jnp.float32)
    key_grad_raw = (
        rotate_back(key_grad, cosine_table, sine_table)
        .astype(jnp.bfloat16)
        .reshape(tok_rows, key_width)
    )
    value_low = value_grad.astype(jnp.bfloat16).reshape(tok_rows, key_width)
    normed_cols = lax.all_to_all(normed_local, ("ctx", "dp"), 0, 0, tiled=True)
    normed_cols = jnp.take(normed_cols, source_of, axis=0)
    grads_mine, grads_theirs = gather_halves(jnp.concatenate([key_grad_raw, value_low], axis=1))

    def weight_grad_rows(pieces):
        def block_term(place):
            term = jnp.einsum(
                "td,tk->dk", normed_cols[place], pieces[place], preferred_element_type=jnp.float32
            )
            return (term * grad_scale).astype(jnp.bfloat16).astype(jnp.float32)

        total = block_term(0)
        for place in range(1, n_blocks):
            total = total + block_term(place)
        return total

    rows_mine, rows_theirs = weight_grad_rows(grads_mine), weight_grad_rows(grads_theirs)
    stacked = jnp.concatenate(
        [pick(first_core, rows_mine, rows_theirs), pick(first_core, rows_theirs, rows_mine)], axis=1
    )
    key_weight_grad = stacked[:, :key_width]
    value_weight_grad = stacked[:, key_width:]
    grads_own = pick(first_core, key_grad_raw, value_low)
    grads_other = pick(first_core, value_low, key_grad_raw)
    normed_grad = jnp.stack(
        [
            jnp.einsum("tk,rk->tr", grads_own, piece_mine, preferred_element_type=jnp.float32)
            + jnp.einsum("tk,rk->tr", grads_other, piece_theirs, preferred_element_type=jnp.float32)
            for piece_mine, piece_theirs in zip(weights_mine, weights_theirs)
        ]
    )
    normed_grad = jnp.swapaxes(jnp.take(normed_grad, offset_of, axis=0), 0, 1)
    normed_grad = normed_grad.reshape(tok_rows, -1)
    scaled = normed_grad * norm_gain
    cubed = inverse * inverse * inverse
    hidden_grad = (
        inverse * scaled - inputs * cubed * jnp.mean(scaled * inputs, axis=-1, keepdims=True)
    ).astype(jnp.bfloat16)
    gain_term = jnp.sum(normed_grad * inputs * inverse, axis=0) * grad_scale
    gain_pieces = lax.all_to_all(
        gain_term.reshape(n_blocks, shard_rows), ("ctx", "dp"), 0, 0, tiled=True
    )
    gain_grad = jnp.sum(gain_pieces, axis=0)
    return (hidden_grad[None], query_gradient[None], key_weight_grad, value_weight_grad, gain_grad)


def solution(mesh):
    return jax.shard_map(
        body,
        mesh=mesh,
        in_specs=(
            P(("groups", "dp"), "ctx", None),
            P(),
            P(("ctx", "dp"), None),
            P(("ctx", "dp"), None),
            P(("groups", "dp"), "ctx", None),
            P(("groups", "dp"), "ctx", None),
        ),
        out_specs=(
            P(("groups", "dp"), "ctx", None),
            P(("groups", "dp"), "ctx", None),
            P(("groups", "ctx", "dp"), None),
            P(("groups", "ctx", "dp"), None),
            P(("groups", "ctx", "dp")),
        ),
        check_vma=False,
    )
```

```python
import jax
import jax.numpy as jnp
from jax import lax
from jax.sharding import PartitionSpec as P

HEADS = 16
KV_HEADS = 8
HEAD_DIM = 128
WINDOW = 256


score_scale = 1.0 / 12.0
grad_scale = 1.0 / 64.0
norm_eps = 1e-06
rope_base = 10000.0
masked_score = -1e30


def from_behind(value, axis, steps):
    count = lax.axis_size(axis)
    initial, last = (max(0, -steps), min(count, count - steps))
    return lax.ppermute(value, axis, [(source, source + steps) for source in range(initial, last)])


def rotation(positions):
    half_dim = HEAD_DIM // 2
    frequency = rope_base ** (-jnp.arange(half_dim, dtype=jnp.float32) / half_dim)
    angles = positions.astype(jnp.float32)[:, None] * frequency[None, :]
    return (jnp.cos(angles)[:, None, :], jnp.sin(angles)[:, None, :])


def rotate(tensor, cosine_table, sine_table):
    half_dim = HEAD_DIM // 2
    front_half = tensor[..., :half_dim]
    back_half = tensor[..., half_dim:]
    return jnp.concatenate(
        [
            front_half * cosine_table - back_half * sine_table,
            back_half * cosine_table + front_half * sine_table,
        ],
        axis=-1,
    )


def rotate_back(tensor, cosine_table, sine_table):
    half_dim = HEAD_DIM // 2
    front_half = tensor[..., :half_dim]
    back_half = tensor[..., half_dim:]
    return jnp.concatenate(
        [
            front_half * cosine_table + back_half * sine_table,
            back_half * cosine_table - front_half * sine_table,
        ],
        axis=-1,
    )


def block_backward(
    query_block, grad_block, nearby_keys, near_values, distant_keys, far_values, has_prev
):
    tok_rows = query_block.shape[0]
    group_size = HEADS // KV_HEADS
    query_head_split = query_block.reshape(tok_rows, KV_HEADS, group_size, HEAD_DIM)
    gradient_heads = grad_block.reshape(tok_rows, KV_HEADS, group_size, HEAD_DIM)
    row_index = jnp.arange(tok_rows)[:, None]
    col_index = jnp.arange(tok_rows)[None, :]
    near_mask = (col_index <= row_index) & (row_index - col_index < WINDOW)
    far_mask = (col_index > row_index + tok_rows - WINDOW) & has_prev

    def pair_products(leftover_heads, key_row_block):
        return jnp.einsum(
            "qbak,wbk->baqw", leftover_heads, key_row_block, preferred_element_type=jnp.float32
        )

    near_scores = jnp.where(
        near_mask, pair_products(query_head_split, nearby_keys) * score_scale, masked_score
    )
    far_scores = jnp.where(
        far_mask, pair_products(query_head_split, distant_keys) * score_scale, masked_score
    )
    row_top = jnp.maximum(jnp.max(near_scores, -1), jnp.max(far_scores, -1))[..., None]
    near_exp = jnp.where(near_mask, jnp.exp(near_scores - row_top), 0.0)
    far_exp = jnp.where(far_mask, jnp.exp(far_scores - row_top), 0.0)
    row_total = (jnp.sum(near_exp, -1) + jnp.sum(far_exp, -1))[..., None]
    near_probs = near_exp / row_total
    far_probs = far_exp / row_total
    near_dprobs = pair_products(gradient_heads, near_values)
    far_dprobs = pair_products(gradient_heads, far_values)
    weighted = (jnp.sum(near_probs * near_dprobs, -1) + jnp.sum(far_probs * far_dprobs, -1))[
        ..., None
    ]
    nearby_score_gradient = (near_probs * (near_dprobs - weighted) * score_scale).astype(
        jnp.bfloat16
    )
    distant_score_gradient = (far_probs * (far_dprobs - weighted) * score_scale).astype(
        jnp.bfloat16
    )
    nearby_reduced = near_probs.astype(jnp.bfloat16)
    distant_reduced = far_probs.astype(jnp.bfloat16)
    query_gradient = jnp.einsum(
        "xqwc,cxi->wxqi", nearby_score_gradient, nearby_keys, preferred_element_type=jnp.float32
    )
    query_gradient = query_gradient + jnp.einsum(
        "xqwc,cxi->wxqi", distant_score_gradient, distant_keys, preferred_element_type=jnp.float32
    )
    nearby_key = jnp.einsum(
        "woia,iwon->awn",
        nearby_score_gradient,
        query_head_split,
        preferred_element_type=jnp.float32,
    )
    distant_key = jnp.einsum(
        "woia,iwon->awn",
        distant_score_gradient,
        query_head_split,
        preferred_element_type=jnp.float32,
    )
    nearby_value = jnp.einsum(
        "woia,iwon->awn", nearby_reduced, gradient_heads, preferred_element_type=jnp.float32
    )
    distant_value = jnp.einsum(
        "woia,iwon->awn", distant_reduced, gradient_heads, preferred_element_type=jnp.float32
    )
    query_out = query_gradient.reshape(tok_rows, HEADS * HEAD_DIM).astype(jnp.bfloat16)
    return (query_out, nearby_key, nearby_value, distant_key, distant_value)


def ring_order(n_ctx, n_dp):
    if n_ctx % 2 == 0:
        half = n_ctx // 2
        chips = [2 * a for a in range(half)] + [2 * a + 1 for a in reversed(range(half))]
    else:
        chips = list(range(n_ctx))
    return [chip * n_dp + core for chip in chips for core in range(n_dp)]


def ring_gather(piece, axes, ring):
    count = len(ring)
    ahead = [(ring[i], ring[(i + 1) % count]) for i in range(count)]
    behind = [(ring[i], ring[(i - 1) % count]) for i in range(count)]
    n_ahead = count // 2
    from_left, from_right = [], []
    moving = piece
    for _ in range(n_ahead):
        moving = lax.ppermute(moving, axes, ahead)
        from_left.append(moving)
    moving = piece
    for _ in range(count - 1 - n_ahead):
        moving = lax.ppermute(moving, axes, behind)
        from_right.append(moving)
    return [piece] + from_right + from_left[::-1]


def body(hidden_in, norm_gain, key_weight, value_weight, queries, out_grad):
    tok_rows = hidden_in.shape[1]
    key_width = key_weight.shape[1]
    inputs = hidden_in[0].astype(jnp.float32)
    inverse = lax.rsqrt(jnp.mean(inputs * inputs, axis=-1, keepdims=True) + norm_eps)
    normed = (inputs * inverse * norm_gain).astype(jnp.bfloat16)
    n_ctx = lax.axis_size("ctx")
    n_dp = lax.axis_size("dp")
    n_blocks = n_ctx * n_dp
    shard_rows = normed.shape[1] // n_blocks
    ring = ring_order(n_ctx, n_dp)
    ring_pos = [0] * n_blocks
    for place, member in enumerate(ring):
        ring_pos[member] = place
    my_place = jnp.array(ring_pos, jnp.int32)[lax.axis_index("ctx") * n_dp + lax.axis_index("dp")]
    offsets = jnp.arange(n_blocks, dtype=jnp.int32)
    source_of = jnp.array(ring, jnp.int32)[(my_place + offsets) % n_blocks]
    offset_of = (jnp.array(ring_pos, jnp.int32) - my_place) % n_blocks
    weights = ring_gather(
        jnp.concatenate([key_weight, value_weight], axis=1), ("ctx", "dp"), ring
    )
    normed_local = jnp.swapaxes(normed.reshape(tok_rows, n_blocks, shard_rows), 0, 1)
    normed_blocks = jnp.take(normed_local, source_of, axis=0)
    projected = jnp.dot(normed_blocks[0], weights[0], preferred_element_type=jnp.float32)
    for place in range(1, n_blocks):
        projected = projected + jnp.dot(
            normed_blocks[place], weights[place], preferred_element_type=jnp.float32
        )
    normed_late, projected = lax.optimization_barrier((normed_local, projected))
    key_raw = projected[:, :key_width]
    value_rows = projected[:, key_width:].astype(jnp.bfloat16)
    ctx_index = lax.axis_index("ctx")
    positions = ctx_index * tok_rows + jnp.arange(tok_rows, dtype=jnp.int32)
    cosine_table, sine_table = rotation(positions)
    key_row_block = rotate(key_raw.reshape(tok_rows, KV_HEADS, HEAD_DIM), cosine_table, sine_table)
    key_row_block = key_row_block.astype(jnp.bfloat16).reshape(tok_rows, key_width)
    prev_key, prev_value = from_behind((key_row_block, value_rows), "ctx", 1)
    head_shape = (tok_rows, KV_HEADS, HEAD_DIM)
    query_gradient, nearby_key, nearby_value, distant_key, distant_value = block_backward(
        queries[0],
        out_grad[0],
        key_row_block.reshape(head_shape),
        value_rows.reshape(head_shape),
        prev_key.reshape(head_shape),
        prev_value.reshape(head_shape),
        ctx_index > 0,
    )
    incoming_key, incoming_value = from_behind(
        (distant_key.astype(jnp.bfloat16), distant_value.astype(jnp.bfloat16)), "ctx", -1
    )
    key_grad = nearby_key + incoming_key.astype(jnp.float32)
    value_grad = nearby_value + incoming_value.astype(jnp.float32)
    key_grad_raw = (
        rotate_back(key_grad, cosine_table, sine_table)
        .astype(jnp.bfloat16)
        .reshape(tok_rows, key_width)
    )
    value_low = value_grad.astype(jnp.bfloat16).reshape(tok_rows, key_width)
    normed_cols = lax.all_to_all(normed_late, ("ctx", "dp"), 0, 0, tiled=True)
    normed_cols = jnp.take(normed_cols, source_of, axis=0)
    grads_cat = jnp.concatenate([key_grad_raw, value_low], axis=1)
    grads_low = ring_gather(grads_cat, ("ctx", "dp"), ring)

    def block_term(place):
        term = jnp.einsum(
            "td,tk->dk", normed_cols[place], grads_low[place], preferred_element_type=jnp.float32
        )
        return (term * grad_scale).astype(jnp.bfloat16).astype(jnp.float32)

    stacked = block_term(0)
    for place in range(1, n_blocks):
        stacked = stacked + block_term(place)
    key_weight_grad = stacked[:, :key_width]
    value_weight_grad = stacked[:, key_width:]
    normed_grad = jnp.stack(
        [
            jnp.einsum("tk,rk->tr", grads_cat, piece, preferred_element_type=jnp.float32)
            for piece in weights
        ]
    )
    normed_grad = jnp.swapaxes(jnp.take(normed_grad, offset_of, axis=0), 0, 1)
    normed_grad = normed_grad.reshape(tok_rows, -1)
    scaled = normed_grad * norm_gain
    cubed = inverse * inverse * inverse
    hidden_grad = (
        inverse * scaled - inputs * cubed * jnp.mean(scaled * inputs, axis=-1, keepdims=True)
    ).astype(jnp.bfloat16)
    gain_term = jnp.sum(normed_grad * inputs * inverse, axis=0) * grad_scale
    gain_pieces = lax.all_to_all(
        gain_term.reshape(n_blocks, shard_rows), ("ctx", "dp"), 0, 0, tiled=True
    )
    gain_grad = jnp.sum(gain_pieces, axis=0)
    return (hidden_grad[None], query_gradient[None], key_weight_grad, value_weight_grad, gain_grad)


def solution(mesh):
    return jax.shard_map(
        body,
        mesh=mesh,
        in_specs=(
            P(("groups", "dp"), "ctx", None),
            P(),
            P(("ctx", "dp"), None),
            P(("ctx", "dp"), None),
            P(("groups", "dp"), "ctx", None),
            P(("groups", "dp"), "ctx", None),
        ),
        out_specs=(
            P(("groups", "dp"), "ctx", None),
            P(("groups", "dp"), "ctx", None),
            P(("groups", "ctx", "dp"), None),
            P(("groups", "ctx", "dp"), None),
            P(("groups", "ctx", "dp")),
        ),
        check_vma=False,
    )
```

```python
import jax
import jax.numpy as jnp
from jax import lax
from jax.sharding import PartitionSpec as P

HEADS = 16
KV_HEADS = 8
HEAD_DIM = 128
WINDOW = 256


score_scale = 1.0 / 12.0
grad_scale = 1.0 / 64.0
norm_eps = 1e-06
rope_base = 10000.0
masked_score = -1e30


def from_behind(value, axis, steps):
    count = lax.axis_size(axis)
    initial, last = (max(0, -steps), min(count, count - steps))
    return lax.ppermute(value, axis, [(source, source + steps) for source in range(initial, last)])


def rotation(positions):
    half_dim = HEAD_DIM // 2
    frequency = rope_base ** (-jnp.arange(half_dim, dtype=jnp.float32) / half_dim)
    angles = positions.astype(jnp.float32)[:, None] * frequency[None, :]
    return (jnp.cos(angles)[:, None, :], jnp.sin(angles)[:, None, :])


def rotate(tensor, cosine_table, sine_table):
    half_dim = HEAD_DIM // 2
    front_half = tensor[..., :half_dim]
    back_half = tensor[..., half_dim:]
    return jnp.concatenate(
        [
            front_half * cosine_table - back_half * sine_table,
            back_half * cosine_table + front_half * sine_table,
        ],
        axis=-1,
    )


def rotate_back(tensor, cosine_table, sine_table):
    half_dim = HEAD_DIM // 2
    front_half = tensor[..., :half_dim]
    back_half = tensor[..., half_dim:]
    return jnp.concatenate(
        [
            front_half * cosine_table + back_half * sine_table,
            back_half * cosine_table - front_half * sine_table,
        ],
        axis=-1,
    )


def block_backward(
    query_block, grad_block, nearby_keys, near_values, distant_keys, far_values, has_prev
):
    tok_rows = query_block.shape[0]
    group_size = HEADS // KV_HEADS
    query_head_split = query_block.reshape(tok_rows, KV_HEADS, group_size, HEAD_DIM)
    gradient_heads = grad_block.reshape(tok_rows, KV_HEADS, group_size, HEAD_DIM)
    row_index = jnp.arange(tok_rows)[:, None]
    col_index = jnp.arange(tok_rows)[None, :]
    near_mask = (col_index <= row_index) & (row_index - col_index < WINDOW)
    far_mask = (col_index > row_index + tok_rows - WINDOW) & has_prev

    def pair_products(leftover_heads, key_row_block):
        return jnp.einsum(
            "qbak,wbk->baqw", leftover_heads, key_row_block, preferred_element_type=jnp.float32
        )

    near_scores = jnp.where(
        near_mask, pair_products(query_head_split, nearby_keys) * score_scale, masked_score
    )
    far_scores = jnp.where(
        far_mask, pair_products(query_head_split, distant_keys) * score_scale, masked_score
    )
    row_top = jnp.maximum(jnp.max(near_scores, -1), jnp.max(far_scores, -1))[..., None]
    near_exp = jnp.where(near_mask, jnp.exp(near_scores - row_top), 0.0)
    far_exp = jnp.where(far_mask, jnp.exp(far_scores - row_top), 0.0)
    row_total = (jnp.sum(near_exp, -1) + jnp.sum(far_exp, -1))[..., None]
    near_probs = near_exp / row_total
    far_probs = far_exp / row_total
    near_dprobs = pair_products(gradient_heads, near_values)
    far_dprobs = pair_products(gradient_heads, far_values)
    weighted = (jnp.sum(near_probs * near_dprobs, -1) + jnp.sum(far_probs * far_dprobs, -1))[
        ..., None
    ]
    nearby_score_gradient = (near_probs * (near_dprobs - weighted) * score_scale).astype(
        jnp.bfloat16
    )
    distant_score_gradient = (far_probs * (far_dprobs - weighted) * score_scale).astype(
        jnp.bfloat16
    )
    nearby_reduced = near_probs.astype(jnp.bfloat16)
    distant_reduced = far_probs.astype(jnp.bfloat16)
    query_gradient = jnp.einsum(
        "xqwc,cxi->wxqi", nearby_score_gradient, nearby_keys, preferred_element_type=jnp.float32
    )
    query_gradient = query_gradient + jnp.einsum(
        "xqwc,cxi->wxqi", distant_score_gradient, distant_keys, preferred_element_type=jnp.float32
    )
    nearby_key = jnp.einsum(
        "woia,iwon->awn",
        nearby_score_gradient,
        query_head_split,
        preferred_element_type=jnp.float32,
    )
    distant_key = jnp.einsum(
        "woia,iwon->awn",
        distant_score_gradient,
        query_head_split,
        preferred_element_type=jnp.float32,
    )
    nearby_value = jnp.einsum(
        "woia,iwon->awn", nearby_reduced, gradient_heads, preferred_element_type=jnp.float32
    )
    distant_value = jnp.einsum(
        "woia,iwon->awn", distant_reduced, gradient_heads, preferred_element_type=jnp.float32
    )
    query_out = query_gradient.reshape(tok_rows, HEADS * HEAD_DIM).astype(jnp.bfloat16)
    return (query_out, nearby_key, nearby_value, distant_key, distant_value)


def ring_order(n_ctx, n_dp):
    if n_ctx % 2 == 0:
        half = n_ctx // 2
        chips = [2 * a for a in range(half)] + [2 * a + 1 for a in reversed(range(half))]
    else:
        chips = list(range(n_ctx))
    return [chip * n_dp + core for chip in chips for core in range(n_dp)]


def ring_gather(piece, axes, ring):
    count = len(ring)
    ahead = [(ring[i], ring[(i + 1) % count]) for i in range(count)]
    behind = [(ring[i], ring[(i - 1) % count]) for i in range(count)]
    n_ahead = count // 2
    from_left, from_right = [], []
    moving = piece
    for _ in range(n_ahead):
        moving = lax.ppermute(moving, axes, ahead)
        from_left.append(moving)
    moving = piece
    for _ in range(count - 1 - n_ahead):
        moving = lax.ppermute(moving, axes, behind)
        from_right.append(moving)
    return [piece] + from_right + from_left[::-1]


def body(hidden_in, norm_gain, key_weight, value_weight, queries, out_grad):
    tok_rows = hidden_in.shape[1]
    key_width = key_weight.shape[1]
    inputs = hidden_in[0].astype(jnp.float32)
    inverse = lax.rsqrt(jnp.mean(inputs * inputs, axis=-1, keepdims=True) + norm_eps)
    normed = (inputs * inverse * norm_gain).astype(jnp.bfloat16)
    n_ctx = lax.axis_size("ctx")
    n_dp = lax.axis_size("dp")
    n_blocks = n_ctx * n_dp
    shard_rows = normed.shape[1] // n_blocks
    ring = ring_order(n_ctx, n_dp)
    ring_pos = [0] * n_blocks
    for place, member in enumerate(ring):
        ring_pos[member] = place
    my_place = jnp.array(ring_pos, jnp.int32)[lax.axis_index("ctx") * n_dp + lax.axis_index("dp")]
    offsets = jnp.arange(n_blocks, dtype=jnp.int32)
    source_of = jnp.array(ring, jnp.int32)[(my_place + offsets) % n_blocks]
    offset_of = (jnp.array(ring_pos, jnp.int32) - my_place) % n_blocks
    key_pieces = ring_gather(key_weight, ("ctx", "dp"), ring)
    value_pieces = ring_gather(value_weight, ("ctx", "dp"), ring)
    normed_local = jnp.swapaxes(normed.reshape(tok_rows, n_blocks, shard_rows), 0, 1)
    normed_blocks = jnp.take(normed_local, source_of, axis=0)

    def project(pieces):
        total = jnp.dot(normed_blocks[0], pieces[0], preferred_element_type=jnp.float32)
        for place in range(1, n_blocks):
            total = total + jnp.dot(
                normed_blocks[place], pieces[place], preferred_element_type=jnp.float32
            )
        return total

    key_raw = project(key_pieces)
    value_rows = project(value_pieces).astype(jnp.bfloat16)
    ctx_index = lax.axis_index("ctx")
    positions = ctx_index * tok_rows + jnp.arange(tok_rows, dtype=jnp.int32)
    cosine_table, sine_table = rotation(positions)
    key_row_block = rotate(key_raw.reshape(tok_rows, KV_HEADS, HEAD_DIM), cosine_table, sine_table)
    key_row_block = key_row_block.astype(jnp.bfloat16).reshape(tok_rows, key_width)
    prev_key, prev_value = from_behind((key_row_block, value_rows), "ctx", 1)
    head_shape = (tok_rows, KV_HEADS, HEAD_DIM)
    query_gradient, nearby_key, nearby_value, distant_key, distant_value = block_backward(
        queries[0],
        out_grad[0],
        key_row_block.reshape(head_shape),
        value_rows.reshape(head_shape),
        prev_key.reshape(head_shape),
        prev_value.reshape(head_shape),
        ctx_index > 0,
    )
    incoming_key, incoming_value = from_behind(
        (distant_key.astype(jnp.bfloat16), distant_value.astype(jnp.bfloat16)), "ctx", -1
    )
    key_grad = nearby_key + incoming_key.astype(jnp.float32)
    value_grad = nearby_value + incoming_value.astype(jnp.float32)
    key_grad_raw = (
        rotate_back(key_grad, cosine_table, sine_table)
        .astype(jnp.bfloat16)
        .reshape(tok_rows, key_width)
    )
    value_low = value_grad.astype(jnp.bfloat16).reshape(tok_rows, key_width)
    normed_cols = lax.all_to_all(normed_local, ("ctx", "dp"), 0, 0, tiled=True)
    normed_cols = jnp.take(normed_cols, source_of, axis=0)
    key_grads = ring_gather(key_grad_raw, ("ctx", "dp"), ring)
    value_grads = ring_gather(value_low, ("ctx", "dp"), ring)

    def weight_grad_rows(pieces):
        def block_term(place):
            term = jnp.einsum(
                "td,tk->dk", normed_cols[place], pieces[place], preferred_element_type=jnp.float32
            )
            return (term * grad_scale).astype(jnp.bfloat16).astype(jnp.float32)

        total = block_term(0)
        for place in range(1, n_blocks):
            total = total + block_term(place)
        return total

    stacked = jnp.concatenate([weight_grad_rows(key_grads), weight_grad_rows(value_grads)], axis=1)
    key_weight_grad = stacked[:, :key_width]
    value_weight_grad = stacked[:, key_width:]
    normed_grad = jnp.stack(
        [
            jnp.einsum("tk,rk->tr", key_grad_raw, piece_k, preferred_element_type=jnp.float32)
            + jnp.einsum("tk,rk->tr", value_low, piece_v, preferred_element_type=jnp.float32)
            for piece_k, piece_v in zip(key_pieces, value_pieces)
        ]
    )
    normed_grad = jnp.swapaxes(jnp.take(normed_grad, offset_of, axis=0), 0, 1)
    normed_grad = normed_grad.reshape(tok_rows, -1)
    scaled = normed_grad * norm_gain
    cubed = inverse * inverse * inverse
    hidden_grad = (
        inverse * scaled - inputs * cubed * jnp.mean(scaled * inputs, axis=-1, keepdims=True)
    ).astype(jnp.bfloat16)
    gain_term = jnp.sum(normed_grad * inputs * inverse, axis=0) * grad_scale
    gain_pieces = lax.all_to_all(
        gain_term.reshape(n_blocks, shard_rows), ("ctx", "dp"), 0, 0, tiled=True
    )
    gain_grad = jnp.sum(gain_pieces, axis=0)
    return (hidden_grad[None], query_gradient[None], key_weight_grad, value_weight_grad, gain_grad)


def solution(mesh):
    return jax.shard_map(
        body,
        mesh=mesh,
        in_specs=(
            P(("groups", "dp"), "ctx", None),
            P(),
            P(("ctx", "dp"), None),
            P(("ctx", "dp"), None),
            P(("groups", "dp"), "ctx", None),
            P(("groups", "dp"), "ctx", None),
        ),
        out_specs=(
            P(("groups", "dp"), "ctx", None),
            P(("groups", "dp"), "ctx", None),
            P(("groups", "ctx", "dp"), None),
            P(("groups", "ctx", "dp"), None),
            P(("groups", "ctx", "dp")),
        ),
        check_vma=False,
    )
```

```python
import jax
import jax.numpy as jnp
from jax import lax
from jax.sharding import PartitionSpec as P

HEADS = 16
KV_HEADS = 8
HEAD_DIM = 128
WINDOW = 256


score_scale = 1.0 / 12.0
grad_scale = 1.0 / 64.0
norm_eps = 1e-06
rope_base = 10000.0
masked_score = -1e30


def from_behind(value, axis, steps):
    count = lax.axis_size(axis)
    initial, last = (max(0, -steps), min(count, count - steps))
    return lax.ppermute(value, axis, [(source, source + steps) for source in range(initial, last)])


def rotation(positions):
    half_dim = HEAD_DIM // 2
    frequency = rope_base ** (-jnp.arange(half_dim, dtype=jnp.float32) / half_dim)
    angles = positions.astype(jnp.float32)[:, None] * frequency[None, :]
    return (jnp.cos(angles)[:, None, :], jnp.sin(angles)[:, None, :])


def rotate(tensor, cosine_table, sine_table):
    half_dim = HEAD_DIM // 2
    front_half = tensor[..., :half_dim]
    back_half = tensor[..., half_dim:]
    return jnp.concatenate(
        [
            front_half * cosine_table - back_half * sine_table,
            back_half * cosine_table + front_half * sine_table,
        ],
        axis=-1,
    )


def rotate_back(tensor, cosine_table, sine_table):
    half_dim = HEAD_DIM // 2
    front_half = tensor[..., :half_dim]
    back_half = tensor[..., half_dim:]
    return jnp.concatenate(
        [
            front_half * cosine_table + back_half * sine_table,
            back_half * cosine_table - front_half * sine_table,
        ],
        axis=-1,
    )


def block_backward(
    query_block, grad_block, nearby_keys, near_values, distant_keys, far_values, has_prev
):
    tok_rows = query_block.shape[0]
    group_size = HEADS // KV_HEADS
    query_head_split = query_block.reshape(tok_rows, KV_HEADS, group_size, HEAD_DIM)
    gradient_heads = grad_block.reshape(tok_rows, KV_HEADS, group_size, HEAD_DIM)
    row_index = jnp.arange(tok_rows)[:, None]
    col_index = jnp.arange(tok_rows)[None, :]
    near_mask = (col_index <= row_index) & (row_index - col_index < WINDOW)
    far_mask = (col_index > row_index + tok_rows - WINDOW) & has_prev

    def pair_products(leftover_heads, key_row_block):
        return jnp.einsum(
            "qbak,wbk->baqw", leftover_heads, key_row_block, preferred_element_type=jnp.float32
        )

    near_scores = jnp.where(
        near_mask, pair_products(query_head_split, nearby_keys) * score_scale, masked_score
    )
    far_scores = jnp.where(
        far_mask, pair_products(query_head_split, distant_keys) * score_scale, masked_score
    )
    row_top = jnp.maximum(jnp.max(near_scores, -1), jnp.max(far_scores, -1))[..., None]
    near_exp = jnp.where(near_mask, jnp.exp(near_scores - row_top), 0.0)
    far_exp = jnp.where(far_mask, jnp.exp(far_scores - row_top), 0.0)
    row_total = (jnp.sum(near_exp, -1) + jnp.sum(far_exp, -1))[..., None]
    near_probs = near_exp / row_total
    far_probs = far_exp / row_total
    near_dprobs = pair_products(gradient_heads, near_values)
    far_dprobs = pair_products(gradient_heads, far_values)
    weighted = (jnp.sum(near_probs * near_dprobs, -1) + jnp.sum(far_probs * far_dprobs, -1))[
        ..., None
    ]
    nearby_score_gradient = (near_probs * (near_dprobs - weighted) * score_scale).astype(
        jnp.bfloat16
    )
    distant_score_gradient = (far_probs * (far_dprobs - weighted) * score_scale).astype(
        jnp.bfloat16
    )
    nearby_reduced = near_probs.astype(jnp.bfloat16)
    distant_reduced = far_probs.astype(jnp.bfloat16)
    query_gradient = jnp.einsum(
        "xqwc,cxi->wxqi", nearby_score_gradient, nearby_keys, preferred_element_type=jnp.float32
    )
    query_gradient = query_gradient + jnp.einsum(
        "xqwc,cxi->wxqi", distant_score_gradient, distant_keys, preferred_element_type=jnp.float32
    )
    nearby_key = jnp.einsum(
        "woia,iwon->awn",
        nearby_score_gradient,
        query_head_split,
        preferred_element_type=jnp.float32,
    )
    distant_key = jnp.einsum(
        "woia,iwon->awn",
        distant_score_gradient,
        query_head_split,
        preferred_element_type=jnp.float32,
    )
    nearby_value = jnp.einsum(
        "woia,iwon->awn", nearby_reduced, gradient_heads, preferred_element_type=jnp.float32
    )
    distant_value = jnp.einsum(
        "woia,iwon->awn", distant_reduced, gradient_heads, preferred_element_type=jnp.float32
    )
    query_out = query_gradient.reshape(tok_rows, HEADS * HEAD_DIM).astype(jnp.bfloat16)
    return (query_out, nearby_key, nearby_value, distant_key, distant_value)


def ring_order(n_ctx, n_dp):
    if n_ctx % 2 == 0:
        half = n_ctx // 2
        chips = [2 * a for a in range(half)] + [2 * a + 1 for a in reversed(range(half))]
    else:
        chips = list(range(n_ctx))
    return [chip * n_dp + core for chip in chips for core in range(n_dp)]


def ring_gather(piece, axes, ring):
    count = len(ring)
    ahead = [(ring[i], ring[(i + 1) % count]) for i in range(count)]
    behind = [(ring[i], ring[(i - 1) % count]) for i in range(count)]
    n_ahead = count // 2
    from_left, from_right = [], []
    moving = piece
    for _ in range(n_ahead):
        moving = lax.ppermute(moving, axes, ahead)
        from_left.append(moving)
    moving = piece
    for _ in range(count - 1 - n_ahead):
        moving = lax.ppermute(moving, axes, behind)
        from_right.append(moving)
    return [piece] + from_right + from_left[::-1]


def body(hidden_in, norm_gain, key_weight, value_weight, queries, out_grad):
    tok_rows = hidden_in.shape[1]
    key_width = key_weight.shape[1]
    inputs = hidden_in[0].astype(jnp.float32)
    inverse = lax.rsqrt(jnp.mean(inputs * inputs, axis=-1, keepdims=True) + norm_eps)
    normed = (inputs * inverse * norm_gain).astype(jnp.bfloat16)
    n_ctx = lax.axis_size("ctx")
    n_dp = lax.axis_size("dp")
    n_blocks = n_ctx * n_dp
    shard_rows = normed.shape[1] // n_blocks
    ring = ring_order(n_ctx, n_dp)
    ring_pos = [0] * n_blocks
    for place, member in enumerate(ring):
        ring_pos[member] = place
    my_place = jnp.array(ring_pos, jnp.int32)[lax.axis_index("ctx") * n_dp + lax.axis_index("dp")]
    offsets = jnp.arange(n_blocks, dtype=jnp.int32)
    source_of = jnp.array(ring, jnp.int32)[(my_place + offsets) % n_blocks]
    offset_of = (jnp.array(ring_pos, jnp.int32) - my_place) % n_blocks
    weights = ring_gather(
        jnp.concatenate([key_weight, value_weight], axis=1), ("ctx", "dp"), ring
    )
    normed_local = jnp.swapaxes(normed.reshape(tok_rows, n_blocks, shard_rows), 0, 1)
    normed_blocks = jnp.take(normed_local, source_of, axis=0)
    projected = jnp.dot(normed_blocks[0], weights[0], preferred_element_type=jnp.float32)
    for place in range(1, n_blocks):
        projected = projected + jnp.dot(
            normed_blocks[place], weights[place], preferred_element_type=jnp.float32
        )
    key_raw = projected[:, :key_width]
    value_rows = projected[:, key_width:].astype(jnp.bfloat16)
    ctx_index = lax.axis_index("ctx")
    positions = ctx_index * tok_rows + jnp.arange(tok_rows, dtype=jnp.int32)
    cosine_table, sine_table = rotation(positions)
    key_row_block = rotate(key_raw.reshape(tok_rows, KV_HEADS, HEAD_DIM), cosine_table, sine_table)
    key_row_block = key_row_block.astype(jnp.bfloat16).reshape(tok_rows, key_width)
    prev_key, prev_value = from_behind((key_row_block, value_rows), "ctx", 1)
    head_shape = (tok_rows, KV_HEADS, HEAD_DIM)
    query_gradient, nearby_key, nearby_value, distant_key, distant_value = block_backward(
        queries[0],
        out_grad[0],
        key_row_block.reshape(head_shape),
        value_rows.reshape(head_shape),
        prev_key.reshape(head_shape),
        prev_value.reshape(head_shape),
        ctx_index > 0,
    )
    incoming_key, incoming_value = from_behind(
        (distant_key.astype(jnp.bfloat16), distant_value.astype(jnp.bfloat16)), "ctx", -1
    )
    key_grad = nearby_key + incoming_key.astype(jnp.float32)
    value_grad = nearby_value + incoming_value.astype(jnp.float32)
    key_grad_raw = (
        rotate_back(key_grad, cosine_table, sine_table)
        .astype(jnp.bfloat16)
        .reshape(tok_rows, key_width)
    )
    value_low = value_grad.astype(jnp.bfloat16).reshape(tok_rows, key_width)
    grads_cat = jnp.concatenate([key_grad_raw, value_low], axis=1)

    def block_term(place):
        term = jnp.einsum(
            "td,tk->dk", normed_blocks[place], grads_cat, preferred_element_type=jnp.float32
        )
        return (term * grad_scale).astype(jnp.bfloat16).astype(jnp.float32)

    ahead = [(ring[i], ring[(i + 1) % n_blocks]) for i in range(n_blocks)]
    behind = [(ring[i], ring[(i - 1) % n_blocks]) for i in range(n_blocks)]
    n_ahead = n_blocks // 2
    carried = block_term(n_ahead)
    for step in range(2, n_ahead + 1):
        arrived = lax.ppermute(carried.astype(jnp.bfloat16), ("ctx", "dp"), ahead)
        carried = arrived.astype(jnp.float32) + block_term(n_ahead + 1 - step)
    from_left = lax.ppermute(carried.astype(jnp.bfloat16), ("ctx", "dp"), ahead)
    n_behind = n_blocks - 1 - n_ahead
    carried = block_term(n_blocks - n_behind)
    for step in range(2, n_behind + 1):
        arrived = lax.ppermute(carried.astype(jnp.bfloat16), ("ctx", "dp"), behind)
        carried = arrived.astype(jnp.float32) + block_term(n_blocks - n_behind - 1 + step)
    from_right = lax.ppermute(carried.astype(jnp.bfloat16), ("ctx", "dp"), behind)
    stacked = block_term(0) + from_left.astype(jnp.float32) + from_right.astype(jnp.float32)
    key_weight_grad = stacked[:, :key_width]
    value_weight_grad = stacked[:, key_width:]
    normed_grad = jnp.stack(
        [
            jnp.einsum("tk,rk->tr", grads_cat, piece, preferred_element_type=jnp.float32)
            for piece in weights
        ]
    )
    normed_grad = jnp.swapaxes(jnp.take(normed_grad, offset_of, axis=0), 0, 1)
    normed_grad = normed_grad.reshape(tok_rows, -1)
    scaled = normed_grad * norm_gain
    cubed = inverse * inverse * inverse
    hidden_grad = (
        inverse * scaled - inputs * cubed * jnp.mean(scaled * inputs, axis=-1, keepdims=True)
    ).astype(jnp.bfloat16)
    gain_term = jnp.sum(normed_grad * inputs * inverse, axis=0) * grad_scale
    gain_pieces = lax.all_to_all(
        gain_term.reshape(n_blocks, shard_rows), ("ctx", "dp"), 0, 0, tiled=True
    )
    gain_grad = jnp.sum(gain_pieces, axis=0)
    return (hidden_grad[None], query_gradient[None], key_weight_grad, value_weight_grad, gain_grad)


def solution(mesh):
    return jax.shard_map(
        body,
        mesh=mesh,
        in_specs=(
            P(("groups", "dp"), "ctx", None),
            P(),
            P(("ctx", "dp"), None),
            P(("ctx", "dp"), None),
            P(("groups", "dp"), "ctx", None),
            P(("groups", "dp"), "ctx", None),
        ),
        out_specs=(
            P(("groups", "dp"), "ctx", None),
            P(("groups", "dp"), "ctx", None),
            P(("groups", "ctx", "dp"), None),
            P(("groups", "ctx", "dp"), None),
            P(("groups", "ctx", "dp")),
        ),
        check_vma=False,
    )
```

```python
import jax
import jax.numpy as jnp
from jax import lax
from jax.sharding import PartitionSpec as P

HEADS = 16
KV_HEADS = 8
HEAD_DIM = 128
WINDOW = 256


score_scale = 1.0 / 12.0
grad_scale = 1.0 / 64.0
norm_eps = 1e-06
rope_base = 10000.0
masked_score = -1e30


def from_behind(value, axis, steps):
    count = lax.axis_size(axis)
    initial, last = (max(0, -steps), min(count, count - steps))
    return lax.ppermute(value, axis, [(source, source + steps) for source in range(initial, last)])


def rotation(positions):
    half_dim = HEAD_DIM // 2
    frequency = rope_base ** (-jnp.arange(half_dim, dtype=jnp.float32) / half_dim)
    angles = positions.astype(jnp.float32)[:, None] * frequency[None, :]
    return (jnp.cos(angles)[:, None, :], jnp.sin(angles)[:, None, :])


def rotate(tensor, cosine_table, sine_table):
    half_dim = HEAD_DIM // 2
    front_half = tensor[..., :half_dim]
    back_half = tensor[..., half_dim:]
    return jnp.concatenate(
        [
            front_half * cosine_table - back_half * sine_table,
            back_half * cosine_table + front_half * sine_table,
        ],
        axis=-1,
    )


def rotate_back(tensor, cosine_table, sine_table):
    half_dim = HEAD_DIM // 2
    front_half = tensor[..., :half_dim]
    back_half = tensor[..., half_dim:]
    return jnp.concatenate(
        [
            front_half * cosine_table + back_half * sine_table,
            back_half * cosine_table - front_half * sine_table,
        ],
        axis=-1,
    )


def block_backward(
    query_block, grad_block, nearby_keys, near_values, distant_keys, far_values, has_prev
):
    tok_rows = query_block.shape[0]
    kv_heads = nearby_keys.shape[1]
    group_size = HEADS // KV_HEADS
    query_head_split = query_block.reshape(tok_rows, kv_heads, group_size, HEAD_DIM)
    gradient_heads = grad_block.reshape(tok_rows, kv_heads, group_size, HEAD_DIM)
    row_index = jnp.arange(tok_rows)[:, None]
    col_index = jnp.arange(tok_rows)[None, :]
    near_mask = (col_index <= row_index) & (row_index - col_index < WINDOW)
    far_mask = (col_index > row_index + tok_rows - WINDOW) & has_prev

    def pair_products(leftover_heads, key_row_block):
        return jnp.einsum(
            "qbak,wbk->baqw", leftover_heads, key_row_block, preferred_element_type=jnp.float32
        )

    near_scores = jnp.where(
        near_mask, pair_products(query_head_split, nearby_keys) * score_scale, masked_score
    )
    far_scores = jnp.where(
        far_mask, pair_products(query_head_split, distant_keys) * score_scale, masked_score
    )
    row_top = jnp.maximum(jnp.max(near_scores, -1), jnp.max(far_scores, -1))[..., None]
    near_exp = jnp.where(near_mask, jnp.exp(near_scores - row_top), 0.0)
    far_exp = jnp.where(far_mask, jnp.exp(far_scores - row_top), 0.0)
    row_total = (jnp.sum(near_exp, -1) + jnp.sum(far_exp, -1))[..., None]
    near_probs = near_exp / row_total
    far_probs = far_exp / row_total
    near_dprobs = pair_products(gradient_heads, near_values)
    far_dprobs = pair_products(gradient_heads, far_values)
    weighted = (jnp.sum(near_probs * near_dprobs, -1) + jnp.sum(far_probs * far_dprobs, -1))[
        ..., None
    ]
    nearby_score_gradient = (near_probs * (near_dprobs - weighted) * score_scale).astype(
        jnp.bfloat16
    )
    distant_score_gradient = (far_probs * (far_dprobs - weighted) * score_scale).astype(
        jnp.bfloat16
    )
    nearby_reduced = near_probs.astype(jnp.bfloat16)
    distant_reduced = far_probs.astype(jnp.bfloat16)
    query_gradient = jnp.einsum(
        "xqwc,cxi->wxqi", nearby_score_gradient, nearby_keys, preferred_element_type=jnp.float32
    )
    query_gradient = query_gradient + jnp.einsum(
        "xqwc,cxi->wxqi", distant_score_gradient, distant_keys, preferred_element_type=jnp.float32
    )
    nearby_key = jnp.einsum(
        "woia,iwon->awn",
        nearby_score_gradient,
        query_head_split,
        preferred_element_type=jnp.float32,
    )
    distant_key = jnp.einsum(
        "woia,iwon->awn",
        distant_score_gradient,
        query_head_split,
        preferred_element_type=jnp.float32,
    )
    nearby_value = jnp.einsum(
        "woia,iwon->awn", nearby_reduced, gradient_heads, preferred_element_type=jnp.float32
    )
    distant_value = jnp.einsum(
        "woia,iwon->awn", distant_reduced, gradient_heads, preferred_element_type=jnp.float32
    )
    query_out = query_gradient.reshape(tok_rows, -1).astype(jnp.bfloat16)
    return (query_out, nearby_key, nearby_value, distant_key, distant_value)


def ring_order(n_ctx, n_dp):
    if n_ctx % 2 == 0:
        half = n_ctx // 2
        chips = [2 * a for a in range(half)] + [2 * a + 1 for a in reversed(range(half))]
    else:
        chips = list(range(n_ctx))
    return [chip * n_dp + core for chip in chips for core in range(n_dp)]


def ring_gather(piece, axes, ring):
    count = len(ring)
    ahead = [(ring[i], ring[(i + 1) % count]) for i in range(count)]
    behind = [(ring[i], ring[(i - 1) % count]) for i in range(count)]
    n_ahead = count // 2
    from_left, from_right = [], []
    moving = piece
    for _ in range(n_ahead):
        moving = lax.ppermute(moving, axes, ahead)
        from_left.append(moving)
    moving = piece
    for _ in range(count - 1 - n_ahead):
        moving = lax.ppermute(moving, axes, behind)
        from_right.append(moving)
    return [piece] + from_right + from_left[::-1]


def body(hidden_in, norm_gain, key_weight, value_weight, queries, out_grad):
    tok_rows = hidden_in.shape[1]
    key_width = key_weight.shape[1]
    inputs = hidden_in[0].astype(jnp.float32)
    inverse = lax.rsqrt(jnp.mean(inputs * inputs, axis=-1, keepdims=True) + norm_eps)
    normed = (inputs * inverse * norm_gain).astype(jnp.bfloat16)
    n_ctx = lax.axis_size("ctx")
    n_dp = lax.axis_size("dp")
    n_blocks = n_ctx * n_dp
    shard_rows = normed.shape[1] // n_blocks
    ring = ring_order(n_ctx, n_dp)
    ring_pos = [0] * n_blocks
    for place, member in enumerate(ring):
        ring_pos[member] = place
    my_place = jnp.array(ring_pos, jnp.int32)[lax.axis_index("ctx") * n_dp + lax.axis_index("dp")]
    offsets = jnp.arange(n_blocks, dtype=jnp.int32)
    source_of = jnp.array(ring, jnp.int32)[(my_place + offsets) % n_blocks]
    offset_of = (jnp.array(ring_pos, jnp.int32) - my_place) % n_blocks
    normed_local = jnp.swapaxes(normed.reshape(tok_rows, n_blocks, shard_rows), 0, 1)
    normed_blocks = jnp.take(normed_local, source_of, axis=0)
    ctx_index = lax.axis_index("ctx")
    positions = ctx_index * tok_rows + jnp.arange(tok_rows, dtype=jnp.int32)
    cosine_table, sine_table = rotation(positions)
    ahead = [(ring[i], ring[(i + 1) % n_blocks]) for i in range(n_blocks)]
    behind = [(ring[i], ring[(i - 1) % n_blocks]) for i in range(n_blocks)]
    n_ahead = n_blocks // 2
    n_behind = n_blocks - 1 - n_ahead

    def ring_reduce(grads_cat):
        def block_term(place):
            term = jnp.einsum(
                "td,tk->dk", normed_blocks[place], grads_cat, preferred_element_type=jnp.float32
            )
            return (term * grad_scale).astype(jnp.bfloat16).astype(jnp.float32)

        carried = block_term(n_ahead)
        for step in range(2, n_ahead + 1):
            arrived = lax.ppermute(carried.astype(jnp.bfloat16), ("ctx", "dp"), ahead)
            carried = arrived.astype(jnp.float32) + block_term(n_ahead + 1 - step)
        from_left = lax.ppermute(carried.astype(jnp.bfloat16), ("ctx", "dp"), ahead)
        carried = block_term(n_blocks - n_behind)
        for step in range(2, n_behind + 1):
            arrived = lax.ppermute(carried.astype(jnp.bfloat16), ("ctx", "dp"), behind)
            carried = arrived.astype(jnp.float32) + block_term(n_blocks - n_behind - 1 + step)
        from_right = lax.ppermute(carried.astype(jnp.bfloat16), ("ctx", "dp"), behind)
        return block_term(0) + from_left.astype(jnp.float32) + from_right.astype(jnp.float32)

    n_parts = 2
    part_width = key_width // n_parts
    part_heads = part_width // HEAD_DIM
    query_width = queries.shape[2] // n_parts
    weight_parts, grad_parts, query_parts, weight_grad_parts = [], [], [], []
    for part in range(n_parts):
        kv_cols = slice(part * part_width, (part + 1) * part_width)
        q_cols = slice(part * query_width, (part + 1) * query_width)
        weights = ring_gather(
            jnp.concatenate([key_weight[:, kv_cols], value_weight[:, kv_cols]], axis=1),
            ("ctx", "dp"),
            ring,
        )
        projected = jnp.dot(normed_blocks[0], weights[0], preferred_element_type=jnp.float32)
        for place in range(1, n_blocks):
            projected = projected + jnp.dot(
                normed_blocks[place], weights[place], preferred_element_type=jnp.float32
            )
        key_raw = projected[:, :part_width]
        value_rows = projected[:, part_width:].astype(jnp.bfloat16)
        head_shape = (tok_rows, part_heads, HEAD_DIM)
        key_row_block = rotate(key_raw.reshape(head_shape), cosine_table, sine_table)
        key_row_block = key_row_block.astype(jnp.bfloat16).reshape(tok_rows, part_width)
        prev_key, prev_value = from_behind((key_row_block, value_rows), "ctx", 1)
        query_gradient, nearby_key, nearby_value, distant_key, distant_value = block_backward(
            queries[0][:, q_cols],
            out_grad[0][:, q_cols],
            key_row_block.reshape(head_shape),
            value_rows.reshape(head_shape),
            prev_key.reshape(head_shape),
            prev_value.reshape(head_shape),
            ctx_index > 0,
        )
        incoming_key, incoming_value = from_behind(
            (distant_key.astype(jnp.bfloat16), distant_value.astype(jnp.bfloat16)), "ctx", -1
        )
        key_grad = nearby_key + incoming_key.astype(jnp.float32)
        value_grad = nearby_value + incoming_value.astype(jnp.float32)
        key_grad_raw = (
            rotate_back(key_grad, cosine_table, sine_table)
            .astype(jnp.bfloat16)
            .reshape(tok_rows, part_width)
        )
        value_low = value_grad.astype(jnp.bfloat16).reshape(tok_rows, part_width)
        grads_cat = jnp.concatenate([key_grad_raw, value_low], axis=1)
        weight_parts.append(weights)
        grad_parts.append(grads_cat)
        query_parts.append(query_gradient)
        weight_grad_parts.append(ring_reduce(grads_cat))
    query_gradient = jnp.concatenate(query_parts, axis=1)
    key_weight_grad = jnp.concatenate([rows[:, :part_width] for rows in weight_grad_parts], axis=1)
    value_weight_grad = jnp.concatenate(
        [rows[:, part_width:] for rows in weight_grad_parts], axis=1
    )
    normed_grad = jnp.stack(
        [
            sum(
                jnp.einsum("tk,rk->tr", grads, pieces[place], preferred_element_type=jnp.float32)
                for grads, pieces in zip(grad_parts, weight_parts)
            )
            for place in range(n_blocks)
        ]
    )
    normed_grad = jnp.swapaxes(jnp.take(normed_grad, offset_of, axis=0), 0, 1)
    normed_grad = normed_grad.reshape(tok_rows, -1)
    scaled = normed_grad * norm_gain
    cubed = inverse * inverse * inverse
    hidden_grad = (
        inverse * scaled - inputs * cubed * jnp.mean(scaled * inputs, axis=-1, keepdims=True)
    ).astype(jnp.bfloat16)
    gain_term = jnp.sum(normed_grad * inputs * inverse, axis=0) * grad_scale
    gain_pieces = lax.all_to_all(
        gain_term.reshape(n_blocks, shard_rows), ("ctx", "dp"), 0, 0, tiled=True
    )
    gain_grad = jnp.sum(gain_pieces, axis=0)
    return (hidden_grad[None], query_gradient[None], key_weight_grad, value_weight_grad, gain_grad)


def solution(mesh):
    return jax.shard_map(
        body,
        mesh=mesh,
        in_specs=(
            P(("groups", "dp"), "ctx", None),
            P(),
            P(("ctx", "dp"), None),
            P(("ctx", "dp"), None),
            P(("groups", "dp"), "ctx", None),
            P(("groups", "dp"), "ctx", None),
        ),
        out_specs=(
            P(("groups", "dp"), "ctx", None),
            P(("groups", "dp"), "ctx", None),
            P(("groups", "ctx", "dp"), None),
            P(("groups", "ctx", "dp"), None),
            P(("groups", "ctx", "dp")),
        ),
        check_vma=False,
    )
```

```python
import jax
import jax.numpy as jnp
from jax import lax
from jax.sharding import PartitionSpec as P

HEADS = 16
KV_HEADS = 8
HEAD_DIM = 128
WINDOW = 256


score_scale = 1.0 / 12.0
grad_scale = 1.0 / 64.0
norm_eps = 1e-06
rope_base = 10000.0
masked_score = -1e30


def from_behind(value, axis, steps):
    count = lax.axis_size(axis)
    initial, last = (max(0, -steps), min(count, count - steps))
    return lax.ppermute(value, axis, [(source, source + steps) for source in range(initial, last)])


def rotation(positions):
    half_dim = HEAD_DIM // 2
    frequency = rope_base ** (-jnp.arange(half_dim, dtype=jnp.float32) / half_dim)
    angles = positions.astype(jnp.float32)[:, None] * frequency[None, :]
    return (jnp.cos(angles)[:, None, :], jnp.sin(angles)[:, None, :])


def rotate(tensor, cosine_table, sine_table):
    half_dim = HEAD_DIM // 2
    front_half = tensor[..., :half_dim]
    back_half = tensor[..., half_dim:]
    return jnp.concatenate(
        [
            front_half * cosine_table - back_half * sine_table,
            back_half * cosine_table + front_half * sine_table,
        ],
        axis=-1,
    )


def rotate_back(tensor, cosine_table, sine_table):
    half_dim = HEAD_DIM // 2
    front_half = tensor[..., :half_dim]
    back_half = tensor[..., half_dim:]
    return jnp.concatenate(
        [
            front_half * cosine_table + back_half * sine_table,
            back_half * cosine_table - front_half * sine_table,
        ],
        axis=-1,
    )


def block_backward(
    query_block, grad_block, nearby_keys, near_values, distant_keys, far_values, has_prev
):
    tok_rows = query_block.shape[0]
    group_size = HEADS // KV_HEADS
    query_head_split = query_block.reshape(tok_rows, KV_HEADS, group_size, HEAD_DIM)
    gradient_heads = grad_block.reshape(tok_rows, KV_HEADS, group_size, HEAD_DIM)
    row_index = jnp.arange(tok_rows)[:, None]
    col_index = jnp.arange(tok_rows)[None, :]
    near_mask = (col_index <= row_index) & (row_index - col_index < WINDOW)
    far_mask = (col_index > row_index + tok_rows - WINDOW) & has_prev

    def pair_products(leftover_heads, key_row_block):
        return jnp.einsum(
            "qbak,wbk->baqw", leftover_heads, key_row_block, preferred_element_type=jnp.float32
        )

    near_scores = jnp.where(
        near_mask, pair_products(query_head_split, nearby_keys) * score_scale, masked_score
    )
    far_scores = jnp.where(
        far_mask, pair_products(query_head_split, distant_keys) * score_scale, masked_score
    )
    row_top = jnp.maximum(jnp.max(near_scores, -1), jnp.max(far_scores, -1))[..., None]
    near_exp = jnp.where(near_mask, jnp.exp(near_scores - row_top), 0.0)
    far_exp = jnp.where(far_mask, jnp.exp(far_scores - row_top), 0.0)
    row_total = (jnp.sum(near_exp, -1) + jnp.sum(far_exp, -1))[..., None]
    near_probs = near_exp / row_total
    far_probs = far_exp / row_total
    near_dprobs = pair_products(gradient_heads, near_values)
    far_dprobs = pair_products(gradient_heads, far_values)
    weighted = (jnp.sum(near_probs * near_dprobs, -1) + jnp.sum(far_probs * far_dprobs, -1))[
        ..., None
    ]
    nearby_score_gradient = (near_probs * (near_dprobs - weighted) * score_scale).astype(
        jnp.bfloat16
    )
    distant_score_gradient = (far_probs * (far_dprobs - weighted) * score_scale).astype(
        jnp.bfloat16
    )
    nearby_reduced = near_probs.astype(jnp.bfloat16)
    distant_reduced = far_probs.astype(jnp.bfloat16)
    query_gradient = jnp.einsum(
        "xqwc,cxi->wxqi", nearby_score_gradient, nearby_keys, preferred_element_type=jnp.float32
    )
    query_gradient = query_gradient + jnp.einsum(
        "xqwc,cxi->wxqi", distant_score_gradient, distant_keys, preferred_element_type=jnp.float32
    )
    nearby_key = jnp.einsum(
        "woia,iwon->awn",
        nearby_score_gradient,
        query_head_split,
        preferred_element_type=jnp.float32,
    )
    distant_key = jnp.einsum(
        "woia,iwon->awn",
        distant_score_gradient,
        query_head_split,
        preferred_element_type=jnp.float32,
    )
    nearby_value = jnp.einsum(
        "woia,iwon->awn", nearby_reduced, gradient_heads, preferred_element_type=jnp.float32
    )
    distant_value = jnp.einsum(
        "woia,iwon->awn", distant_reduced, gradient_heads, preferred_element_type=jnp.float32
    )
    query_out = query_gradient.reshape(tok_rows, HEADS * HEAD_DIM).astype(jnp.bfloat16)
    return (query_out, nearby_key, nearby_value, distant_key, distant_value)


def ring_order(n_ctx, n_dp):
    if n_ctx % 2 == 0:
        half = n_ctx // 2
        chips = [2 * a for a in range(half)] + [2 * a + 1 for a in reversed(range(half))]
    else:
        chips = list(range(n_ctx))
    return [chip * n_dp + core for chip in chips for core in range(n_dp)]


def ring_gather(piece, axes, ring):
    count = len(ring)
    ahead = [(ring[i], ring[(i + 1) % count]) for i in range(count)]
    behind = [(ring[i], ring[(i - 1) % count]) for i in range(count)]
    n_ahead = count // 2
    from_left, from_right = [], []
    moving = piece
    for _ in range(n_ahead):
        moving = lax.ppermute(moving, axes, ahead)
        from_left.append(moving)
    moving = piece
    for _ in range(count - 1 - n_ahead):
        moving = lax.ppermute(moving, axes, behind)
        from_right.append(moving)
    return [piece] + from_right + from_left[::-1]


def body(hidden_in, norm_gain, key_weight, value_weight, queries, out_grad):
    tok_rows = hidden_in.shape[1]
    key_width = key_weight.shape[1]
    inputs = hidden_in[0].astype(jnp.float32)
    inverse = lax.rsqrt(jnp.mean(inputs * inputs, axis=-1, keepdims=True) + norm_eps)
    normed = (inputs * inverse * norm_gain).astype(jnp.bfloat16)
    n_ctx = lax.axis_size("ctx")
    n_dp = lax.axis_size("dp")
    n_blocks = n_ctx * n_dp
    shard_rows = normed.shape[1] // n_blocks
    ring = ring_order(n_ctx, n_dp)
    ring_pos = [0] * n_blocks
    for place, member in enumerate(ring):
        ring_pos[member] = place
    my_place = jnp.array(ring_pos, jnp.int32)[lax.axis_index("ctx") * n_dp + lax.axis_index("dp")]
    offsets = jnp.arange(n_blocks, dtype=jnp.int32)
    source_of = jnp.array(ring, jnp.int32)[(my_place + offsets) % n_blocks]
    offset_of = (jnp.array(ring_pos, jnp.int32) - my_place) % n_blocks
    weights = ring_gather(
        jnp.concatenate([key_weight, value_weight], axis=1), ("ctx", "dp"), ring
    )
    normed_local = jnp.swapaxes(normed.reshape(tok_rows, n_blocks, shard_rows), 0, 1)
    normed_blocks = jnp.take(normed_local, source_of, axis=0)
    projected = jnp.dot(normed_blocks[0], weights[0], preferred_element_type=jnp.float32)
    for place in range(1, n_blocks):
        projected = projected + jnp.dot(
            normed_blocks[place], weights[place], preferred_element_type=jnp.float32
        )
    key_raw = projected[:, :key_width]
    value_rows = projected[:, key_width:].astype(jnp.bfloat16)
    ctx_index = lax.axis_index("ctx")
    positions = ctx_index * tok_rows + jnp.arange(tok_rows, dtype=jnp.int32)
    cosine_table, sine_table = rotation(positions)
    key_row_block = rotate(key_raw.reshape(tok_rows, KV_HEADS, HEAD_DIM), cosine_table, sine_table)
    key_row_block = key_row_block.astype(jnp.bfloat16).reshape(tok_rows, key_width)
    prev_key, prev_value = from_behind((key_row_block, value_rows), "ctx", 1)
    head_shape = (tok_rows, KV_HEADS, HEAD_DIM)
    query_gradient, nearby_key, nearby_value, distant_key, distant_value = block_backward(
        queries[0],
        out_grad[0],
        key_row_block.reshape(head_shape),
        value_rows.reshape(head_shape),
        prev_key.reshape(head_shape),
        prev_value.reshape(head_shape),
        ctx_index > 0,
    )
    incoming_key, incoming_value = from_behind(
        (distant_key.astype(jnp.bfloat16), distant_value.astype(jnp.bfloat16)), "ctx", -1
    )
    key_grad = nearby_key + incoming_key.astype(jnp.float32)
    value_grad = nearby_value + incoming_value.astype(jnp.float32)
    key_grad_raw = (
        rotate_back(key_grad, cosine_table, sine_table)
        .astype(jnp.bfloat16)
        .reshape(tok_rows, key_width)
    )
    value_low = value_grad.astype(jnp.bfloat16).reshape(tok_rows, key_width)
    grads_cat = jnp.concatenate([key_grad_raw, value_low], axis=1)

    def block_term(place):
        term = jnp.einsum(
            "td,tk->dk", normed_blocks[place], grads_cat, preferred_element_type=jnp.float32
        )
        return lax.optimization_barrier((term * grad_scale).astype(jnp.bfloat16)).astype(
            jnp.float32
        )

    ahead = [(ring[i], ring[(i + 1) % n_blocks]) for i in range(n_blocks)]
    behind = [(ring[i], ring[(i - 1) % n_blocks]) for i in range(n_blocks)]
    n_ahead = n_blocks // 2
    carried = block_term(n_ahead)
    for step in range(2, n_ahead + 1):
        arrived = lax.ppermute(carried.astype(jnp.bfloat16), ("ctx", "dp"), ahead)
        carried = arrived.astype(jnp.float32) + block_term(n_ahead + 1 - step)
    from_left = lax.ppermute(carried.astype(jnp.bfloat16), ("ctx", "dp"), ahead)
    n_behind = n_blocks - 1 - n_ahead
    carried = block_term(n_blocks - n_behind)
    for step in range(2, n_behind + 1):
        arrived = lax.ppermute(carried.astype(jnp.bfloat16), ("ctx", "dp"), behind)
        carried = arrived.astype(jnp.float32) + block_term(n_blocks - n_behind - 1 + step)
    from_right = lax.ppermute(carried.astype(jnp.bfloat16), ("ctx", "dp"), behind)
    stacked = block_term(0) + from_left.astype(jnp.float32) + from_right.astype(jnp.float32)
    key_weight_grad = stacked[:, :key_width]
    value_weight_grad = stacked[:, key_width:]
    normed_grad = jnp.stack(
        [
            jnp.einsum("tk,rk->tr", grads_cat, piece, preferred_element_type=jnp.float32)
            for piece in weights
        ]
    )
    normed_grad = jnp.swapaxes(jnp.take(normed_grad, offset_of, axis=0), 0, 1)
    normed_grad = normed_grad.reshape(tok_rows, -1)
    scaled = normed_grad * norm_gain
    cubed = inverse * inverse * inverse
    hidden_grad = (
        inverse * scaled - inputs * cubed * jnp.mean(scaled * inputs, axis=-1, keepdims=True)
    ).astype(jnp.bfloat16)
    gain_term = jnp.sum(normed_grad * inputs * inverse, axis=0) * grad_scale
    gain_pieces = lax.all_to_all(
        gain_term.reshape(n_blocks, shard_rows), ("ctx", "dp"), 0, 0, tiled=True
    )
    gain_grad = jnp.sum(gain_pieces, axis=0)
    return (hidden_grad[None], query_gradient[None], key_weight_grad, value_weight_grad, gain_grad)


def solution(mesh):
    return jax.shard_map(
        body,
        mesh=mesh,
        in_specs=(
            P(("groups", "dp"), "ctx", None),
            P(),
            P(("ctx", "dp"), None),
            P(("ctx", "dp"), None),
            P(("groups", "dp"), "ctx", None),
            P(("groups", "dp"), "ctx", None),
        ),
        out_specs=(
            P(("groups", "dp"), "ctx", None),
            P(("groups", "dp"), "ctx", None),
            P(("groups", "ctx", "dp"), None),
            P(("groups", "ctx", "dp"), None),
            P(("groups", "ctx", "dp")),
        ),
        check_vma=False,
    )
```

```python
import jax
import jax.numpy as jnp
from jax import lax
from jax.sharding import PartitionSpec as P

HEADS = 16
KV_HEADS = 8
HEAD_DIM = 128
WINDOW = 256


score_scale = 1.0 / 12.0
grad_scale = 1.0 / 64.0
norm_eps = 1e-06
rope_base = 10000.0
masked_score = -1e30


def from_behind(value, axis, steps):
    count = lax.axis_size(axis)
    initial, last = (max(0, -steps), min(count, count - steps))
    return lax.ppermute(value, axis, [(source, source + steps) for source in range(initial, last)])


def rotation(positions):
    half_dim = HEAD_DIM // 2
    frequency = rope_base ** (-jnp.arange(half_dim, dtype=jnp.float32) / half_dim)
    angles = positions.astype(jnp.float32)[:, None] * frequency[None, :]
    return (jnp.cos(angles)[:, None, :], jnp.sin(angles)[:, None, :])


def rotate(tensor, cosine_table, sine_table):
    half_dim = HEAD_DIM // 2
    front_half = tensor[..., :half_dim]
    back_half = tensor[..., half_dim:]
    return jnp.concatenate(
        [
            front_half * cosine_table - back_half * sine_table,
            back_half * cosine_table + front_half * sine_table,
        ],
        axis=-1,
    )


def rotate_back(tensor, cosine_table, sine_table):
    half_dim = HEAD_DIM // 2
    front_half = tensor[..., :half_dim]
    back_half = tensor[..., half_dim:]
    return jnp.concatenate(
        [
            front_half * cosine_table + back_half * sine_table,
            back_half * cosine_table - front_half * sine_table,
        ],
        axis=-1,
    )


def block_backward(
    query_block, grad_block, nearby_keys, near_values, distant_keys, far_values, has_prev
):
    tok_rows = query_block.shape[0]
    group_size = HEADS // KV_HEADS
    query_head_split = query_block.reshape(tok_rows, KV_HEADS, group_size, HEAD_DIM)
    gradient_heads = grad_block.reshape(tok_rows, KV_HEADS, group_size, HEAD_DIM)
    row_index = jnp.arange(tok_rows)[:, None]
    col_index = jnp.arange(tok_rows)[None, :]
    near_mask = (col_index <= row_index) & (row_index - col_index < WINDOW)
    far_mask = (col_index > row_index + tok_rows - WINDOW) & has_prev

    def pair_products(leftover_heads, key_row_block):
        return jnp.einsum(
            "qbak,wbk->baqw", leftover_heads, key_row_block, preferred_element_type=jnp.float32
        )

    near_scores = jnp.where(
        near_mask, pair_products(query_head_split, nearby_keys) * score_scale, masked_score
    )
    far_scores = jnp.where(
        far_mask, pair_products(query_head_split, distant_keys) * score_scale, masked_score
    )
    row_top = jnp.maximum(jnp.max(near_scores, -1), jnp.max(far_scores, -1))[..., None]
    near_exp = jnp.where(near_mask, jnp.exp(near_scores - row_top), 0.0)
    far_exp = jnp.where(far_mask, jnp.exp(far_scores - row_top), 0.0)
    row_total = (jnp.sum(near_exp, -1) + jnp.sum(far_exp, -1))[..., None]
    near_probs = near_exp / row_total
    far_probs = far_exp / row_total
    near_dprobs = pair_products(gradient_heads, near_values)
    far_dprobs = pair_products(gradient_heads, far_values)
    weighted = (jnp.sum(near_probs * near_dprobs, -1) + jnp.sum(far_probs * far_dprobs, -1))[
        ..., None
    ]
    nearby_score_gradient = (near_probs * (near_dprobs - weighted) * score_scale).astype(
        jnp.bfloat16
    )
    distant_score_gradient = (far_probs * (far_dprobs - weighted) * score_scale).astype(
        jnp.bfloat16
    )
    nearby_reduced = near_probs.astype(jnp.bfloat16)
    distant_reduced = far_probs.astype(jnp.bfloat16)
    query_gradient = jnp.einsum(
        "xqwc,cxi->wxqi", nearby_score_gradient, nearby_keys, preferred_element_type=jnp.float32
    )
    query_gradient = query_gradient + jnp.einsum(
        "xqwc,cxi->wxqi", distant_score_gradient, distant_keys, preferred_element_type=jnp.float32
    )
    nearby_key = jnp.einsum(
        "woia,iwon->awn",
        nearby_score_gradient,
        query_head_split,
        preferred_element_type=jnp.float32,
    )
    distant_key = jnp.einsum(
        "woia,iwon->awn",
        distant_score_gradient,
        query_head_split,
        preferred_element_type=jnp.float32,
    )
    nearby_value = jnp.einsum(
        "woia,iwon->awn", nearby_reduced, gradient_heads, preferred_element_type=jnp.float32
    )
    distant_value = jnp.einsum(
        "woia,iwon->awn", distant_reduced, gradient_heads, preferred_element_type=jnp.float32
    )
    query_out = query_gradient.reshape(tok_rows, HEADS * HEAD_DIM).astype(jnp.bfloat16)
    return (query_out, nearby_key, nearby_value, distant_key, distant_value)


def ring_order(n_ctx, n_dp):
    if n_ctx % 2 == 0:
        half = n_ctx // 2
        chips = [2 * a for a in range(half)] + [2 * a + 1 for a in reversed(range(half))]
    else:
        chips = list(range(n_ctx))
    return [chip * n_dp + core for chip in chips for core in range(n_dp)]


def ring_gather(piece, axes, ring):
    count = len(ring)
    ahead = [(ring[i], ring[(i + 1) % count]) for i in range(count)]
    behind = [(ring[i], ring[(i - 1) % count]) for i in range(count)]
    n_ahead = count // 2
    from_left, from_right = [], []
    moving = piece
    for _ in range(n_ahead):
        moving = lax.ppermute(moving, axes, ahead)
        from_left.append(moving)
    moving = piece
    for _ in range(count - 1 - n_ahead):
        moving = lax.ppermute(moving, axes, behind)
        from_right.append(moving)
    return [piece] + from_right + from_left[::-1]


def body(hidden_in, norm_gain, key_weight, value_weight, queries, out_grad):
    tok_rows = hidden_in.shape[1]
    key_width = key_weight.shape[1]
    inputs = hidden_in[0].astype(jnp.float32)
    inverse = lax.rsqrt(jnp.mean(inputs * inputs, axis=-1, keepdims=True) + norm_eps)
    normed = (inputs * inverse * norm_gain).astype(jnp.bfloat16)
    n_ctx = lax.axis_size("ctx")
    n_dp = lax.axis_size("dp")
    n_blocks = n_ctx * n_dp
    shard_rows = normed.shape[1] // n_blocks
    ring = ring_order(n_ctx, n_dp)
    ring_pos = [0] * n_blocks
    for place, member in enumerate(ring):
        ring_pos[member] = place
    my_place = jnp.array(ring_pos, jnp.int32)[lax.axis_index("ctx") * n_dp + lax.axis_index("dp")]
    offsets = jnp.arange(n_blocks, dtype=jnp.int32)
    source_of = jnp.array(ring, jnp.int32)[(my_place + offsets) % n_blocks]
    offset_of = (jnp.array(ring_pos, jnp.int32) - my_place) % n_blocks
    weights = ring_gather(
        jnp.concatenate([key_weight, value_weight], axis=1), ("ctx", "dp"), ring
    )
    normed_local = jnp.swapaxes(normed.reshape(tok_rows, n_blocks, shard_rows), 0, 1)
    normed_blocks = jnp.take(normed_local, source_of, axis=0)
    projected = jnp.dot(normed_blocks[0], weights[0], preferred_element_type=jnp.float32)
    for place in range(1, n_blocks):
        projected = projected + jnp.dot(
            normed_blocks[place], weights[place], preferred_element_type=jnp.float32
        )
    key_raw = projected[:, :key_width]
    value_rows = projected[:, key_width:].astype(jnp.bfloat16)
    ctx_index = lax.axis_index("ctx")
    positions = ctx_index * tok_rows + jnp.arange(tok_rows, dtype=jnp.int32)
    cosine_table, sine_table = rotation(positions)
    key_row_block = rotate(key_raw.reshape(tok_rows, KV_HEADS, HEAD_DIM), cosine_table, sine_table)
    key_row_block = key_row_block.astype(jnp.bfloat16).reshape(tok_rows, key_width)
    prev_both = from_behind(jnp.concatenate([key_row_block, value_rows], axis=1), "ctx", 1)
    prev_key, prev_value = prev_both[:, :key_width], prev_both[:, key_width:]
    head_shape = (tok_rows, KV_HEADS, HEAD_DIM)
    query_gradient, nearby_key, nearby_value, distant_key, distant_value = block_backward(
        queries[0],
        out_grad[0],
        key_row_block.reshape(head_shape),
        value_rows.reshape(head_shape),
        prev_key.reshape(head_shape),
        prev_value.reshape(head_shape),
        ctx_index > 0,
    )
    incoming_both = from_behind(
        jnp.concatenate([distant_key, distant_value], axis=1).astype(jnp.bfloat16), "ctx", -1
    )
    incoming_key = incoming_both[:, :KV_HEADS]
    incoming_value = incoming_both[:, KV_HEADS:]
    key_grad = nearby_key + incoming_key.astype(jnp.float32)
    value_grad = nearby_value + incoming_value.astype(jnp.float32)
    key_grad_raw = (
        rotate_back(key_grad, cosine_table, sine_table)
        .astype(jnp.bfloat16)
        .reshape(tok_rows, key_width)
    )
    value_low = value_grad.astype(jnp.bfloat16).reshape(tok_rows, key_width)
    grads_cat = jnp.concatenate([key_grad_raw, value_low], axis=1)

    def block_term(place):
        term = jnp.einsum(
            "td,tk->dk", normed_blocks[place], grads_cat, preferred_element_type=jnp.float32
        )
        return (term * grad_scale).astype(jnp.bfloat16).astype(jnp.float32)

    ahead = [(ring[i], ring[(i + 1) % n_blocks]) for i in range(n_blocks)]
    behind = [(ring[i], ring[(i - 1) % n_blocks]) for i in range(n_blocks)]
    n_ahead = n_blocks // 2
    carried = block_term(n_ahead)
    for step in range(2, n_ahead + 1):
        arrived = lax.ppermute(carried.astype(jnp.bfloat16), ("ctx", "dp"), ahead)
        carried = arrived.astype(jnp.float32) + block_term(n_ahead + 1 - step)
    from_left = lax.ppermute(carried.astype(jnp.bfloat16), ("ctx", "dp"), ahead)
    n_behind = n_blocks - 1 - n_ahead
    carried = block_term(n_blocks - n_behind)
    for step in range(2, n_behind + 1):
        arrived = lax.ppermute(carried.astype(jnp.bfloat16), ("ctx", "dp"), behind)
        carried = arrived.astype(jnp.float32) + block_term(n_blocks - n_behind - 1 + step)
    from_right = lax.ppermute(carried.astype(jnp.bfloat16), ("ctx", "dp"), behind)
    stacked = block_term(0) + from_left.astype(jnp.float32) + from_right.astype(jnp.float32)
    key_weight_grad = stacked[:, :key_width]
    value_weight_grad = stacked[:, key_width:]
    normed_grad = jnp.stack(
        [
            jnp.einsum("tk,rk->tr", grads_cat, piece, preferred_element_type=jnp.float32)
            for piece in weights
        ]
    )
    normed_grad = jnp.swapaxes(jnp.take(normed_grad, offset_of, axis=0), 0, 1)
    normed_grad = normed_grad.reshape(tok_rows, -1)
    scaled = normed_grad * norm_gain
    cubed = inverse * inverse * inverse
    hidden_grad = (
        inverse * scaled - inputs * cubed * jnp.mean(scaled * inputs, axis=-1, keepdims=True)
    ).astype(jnp.bfloat16)
    gain_term = jnp.sum(normed_grad * inputs * inverse, axis=0) * grad_scale
    gain_pieces = lax.all_to_all(
        gain_term.reshape(n_blocks, shard_rows), ("ctx", "dp"), 0, 0, tiled=True
    )
    gain_grad = jnp.sum(gain_pieces, axis=0)
    return (hidden_grad[None], query_gradient[None], key_weight_grad, value_weight_grad, gain_grad)


def solution(mesh):
    return jax.shard_map(
        body,
        mesh=mesh,
        in_specs=(
            P(("groups", "dp"), "ctx", None),
            P(),
            P(("ctx", "dp"), None),
            P(("ctx", "dp"), None),
            P(("groups", "dp"), "ctx", None),
            P(("groups", "dp"), "ctx", None),
        ),
        out_specs=(
            P(("groups", "dp"), "ctx", None),
            P(("groups", "dp"), "ctx", None),
            P(("groups", "ctx", "dp"), None),
            P(("groups", "ctx", "dp"), None),
            P(("groups", "ctx", "dp")),
        ),
        check_vma=False,
    )
```

```python
import jax
import jax.numpy as jnp
from jax import lax
from jax.sharding import PartitionSpec as P

HEADS = 16
KV_HEADS = 8
HEAD_DIM = 128
WINDOW = 256


score_scale = 1.0 / 12.0
grad_scale = 1.0 / 64.0
norm_eps = 1e-06
rope_base = 10000.0
masked_score = -1e30


def from_behind(value, axis, steps):
    count = lax.axis_size(axis)
    initial, last = (max(0, -steps), min(count, count - steps))
    return lax.ppermute(value, axis, [(source, source + steps) for source in range(initial, last)])


def rotation(positions):
    half_dim = HEAD_DIM // 2
    frequency = rope_base ** (-jnp.arange(half_dim, dtype=jnp.float32) / half_dim)
    angles = positions.astype(jnp.float32)[:, None] * frequency[None, :]
    return (jnp.cos(angles)[:, None, :], jnp.sin(angles)[:, None, :])


def rotate(tensor, cosine_table, sine_table):
    half_dim = HEAD_DIM // 2
    front_half = tensor[..., :half_dim]
    back_half = tensor[..., half_dim:]
    return jnp.concatenate(
        [
            front_half * cosine_table - back_half * sine_table,
            back_half * cosine_table + front_half * sine_table,
        ],
        axis=-1,
    )


def rotate_back(tensor, cosine_table, sine_table):
    half_dim = HEAD_DIM // 2
    front_half = tensor[..., :half_dim]
    back_half = tensor[..., half_dim:]
    return jnp.concatenate(
        [
            front_half * cosine_table + back_half * sine_table,
            back_half * cosine_table - front_half * sine_table,
        ],
        axis=-1,
    )


def block_backward(
    query_block, grad_block, nearby_keys, near_values, distant_keys, far_values, has_prev
):
    tok_rows = query_block.shape[0]
    group_size = HEADS // KV_HEADS
    query_head_split = query_block.reshape(tok_rows, KV_HEADS, group_size, HEAD_DIM)
    gradient_heads = grad_block.reshape(tok_rows, KV_HEADS, group_size, HEAD_DIM)
    row_index = jnp.arange(tok_rows)[:, None]
    col_index = jnp.arange(tok_rows)[None, :]
    near_mask = (col_index <= row_index) & (row_index - col_index < WINDOW)
    far_mask = (col_index > row_index + tok_rows - WINDOW) & has_prev

    def pair_products(leftover_heads, key_row_block):
        return jnp.einsum(
            "qbak,wbk->baqw", leftover_heads, key_row_block, preferred_element_type=jnp.float32
        )

    near_scores = jnp.where(
        near_mask, pair_products(query_head_split, nearby_keys) * score_scale, masked_score
    )
    far_scores = jnp.where(
        far_mask, pair_products(query_head_split, distant_keys) * score_scale, masked_score
    )
    row_top = jnp.maximum(jnp.max(near_scores, -1), jnp.max(far_scores, -1))[..., None]
    near_exp = jnp.where(near_mask, jnp.exp(near_scores - row_top), 0.0)
    far_exp = jnp.where(far_mask, jnp.exp(far_scores - row_top), 0.0)
    row_total = (jnp.sum(near_exp, -1) + jnp.sum(far_exp, -1))[..., None]
    near_probs = near_exp / row_total
    far_probs = far_exp / row_total
    near_dprobs = pair_products(gradient_heads, near_values)
    far_dprobs = pair_products(gradient_heads, far_values)
    weighted = (jnp.sum(near_probs * near_dprobs, -1) + jnp.sum(far_probs * far_dprobs, -1))[
        ..., None
    ]
    nearby_score_gradient = (near_probs * (near_dprobs - weighted) * score_scale).astype(
        jnp.bfloat16
    )
    distant_score_gradient = (far_probs * (far_dprobs - weighted) * score_scale).astype(
        jnp.bfloat16
    )
    nearby_reduced = near_probs.astype(jnp.bfloat16)
    distant_reduced = far_probs.astype(jnp.bfloat16)
    query_gradient = jnp.einsum(
        "xqwc,cxi->wxqi", nearby_score_gradient, nearby_keys, preferred_element_type=jnp.float32
    )
    query_gradient = query_gradient + jnp.einsum(
        "xqwc,cxi->wxqi", distant_score_gradient, distant_keys, preferred_element_type=jnp.float32
    )
    nearby_key = jnp.einsum(
        "woia,iwon->awn",
        nearby_score_gradient,
        query_head_split,
        preferred_element_type=jnp.float32,
    )
    distant_key = jnp.einsum(
        "woia,iwon->awn",
        distant_score_gradient,
        query_head_split,
        preferred_element_type=jnp.float32,
    )
    nearby_value = jnp.einsum(
        "woia,iwon->awn", nearby_reduced, gradient_heads, preferred_element_type=jnp.float32
    )
    distant_value = jnp.einsum(
        "woia,iwon->awn", distant_reduced, gradient_heads, preferred_element_type=jnp.float32
    )
    query_out = query_gradient.reshape(tok_rows, HEADS * HEAD_DIM).astype(jnp.bfloat16)
    return (query_out, nearby_key, nearby_value, distant_key, distant_value)


def ring_order(n_ctx, n_dp):
    if n_ctx % 2 == 0:
        half = n_ctx // 2
        chips = [2 * a for a in range(half)] + [2 * a + 1 for a in reversed(range(half))]
    else:
        chips = list(range(n_ctx))
    return [chip * n_dp + core for chip in chips for core in range(n_dp)]


def ring_gather(piece, axes, ring):
    count = len(ring)
    ahead = [(ring[i], ring[(i + 1) % count]) for i in range(count)]
    behind = [(ring[i], ring[(i - 1) % count]) for i in range(count)]
    n_ahead = count // 2
    from_left, from_right = [], []
    moving = piece
    for _ in range(n_ahead):
        moving = lax.ppermute(moving, axes, ahead)
        from_left.append(moving)
    moving = piece
    for _ in range(count - 1 - n_ahead):
        moving = lax.ppermute(moving, axes, behind)
        from_right.append(moving)
    return [piece] + from_right + from_left[::-1]


def body(hidden_in, norm_gain, key_weight, value_weight, queries, out_grad):
    tok_rows = hidden_in.shape[1]
    key_width = key_weight.shape[1]
    inputs = hidden_in[0].astype(jnp.float32)
    inverse = lax.rsqrt(jnp.mean(inputs * inputs, axis=-1, keepdims=True) + norm_eps)
    normed = (inputs * inverse * norm_gain).astype(jnp.bfloat16)
    n_ctx = lax.axis_size("ctx")
    n_dp = lax.axis_size("dp")
    n_blocks = n_ctx * n_dp
    shard_rows = normed.shape[1] // n_blocks
    ring = ring_order(n_ctx, n_dp)
    ring_pos = [0] * n_blocks
    for place, member in enumerate(ring):
        ring_pos[member] = place
    my_place = jnp.array(ring_pos, jnp.int32)[lax.axis_index("ctx") * n_dp + lax.axis_index("dp")]
    offsets = jnp.arange(n_blocks, dtype=jnp.int32)
    source_of = jnp.array(ring, jnp.int32)[(my_place + offsets) % n_blocks]
    offset_of = (jnp.array(ring_pos, jnp.int32) - my_place) % n_blocks
    weights = ring_gather(
        jnp.concatenate([key_weight, value_weight], axis=1), ("ctx", "dp"), ring
    )
    normed_local = jnp.swapaxes(normed.reshape(tok_rows, n_blocks, shard_rows), 0, 1)
    normed_blocks = jnp.take(normed_local, source_of, axis=0)
    projected = jnp.dot(normed_blocks[0], weights[0], preferred_element_type=jnp.float32)
    for place in range(1, n_blocks):
        projected = projected + jnp.dot(
            normed_blocks[place], weights[place], preferred_element_type=jnp.float32
        )
    key_raw = projected[:, :key_width]
    value_rows = projected[:, key_width:].astype(jnp.bfloat16)
    ctx_index = lax.axis_index("ctx")
    positions = ctx_index * tok_rows + jnp.arange(tok_rows, dtype=jnp.int32)
    cosine_table, sine_table = rotation(positions)
    key_row_block = rotate(key_raw.reshape(tok_rows, KV_HEADS, HEAD_DIM), cosine_table, sine_table)
    key_row_block = key_row_block.astype(jnp.bfloat16).reshape(tok_rows, key_width)
    prev_key, prev_value = from_behind((key_row_block, value_rows), "ctx", 1)
    head_shape = (tok_rows, KV_HEADS, HEAD_DIM)
    query_gradient, nearby_key, nearby_value, distant_key, distant_value = block_backward(
        queries[0],
        out_grad[0],
        key_row_block.reshape(head_shape),
        value_rows.reshape(head_shape),
        prev_key.reshape(head_shape),
        prev_value.reshape(head_shape),
        ctx_index > 0,
    )
    incoming_key, incoming_value = from_behind(
        (distant_key.astype(jnp.bfloat16), distant_value.astype(jnp.bfloat16)), "ctx", -1
    )
    key_grad = nearby_key + incoming_key.astype(jnp.float32)
    value_grad = nearby_value + incoming_value.astype(jnp.float32)
    key_grad_raw = (
        rotate_back(key_grad, cosine_table, sine_table)
        .astype(jnp.bfloat16)
        .reshape(tok_rows, key_width)
    )
    value_low = value_grad.astype(jnp.bfloat16).reshape(tok_rows, key_width)
    grads_cat = jnp.concatenate([key_grad_raw, value_low], axis=1)

    def block_term(place):
        term = jnp.einsum(
            "td,tk->dk", normed_blocks[place], grads_cat, preferred_element_type=jnp.float32
        )
        return (term * grad_scale).astype(jnp.bfloat16).astype(jnp.float32)

    ahead = [(ring[i], ring[(i + 1) % n_blocks]) for i in range(n_blocks)]
    behind = [(ring[i], ring[(i - 1) % n_blocks]) for i in range(n_blocks)]
    n_ahead = n_blocks // 2
    carried = block_term(n_ahead)
    for step in range(2, n_ahead + 1):
        arrived = lax.ppermute(carried.astype(jnp.bfloat16), ("ctx", "dp"), ahead)
        carried = arrived.astype(jnp.float32) + block_term(n_ahead + 1 - step)
    from_left = lax.ppermute(carried.astype(jnp.bfloat16), ("ctx", "dp"), ahead)
    n_behind = n_blocks - 1 - n_ahead
    carried = block_term(n_blocks - n_behind)
    for step in range(2, n_behind + 1):
        arrived = lax.ppermute(carried.astype(jnp.bfloat16), ("ctx", "dp"), behind)
        carried = arrived.astype(jnp.float32) + block_term(n_blocks - n_behind - 1 + step)
    from_right = lax.ppermute(carried.astype(jnp.bfloat16), ("ctx", "dp"), behind)
    stacked = block_term(0) + from_left.astype(jnp.float32) + from_right.astype(jnp.float32)
    key_weight_grad = stacked[:, :key_width]
    value_weight_grad = stacked[:, key_width:]
    normed_grad = jnp.stack(
        [
            jnp.einsum("tk,rk->tr", grads_cat, piece, preferred_element_type=jnp.float32)
            for piece in weights
        ],
        axis=1,
    )
    inputs_moved = jnp.take(inputs.reshape(tok_rows, n_blocks, shard_rows), source_of, axis=1)
    gain_moved = jnp.take(norm_gain.reshape(n_blocks, shard_rows), source_of, axis=0)
    scaled = normed_grad * gain_moved
    cubed = inverse[:, :, None] * inverse[:, :, None] * inverse[:, :, None]
    feature_mean = jnp.sum(scaled * inputs_moved, axis=(1, 2), keepdims=True) / normed.shape[1]
    hidden_grad = (
        inverse[:, :, None] * scaled - inputs_moved * cubed * feature_mean
    ).astype(jnp.bfloat16)
    hidden_grad = jnp.take(hidden_grad, offset_of, axis=1).reshape(tok_rows, -1)
    gain_term = jnp.sum(normed_grad * inputs_moved * inverse[:, :, None], axis=0) * grad_scale
    gain_term = jnp.take(gain_term, offset_of, axis=0)
    gain_pieces = lax.all_to_all(gain_term, ("ctx", "dp"), 0, 0, tiled=True)
    gain_grad = jnp.sum(gain_pieces, axis=0)
    return (hidden_grad[None], query_gradient[None], key_weight_grad, value_weight_grad, gain_grad)


def solution(mesh):
    return jax.shard_map(
        body,
        mesh=mesh,
        in_specs=(
            P(("groups", "dp"), "ctx", None),
            P(),
            P(("ctx", "dp"), None),
            P(("ctx", "dp"), None),
            P(("groups", "dp"), "ctx", None),
            P(("groups", "dp"), "ctx", None),
        ),
        out_specs=(
            P(("groups", "dp"), "ctx", None),
            P(("groups", "dp"), "ctx", None),
            P(("groups", "ctx", "dp"), None),
            P(("groups", "ctx", "dp"), None),
            P(("groups", "ctx", "dp")),
        ),
        check_vma=False,
    )
```

```python
import jax
import jax.numpy as jnp
from jax import lax
from jax.sharding import PartitionSpec as P

HEADS = 16
KV_HEADS = 8
HEAD_DIM = 128
WINDOW = 256


score_scale = 1.0 / 12.0
grad_scale = 1.0 / 64.0
norm_eps = 1e-06
rope_base = 10000.0
masked_score = -1e30


def from_behind(value, axis, steps):
    count = lax.axis_size(axis)
    initial, last = (max(0, -steps), min(count, count - steps))
    return lax.ppermute(value, axis, [(source, source + steps) for source in range(initial, last)])


def rotation(positions):
    half_dim = HEAD_DIM // 2
    frequency = rope_base ** (-jnp.arange(half_dim, dtype=jnp.float32) / half_dim)
    angles = positions.astype(jnp.float32)[:, None] * frequency[None, :]
    return (jnp.cos(angles)[:, None, :], jnp.sin(angles)[:, None, :])


def rotate(tensor, cosine_table, sine_table):
    half_dim = HEAD_DIM // 2
    front_half = tensor[..., :half_dim]
    back_half = tensor[..., half_dim:]
    return jnp.concatenate(
        [
            front_half * cosine_table - back_half * sine_table,
            back_half * cosine_table + front_half * sine_table,
        ],
        axis=-1,
    )


def rotate_back(tensor, cosine_table, sine_table):
    half_dim = HEAD_DIM // 2
    front_half = tensor[..., :half_dim]
    back_half = tensor[..., half_dim:]
    return jnp.concatenate(
        [
            front_half * cosine_table + back_half * sine_table,
            back_half * cosine_table - front_half * sine_table,
        ],
        axis=-1,
    )


def block_backward(
    query_block, grad_block, nearby_keys, near_values, distant_keys, far_values, has_prev
):
    tok_rows = query_block.shape[0]
    group_size = HEADS // KV_HEADS
    query_head_split = query_block.reshape(tok_rows, KV_HEADS, group_size, HEAD_DIM)
    gradient_heads = grad_block.reshape(tok_rows, KV_HEADS, group_size, HEAD_DIM)
    row_index = jnp.arange(tok_rows)[:, None]
    col_index = jnp.arange(tok_rows)[None, :]
    near_mask = (col_index <= row_index) & (row_index - col_index < WINDOW)
    far_mask = (col_index > row_index + tok_rows - WINDOW) & has_prev

    def pair_products(leftover_heads, key_row_block):
        return jnp.einsum(
            "qbak,wbk->baqw", leftover_heads, key_row_block, preferred_element_type=jnp.float32
        )

    near_scores = jnp.where(
        near_mask, pair_products(query_head_split, nearby_keys) * score_scale, masked_score
    )
    far_scores = jnp.where(
        far_mask, pair_products(query_head_split, distant_keys) * score_scale, masked_score
    )
    row_top = jnp.maximum(jnp.max(near_scores, -1), jnp.max(far_scores, -1))[..., None]
    near_exp = jnp.where(near_mask, jnp.exp(near_scores - row_top), 0.0)
    far_exp = jnp.where(far_mask, jnp.exp(far_scores - row_top), 0.0)
    row_total = (jnp.sum(near_exp, -1) + jnp.sum(far_exp, -1))[..., None]
    near_probs = near_exp / row_total
    far_probs = far_exp / row_total
    near_dprobs = pair_products(gradient_heads, near_values)
    far_dprobs = pair_products(gradient_heads, far_values)
    weighted = (jnp.sum(near_probs * near_dprobs, -1) + jnp.sum(far_probs * far_dprobs, -1))[
        ..., None
    ]
    nearby_score_gradient = (near_probs * (near_dprobs - weighted) * score_scale).astype(
        jnp.bfloat16
    )
    distant_score_gradient = (far_probs * (far_dprobs - weighted) * score_scale).astype(
        jnp.bfloat16
    )
    nearby_reduced = near_probs.astype(jnp.bfloat16)
    distant_reduced = far_probs.astype(jnp.bfloat16)
    query_gradient = jnp.einsum(
        "xqwc,cxi->wxqi", nearby_score_gradient, nearby_keys, preferred_element_type=jnp.float32
    )
    query_gradient = query_gradient + jnp.einsum(
        "xqwc,cxi->wxqi", distant_score_gradient, distant_keys, preferred_element_type=jnp.float32
    )
    nearby_key = jnp.einsum(
        "woia,iwon->awn",
        nearby_score_gradient,
        query_head_split,
        preferred_element_type=jnp.float32,
    )
    distant_key = jnp.einsum(
        "woia,iwon->awn",
        distant_score_gradient,
        query_head_split,
        preferred_element_type=jnp.float32,
    )
    nearby_value = jnp.einsum(
        "woia,iwon->awn", nearby_reduced, gradient_heads, preferred_element_type=jnp.float32
    )
    distant_value = jnp.einsum(
        "woia,iwon->awn", distant_reduced, gradient_heads, preferred_element_type=jnp.float32
    )
    query_out = query_gradient.reshape(tok_rows, HEADS * HEAD_DIM).astype(jnp.bfloat16)
    return (query_out, nearby_key, nearby_value, distant_key, distant_value)


def ring_order(n_ctx, n_dp):
    if n_ctx % 2 == 0:
        half = n_ctx // 2
        chips = [2 * a for a in range(half)] + [2 * a + 1 for a in reversed(range(half))]
    else:
        chips = list(range(n_ctx))
    return [chip * n_dp + core for chip in chips for core in range(n_dp)]


def ring_gather(piece, axes, ring):
    count = len(ring)
    ahead = [(ring[i], ring[(i + 1) % count]) for i in range(count)]
    behind = [(ring[i], ring[(i - 1) % count]) for i in range(count)]
    n_each = (count - 1) // 2
    from_left, from_right = [], []
    moving = piece
    for _ in range(n_each):
        moving = lax.ppermute(moving, axes, ahead)
        from_left.append(moving)
    moving = piece
    for _ in range(n_each):
        moving = lax.ppermute(moving, axes, behind)
        from_right.append(moving)
    opposite = []
    if count % 2 == 0:
        half = piece.shape[-1] // 2
        left_source = from_left[-1] if from_left else piece
        right_source = from_right[-1] if from_right else piece
        opposite = [
            jnp.concatenate(
                [
                    lax.ppermute(left_source[..., :half], axes, ahead),
                    lax.ppermute(right_source[..., half:], axes, behind),
                ],
                axis=-1,
            )
        ]
    return [piece] + from_right + opposite + from_left[::-1]


def body(hidden_in, norm_gain, key_weight, value_weight, queries, out_grad):
    tok_rows = hidden_in.shape[1]
    key_width = key_weight.shape[1]
    inputs = hidden_in[0].astype(jnp.float32)
    inverse = lax.rsqrt(jnp.mean(inputs * inputs, axis=-1, keepdims=True) + norm_eps)
    normed = (inputs * inverse * norm_gain).astype(jnp.bfloat16)
    n_ctx = lax.axis_size("ctx")
    n_dp = lax.axis_size("dp")
    n_blocks = n_ctx * n_dp
    shard_rows = normed.shape[1] // n_blocks
    ring = ring_order(n_ctx, n_dp)
    ring_pos = [0] * n_blocks
    for place, member in enumerate(ring):
        ring_pos[member] = place
    my_place = jnp.array(ring_pos, jnp.int32)[lax.axis_index("ctx") * n_dp + lax.axis_index("dp")]
    offsets = jnp.arange(n_blocks, dtype=jnp.int32)
    source_of = jnp.array(ring, jnp.int32)[(my_place + offsets) % n_blocks]
    offset_of = (jnp.array(ring_pos, jnp.int32) - my_place) % n_blocks
    weights = ring_gather(
        jnp.concatenate([key_weight, value_weight], axis=1), ("ctx", "dp"), ring
    )
    normed_local = jnp.swapaxes(normed.reshape(tok_rows, n_blocks, shard_rows), 0, 1)
    normed_blocks = jnp.take(normed_local, source_of, axis=0)
    projected = jnp.dot(normed_blocks[0], weights[0], preferred_element_type=jnp.float32)
    for place in range(1, n_blocks):
        projected = projected + jnp.dot(
            normed_blocks[place], weights[place], preferred_element_type=jnp.float32
        )
    key_raw = projected[:, :key_width]
    value_rows = projected[:, key_width:].astype(jnp.bfloat16)
    ctx_index = lax.axis_index("ctx")
    positions = ctx_index * tok_rows + jnp.arange(tok_rows, dtype=jnp.int32)
    cosine_table, sine_table = rotation(positions)
    key_row_block = rotate(key_raw.reshape(tok_rows, KV_HEADS, HEAD_DIM), cosine_table, sine_table)
    key_row_block = key_row_block.astype(jnp.bfloat16).reshape(tok_rows, key_width)
    prev_key, prev_value = from_behind((key_row_block, value_rows), "ctx", 1)
    head_shape = (tok_rows, KV_HEADS, HEAD_DIM)
    query_gradient, nearby_key, nearby_value, distant_key, distant_value = block_backward(
        queries[0],
        out_grad[0],
        key_row_block.reshape(head_shape),
        value_rows.reshape(head_shape),
        prev_key.reshape(head_shape),
        prev_value.reshape(head_shape),
        ctx_index > 0,
    )
    incoming_key, incoming_value = from_behind(
        (distant_key.astype(jnp.bfloat16), distant_value.astype(jnp.bfloat16)), "ctx", -1
    )
    key_grad = nearby_key + incoming_key.astype(jnp.float32)
    value_grad = nearby_value + incoming_value.astype(jnp.float32)
    key_grad_raw = (
        rotate_back(key_grad, cosine_table, sine_table)
        .astype(jnp.bfloat16)
        .reshape(tok_rows, key_width)
    )
    value_low = value_grad.astype(jnp.bfloat16).reshape(tok_rows, key_width)
    grads_cat = jnp.concatenate([key_grad_raw, value_low], axis=1)

    def block_term(place):
        term = jnp.einsum(
            "td,tk->dk", normed_blocks[place], grads_cat, preferred_element_type=jnp.float32
        )
        return (term * grad_scale).astype(jnp.bfloat16).astype(jnp.float32)

    ahead = [(ring[i], ring[(i + 1) % n_blocks]) for i in range(n_blocks)]
    behind = [(ring[i], ring[(i - 1) % n_blocks]) for i in range(n_blocks)]
    n_ahead = n_blocks // 2
    carried = block_term(n_ahead)
    for step in range(2, n_ahead + 1):
        arrived = lax.ppermute(carried.astype(jnp.bfloat16), ("ctx", "dp"), ahead)
        carried = arrived.astype(jnp.float32) + block_term(n_ahead + 1 - step)
    from_left = lax.ppermute(carried.astype(jnp.bfloat16), ("ctx", "dp"), ahead)
    n_behind = n_blocks - 1 - n_ahead
    carried = block_term(n_blocks - n_behind)
    for step in range(2, n_behind + 1):
        arrived = lax.ppermute(carried.astype(jnp.bfloat16), ("ctx", "dp"), behind)
        carried = arrived.astype(jnp.float32) + block_term(n_blocks - n_behind - 1 + step)
    from_right = lax.ppermute(carried.astype(jnp.bfloat16), ("ctx", "dp"), behind)
    stacked = block_term(0) + from_left.astype(jnp.float32) + from_right.astype(jnp.float32)
    key_weight_grad = stacked[:, :key_width]
    value_weight_grad = stacked[:, key_width:]
    normed_grad = jnp.stack(
        [
            jnp.einsum("tk,rk->tr", grads_cat, piece, preferred_element_type=jnp.float32)
            for piece in weights
        ]
    )
    normed_grad = jnp.swapaxes(jnp.take(normed_grad, offset_of, axis=0), 0, 1)
    normed_grad = normed_grad.reshape(tok_rows, -1)
    scaled = normed_grad * norm_gain
    cubed = inverse * inverse * inverse
    hidden_grad = (
        inverse * scaled - inputs * cubed * jnp.mean(scaled * inputs, axis=-1, keepdims=True)
    ).astype(jnp.bfloat16)
    gain_term = jnp.sum(normed_grad * inputs * inverse, axis=0) * grad_scale
    gain_pieces = lax.all_to_all(
        gain_term.reshape(n_blocks, shard_rows), ("ctx", "dp"), 0, 0, tiled=True
    )
    gain_grad = jnp.sum(gain_pieces, axis=0)
    return (hidden_grad[None], query_gradient[None], key_weight_grad, value_weight_grad, gain_grad)


def solution(mesh):
    return jax.shard_map(
        body,
        mesh=mesh,
        in_specs=(
            P(("groups", "dp"), "ctx", None),
            P(),
            P(("ctx", "dp"), None),
            P(("ctx", "dp"), None),
            P(("groups", "dp"), "ctx", None),
            P(("groups", "dp"), "ctx", None),
        ),
        out_specs=(
            P(("groups", "dp"), "ctx", None),
            P(("groups", "dp"), "ctx", None),
            P(("groups", "ctx", "dp"), None),
            P(("groups", "ctx", "dp"), None),
            P(("groups", "ctx", "dp")),
        ),
        check_vma=False,
    )
```

```python
import jax
import jax.numpy as jnp
from jax import lax
from jax.sharding import PartitionSpec as P

HEADS = 16
KV_HEADS = 8
HEAD_DIM = 128
WINDOW = 256


score_scale = 1.0 / 12.0
grad_scale = 1.0 / 64.0
norm_eps = 1e-06
rope_base = 10000.0
masked_score = -1e30


def from_behind(value, axis, steps):
    count = lax.axis_size(axis)
    initial, last = (max(0, -steps), min(count, count - steps))
    return lax.ppermute(value, axis, [(source, source + steps) for source in range(initial, last)])


def rotation(positions):
    half_dim = HEAD_DIM // 2
    frequency = rope_base ** (-jnp.arange(half_dim, dtype=jnp.float32) / half_dim)
    angles = positions.astype(jnp.float32)[:, None] * frequency[None, :]
    return (jnp.cos(angles)[:, None, :], jnp.sin(angles)[:, None, :])


def rotate(tensor, cosine_table, sine_table):
    half_dim = HEAD_DIM // 2
    front_half = tensor[..., :half_dim]
    back_half = tensor[..., half_dim:]
    return jnp.concatenate(
        [
            front_half * cosine_table - back_half * sine_table,
            back_half * cosine_table + front_half * sine_table,
        ],
        axis=-1,
    )


def rotate_back(tensor, cosine_table, sine_table):
    half_dim = HEAD_DIM // 2
    front_half = tensor[..., :half_dim]
    back_half = tensor[..., half_dim:]
    return jnp.concatenate(
        [
            front_half * cosine_table + back_half * sine_table,
            back_half * cosine_table - front_half * sine_table,
        ],
        axis=-1,
    )


def block_backward(
    query_block, grad_block, nearby_keys, near_values, distant_keys, far_values, has_prev
):
    tok_rows = query_block.shape[0]
    group_size = HEADS // KV_HEADS
    query_head_split = query_block.reshape(tok_rows, KV_HEADS, group_size, HEAD_DIM)
    gradient_heads = grad_block.reshape(tok_rows, KV_HEADS, group_size, HEAD_DIM)
    row_index = jnp.arange(tok_rows)[:, None]
    col_index = jnp.arange(tok_rows)[None, :]
    near_mask = (col_index <= row_index) & (row_index - col_index < WINDOW)
    far_mask = (col_index > row_index + tok_rows - WINDOW) & has_prev

    def pair_products(leftover_heads, key_row_block):
        return jnp.einsum(
            "qbak,wbk->baqw", leftover_heads, key_row_block, preferred_element_type=jnp.float32
        )

    near_scores = jnp.where(
        near_mask, pair_products(query_head_split, nearby_keys) * score_scale, masked_score
    )
    far_scores = jnp.where(
        far_mask, pair_products(query_head_split, distant_keys) * score_scale, masked_score
    )
    row_top = jnp.maximum(jnp.max(near_scores, -1), jnp.max(far_scores, -1))[..., None]
    near_exp = jnp.where(near_mask, jnp.exp(near_scores - row_top), 0.0)
    far_exp = jnp.where(far_mask, jnp.exp(far_scores - row_top), 0.0)
    row_total = (jnp.sum(near_exp, -1) + jnp.sum(far_exp, -1))[..., None]
    near_probs = near_exp / row_total
    far_probs = far_exp / row_total
    near_dprobs = pair_products(gradient_heads, near_values)
    far_dprobs = pair_products(gradient_heads, far_values)
    weighted = (jnp.sum(near_probs * near_dprobs, -1) + jnp.sum(far_probs * far_dprobs, -1))[
        ..., None
    ]
    nearby_score_gradient = (near_probs * (near_dprobs - weighted) * score_scale).astype(
        jnp.bfloat16
    )
    distant_score_gradient = (far_probs * (far_dprobs - weighted) * score_scale).astype(
        jnp.bfloat16
    )
    nearby_reduced = near_probs.astype(jnp.bfloat16)
    distant_reduced = far_probs.astype(jnp.bfloat16)
    query_gradient = jnp.einsum(
        "xqwc,cxi->wxqi", nearby_score_gradient, nearby_keys, preferred_element_type=jnp.float32
    )
    query_gradient = query_gradient + jnp.einsum(
        "xqwc,cxi->wxqi", distant_score_gradient, distant_keys, preferred_element_type=jnp.float32
    )
    nearby_key = jnp.einsum(
        "woia,iwon->awn",
        nearby_score_gradient,
        query_head_split,
        preferred_element_type=jnp.float32,
    )
    distant_key = jnp.einsum(
        "woia,iwon->awn",
        distant_score_gradient,
        query_head_split,
        preferred_element_type=jnp.float32,
    )
    nearby_value = jnp.einsum(
        "woia,iwon->awn", nearby_reduced, gradient_heads, preferred_element_type=jnp.float32
    )
    distant_value = jnp.einsum(
        "woia,iwon->awn", distant_reduced, gradient_heads, preferred_element_type=jnp.float32
    )
    query_out = query_gradient.reshape(tok_rows, HEADS * HEAD_DIM).astype(jnp.bfloat16)
    return (query_out, nearby_key, nearby_value, distant_key, distant_value)


def ring_order(n_ctx, n_dp):
    if n_ctx % 2 == 0:
        half = n_ctx // 2
        chips = [2 * a for a in range(half)] + [2 * a + 1 for a in reversed(range(half))]
    else:
        chips = list(range(n_ctx))
    return [chip * n_dp + core for chip in chips for core in range(n_dp)]


def ring_gather(piece, axes, ring):
    count = len(ring)
    ahead = [(ring[i], ring[(i + 1) % count]) for i in range(count)]
    behind = [(ring[i], ring[(i - 1) % count]) for i in range(count)]
    n_each = (count - 1) // 2
    from_left, from_right = [], []
    moving = piece
    for _ in range(n_each):
        moving = lax.ppermute(moving, axes, ahead)
        from_left.append(moving)
    moving = piece
    for _ in range(n_each):
        moving = lax.ppermute(moving, axes, behind)
        from_right.append(moving)
    opposite = []
    if count % 2 == 0:
        half = piece.shape[-1] // 2
        left_source = from_left[-1] if from_left else piece
        right_source = from_right[-1] if from_right else piece
        opposite = [
            jnp.concatenate(
                [
                    lax.ppermute(left_source[..., :half], axes, ahead),
                    lax.ppermute(right_source[..., half:], axes, behind),
                ],
                axis=-1,
            )
        ]
    return [piece] + from_right + opposite + from_left[::-1]


def body(hidden_in, norm_gain, key_weight, value_weight, queries, out_grad):
    tok_rows = hidden_in.shape[1]
    key_width = key_weight.shape[1]
    inputs = hidden_in[0].astype(jnp.float32)
    inverse = lax.rsqrt(jnp.mean(inputs * inputs, axis=-1, keepdims=True) + norm_eps)
    normed = (inputs * inverse * norm_gain).astype(jnp.bfloat16)
    n_ctx = lax.axis_size("ctx")
    n_dp = lax.axis_size("dp")
    n_blocks = n_ctx * n_dp
    shard_rows = normed.shape[1] // n_blocks
    ring = ring_order(n_ctx, n_dp)
    ring_pos = [0] * n_blocks
    for place, member in enumerate(ring):
        ring_pos[member] = place
    my_place = jnp.array(ring_pos, jnp.int32)[lax.axis_index("ctx") * n_dp + lax.axis_index("dp")]
    offsets = jnp.arange(n_blocks, dtype=jnp.int32)
    source_of = jnp.array(ring, jnp.int32)[(my_place + offsets) % n_blocks]
    offset_of = (jnp.array(ring_pos, jnp.int32) - my_place) % n_blocks
    weights = ring_gather(
        jnp.concatenate([key_weight, value_weight], axis=1), ("ctx", "dp"), ring
    )
    normed_local = jnp.swapaxes(normed.reshape(tok_rows, n_blocks, shard_rows), 0, 1)
    normed_blocks = jnp.take(normed_local, source_of, axis=0)
    projected = jnp.dot(normed_blocks[0], weights[0], preferred_element_type=jnp.float32)
    for place in range(1, n_blocks):
        projected = projected + jnp.dot(
            normed_blocks[place], weights[place], preferred_element_type=jnp.float32
        )
    key_raw = projected[:, :key_width]
    value_rows = projected[:, key_width:].astype(jnp.bfloat16)
    ctx_index = lax.axis_index("ctx")
    positions = ctx_index * tok_rows + jnp.arange(tok_rows, dtype=jnp.int32)
    cosine_table, sine_table = rotation(positions)
    key_row_block = rotate(key_raw.reshape(tok_rows, KV_HEADS, HEAD_DIM), cosine_table, sine_table)
    key_row_block = key_row_block.astype(jnp.bfloat16).reshape(tok_rows, key_width)
    prev_key, prev_value = from_behind((key_row_block, value_rows), "ctx", 1)
    head_shape = (tok_rows, KV_HEADS, HEAD_DIM)
    query_gradient, nearby_key, nearby_value, distant_key, distant_value = block_backward(
        queries[0],
        out_grad[0],
        key_row_block.reshape(head_shape),
        value_rows.reshape(head_shape),
        prev_key.reshape(head_shape),
        prev_value.reshape(head_shape),
        ctx_index > 0,
    )
    incoming_key, incoming_value = from_behind(
        (distant_key.astype(jnp.bfloat16), distant_value.astype(jnp.bfloat16)), "ctx", -1
    )
    key_grad = nearby_key + incoming_key.astype(jnp.float32)
    value_grad = nearby_value + incoming_value.astype(jnp.float32)
    key_grad_raw = (
        rotate_back(key_grad, cosine_table, sine_table)
        .astype(jnp.bfloat16)
        .reshape(tok_rows, key_width)
    )
    value_low = value_grad.astype(jnp.bfloat16).reshape(tok_rows, key_width)
    grads_cat = jnp.concatenate([key_grad_raw, value_low], axis=1)

    def block_term(place):
        term = jnp.einsum(
            "td,tk->dk", normed_blocks[place], grads_cat, preferred_element_type=jnp.float32
        )
        return (term * grad_scale).astype(jnp.bfloat16).astype(jnp.float32)

    ahead = [(ring[i], ring[(i + 1) % n_blocks]) for i in range(n_blocks)]
    behind = [(ring[i], ring[(i - 1) % n_blocks]) for i in range(n_blocks)]
    n_each = (n_blocks - 1) // 2
    half_width = grads_cat.shape[1] // 2

    def reduce_chain(pairs, offsets, opening):
        carried = None
        if opening is not None:
            arrived = lax.ppermute(opening.astype(jnp.bfloat16), ("ctx", "dp"), pairs)
            carried = arrived.astype(jnp.float32)
        for place in offsets:
            if carried is None:
                carried = block_term(place)
            elif carried.shape[1] < grads_cat.shape[1]:
                padding = jnp.zeros_like(carried)
                if opening_left[pairs is ahead]:
                    carried = jnp.concatenate([carried, padding], axis=1)
                else:
                    carried = jnp.concatenate([padding, carried], axis=1)
                carried = carried + block_term(place)
            else:
                carried = carried + block_term(place)
            carried = lax.ppermute(carried.astype(jnp.bfloat16), ("ctx", "dp"), pairs).astype(
                jnp.float32
            ) if place != offsets[-1] else carried
        return lax.ppermute(carried.astype(jnp.bfloat16), ("ctx", "dp"), pairs)

    opening_left = {True: True, False: False}
    if n_blocks % 2 == 0:
        opposite = block_term(n_blocks // 2)
        open_ahead, open_behind = opposite[:, :half_width], opposite[:, half_width:]
    else:
        open_ahead, open_behind = None, None
    from_left = reduce_chain(ahead, list(range(n_each, 0, -1)), open_ahead)
    from_right = reduce_chain(behind, list(range(n_blocks - n_each, n_blocks)), open_behind)
    stacked = block_term(0) + from_left.astype(jnp.float32) + from_right.astype(jnp.float32)
    key_weight_grad = stacked[:, :key_width]
    value_weight_grad = stacked[:, key_width:]
    normed_grad = jnp.stack(
        [
            jnp.einsum("tk,rk->tr", grads_cat, piece, preferred_element_type=jnp.float32)
            for piece in weights
        ]
    )
    normed_grad = jnp.swapaxes(jnp.take(normed_grad, offset_of, axis=0), 0, 1)
    normed_grad = normed_grad.reshape(tok_rows, -1)
    scaled = normed_grad * norm_gain
    cubed = inverse * inverse * inverse
    hidden_grad = (
        inverse * scaled - inputs * cubed * jnp.mean(scaled * inputs, axis=-1, keepdims=True)
    ).astype(jnp.bfloat16)
    gain_term = jnp.sum(normed_grad * inputs * inverse, axis=0) * grad_scale
    gain_pieces = lax.all_to_all(
        gain_term.reshape(n_blocks, shard_rows), ("ctx", "dp"), 0, 0, tiled=True
    )
    gain_grad = jnp.sum(gain_pieces, axis=0)
    return (hidden_grad[None], query_gradient[None], key_weight_grad, value_weight_grad, gain_grad)


def solution(mesh):
    return jax.shard_map(
        body,
        mesh=mesh,
        in_specs=(
            P(("groups", "dp"), "ctx", None),
            P(),
            P(("ctx", "dp"), None),
            P(("ctx", "dp"), None),
            P(("groups", "dp"), "ctx", None),
            P(("groups", "dp"), "ctx", None),
        ),
        out_specs=(
            P(("groups", "dp"), "ctx", None),
            P(("groups", "dp"), "ctx", None),
            P(("groups", "ctx", "dp"), None),
            P(("groups", "ctx", "dp"), None),
            P(("groups", "ctx", "dp")),
        ),
        check_vma=False,
    )
```

```python
import jax
import jax.numpy as jnp
from jax import lax
from jax.sharding import PartitionSpec as P

HEADS = 16
KV_HEADS = 8
HEAD_DIM = 128
WINDOW = 256


score_scale = 1.0 / 12.0
grad_scale = 1.0 / 64.0
norm_eps = 1e-06
rope_base = 10000.0
masked_score = -1e30


def from_behind(value, axis, steps):
    count = lax.axis_size(axis)
    initial, last = (max(0, -steps), min(count, count - steps))
    return lax.ppermute(value, axis, [(source, source + steps) for source in range(initial, last)])


def rotation(positions):
    half_dim = HEAD_DIM // 2
    frequency = rope_base ** (-jnp.arange(half_dim, dtype=jnp.float32) / half_dim)
    angles = positions.astype(jnp.float32)[:, None] * frequency[None, :]
    return (jnp.cos(angles)[:, None, :], jnp.sin(angles)[:, None, :])


def rotate(tensor, cosine_table, sine_table):
    half_dim = HEAD_DIM // 2
    front_half = tensor[..., :half_dim]
    back_half = tensor[..., half_dim:]
    return jnp.concatenate(
        [
            front_half * cosine_table - back_half * sine_table,
            back_half * cosine_table + front_half * sine_table,
        ],
        axis=-1,
    )


def rotate_back(tensor, cosine_table, sine_table):
    half_dim = HEAD_DIM // 2
    front_half = tensor[..., :half_dim]
    back_half = tensor[..., half_dim:]
    return jnp.concatenate(
        [
            front_half * cosine_table + back_half * sine_table,
            back_half * cosine_table - front_half * sine_table,
        ],
        axis=-1,
    )


def block_backward(
    query_block, grad_block, nearby_keys, near_values, distant_keys, far_values, has_prev
):
    tok_rows = query_block.shape[0]
    group_size = HEADS // KV_HEADS
    query_head_split = query_block.reshape(tok_rows, KV_HEADS, group_size, HEAD_DIM)
    gradient_heads = grad_block.reshape(tok_rows, KV_HEADS, group_size, HEAD_DIM)
    row_index = jnp.arange(tok_rows)[:, None]
    col_index = jnp.arange(tok_rows)[None, :]
    near_mask = (col_index <= row_index) & (row_index - col_index < WINDOW)
    far_mask = (col_index > row_index + tok_rows - WINDOW) & has_prev

    def pair_products(leftover_heads, key_row_block):
        return jnp.einsum(
            "qbak,wbk->baqw", leftover_heads, key_row_block, preferred_element_type=jnp.float32
        )

    near_scores = jnp.where(
        near_mask, pair_products(query_head_split, nearby_keys) * score_scale, masked_score
    )
    far_scores = jnp.where(
        far_mask, pair_products(query_head_split, distant_keys) * score_scale, masked_score
    )
    row_top = jnp.maximum(jnp.max(near_scores, -1), jnp.max(far_scores, -1))[..., None]
    near_exp = jnp.where(near_mask, jnp.exp(near_scores - row_top), 0.0)
    far_exp = jnp.where(far_mask, jnp.exp(far_scores - row_top), 0.0)
    row_total = (jnp.sum(near_exp, -1) + jnp.sum(far_exp, -1))[..., None]
    near_probs = near_exp / row_total
    far_probs = far_exp / row_total
    near_dprobs = pair_products(gradient_heads, near_values)
    far_dprobs = pair_products(gradient_heads, far_values)
    weighted = (jnp.sum(near_probs * near_dprobs, -1) + jnp.sum(far_probs * far_dprobs, -1))[
        ..., None
    ]
    nearby_score_gradient = (near_probs * (near_dprobs - weighted) * score_scale).astype(
        jnp.bfloat16
    )
    distant_score_gradient = (far_probs * (far_dprobs - weighted) * score_scale).astype(
        jnp.bfloat16
    )
    nearby_reduced = near_probs.astype(jnp.bfloat16)
    distant_reduced = far_probs.astype(jnp.bfloat16)
    query_gradient = jnp.einsum(
        "xqwc,cxi->wxqi", nearby_score_gradient, nearby_keys, preferred_element_type=jnp.float32
    )
    query_gradient = query_gradient + jnp.einsum(
        "xqwc,cxi->wxqi", distant_score_gradient, distant_keys, preferred_element_type=jnp.float32
    )
    nearby_key = jnp.einsum(
        "woia,iwon->awn",
        nearby_score_gradient,
        query_head_split,
        preferred_element_type=jnp.float32,
    )
    distant_key = jnp.einsum(
        "woia,iwon->awn",
        distant_score_gradient,
        query_head_split,
        preferred_element_type=jnp.float32,
    )
    nearby_value = jnp.einsum(
        "woia,iwon->awn", nearby_reduced, gradient_heads, preferred_element_type=jnp.float32
    )
    distant_value = jnp.einsum(
        "woia,iwon->awn", distant_reduced, gradient_heads, preferred_element_type=jnp.float32
    )
    query_out = query_gradient.reshape(tok_rows, HEADS * HEAD_DIM).astype(jnp.bfloat16)
    return (query_out, nearby_key, nearby_value, distant_key, distant_value)


def ring_order(n_ctx, n_dp):
    if n_ctx % 2 == 0:
        half = n_ctx // 2
        chips = [2 * a for a in range(half)] + [2 * a + 1 for a in reversed(range(half))]
    else:
        chips = list(range(n_ctx))
    return [chip * n_dp + core for chip in chips for core in range(n_dp)]


def ring_gather(piece, axes, ring):
    count = len(ring)
    ahead = [(ring[i], ring[(i + 1) % count]) for i in range(count)]
    behind = [(ring[i], ring[(i - 1) % count]) for i in range(count)]
    n_each = (count - 1) // 2
    from_left, from_right = [], []
    moving = piece
    for _ in range(n_each):
        moving = lax.ppermute(moving, axes, ahead)
        from_left.append(moving)
    moving = piece
    for _ in range(n_each):
        moving = lax.ppermute(moving, axes, behind)
        from_right.append(moving)
    opposite = []
    if count % 2 == 0:
        half = piece.shape[-1] // 2
        left_source = from_left[-1] if from_left else piece
        right_source = from_right[-1] if from_right else piece
        opposite = [
            jnp.concatenate(
                [
                    lax.ppermute(left_source[..., :half], axes, ahead),
                    lax.ppermute(right_source[..., half:], axes, behind),
                ],
                axis=-1,
            )
        ]
    return [piece] + from_right + opposite + from_left[::-1]


def body(hidden_in, norm_gain, key_weight, value_weight, queries, out_grad):
    tok_rows = hidden_in.shape[1]
    key_width = key_weight.shape[1]
    inputs = hidden_in[0].astype(jnp.float32)
    inverse = lax.rsqrt(jnp.mean(inputs * inputs, axis=-1, keepdims=True) + norm_eps)
    normed = (inputs * inverse * norm_gain).astype(jnp.bfloat16)
    n_ctx = lax.axis_size("ctx")
    n_dp = lax.axis_size("dp")
    n_blocks = n_ctx * n_dp
    shard_rows = normed.shape[1] // n_blocks
    ring = ring_order(n_ctx, n_dp)
    ring_pos = [0] * n_blocks
    for place, member in enumerate(ring):
        ring_pos[member] = place
    my_place = jnp.array(ring_pos, jnp.int32)[lax.axis_index("ctx") * n_dp + lax.axis_index("dp")]
    offsets = jnp.arange(n_blocks, dtype=jnp.int32)
    source_of = jnp.array(ring, jnp.int32)[(my_place + offsets) % n_blocks]
    offset_of = (jnp.array(ring_pos, jnp.int32) - my_place) % n_blocks
    weights = ring_gather(
        jnp.concatenate([key_weight, value_weight], axis=1), ("ctx", "dp"), ring
    )
    normed_local = jnp.swapaxes(normed.reshape(tok_rows, n_blocks, shard_rows), 0, 1)
    normed_blocks = jnp.take(normed_local, source_of, axis=0)
    projected = jnp.dot(normed_blocks[0], weights[0], preferred_element_type=jnp.float32)
    for place in range(1, n_blocks):
        projected = projected + jnp.dot(
            normed_blocks[place], weights[place], preferred_element_type=jnp.float32
        )
    key_raw = projected[:, :key_width]
    value_rows = projected[:, key_width:].astype(jnp.bfloat16)
    ctx_index = lax.axis_index("ctx")
    positions = ctx_index * tok_rows + jnp.arange(tok_rows, dtype=jnp.int32)
    cosine_table, sine_table = rotation(positions)
    key_row_block = rotate(key_raw.reshape(tok_rows, KV_HEADS, HEAD_DIM), cosine_table, sine_table)
    key_row_block = key_row_block.astype(jnp.bfloat16).reshape(tok_rows, key_width)
    prev_key, prev_value = from_behind((key_row_block, value_rows), "ctx", 1)
    head_shape = (tok_rows, KV_HEADS, HEAD_DIM)
    query_gradient, nearby_key, nearby_value, distant_key, distant_value = block_backward(
        queries[0],
        out_grad[0],
        key_row_block.reshape(head_shape),
        value_rows.reshape(head_shape),
        prev_key.reshape(head_shape),
        prev_value.reshape(head_shape),
        ctx_index > 0,
    )
    incoming_key, incoming_value = from_behind(
        (distant_key.astype(jnp.bfloat16), distant_value.astype(jnp.bfloat16)), "ctx", -1
    )
    key_grad = nearby_key + incoming_key.astype(jnp.float32)
    value_grad = nearby_value + incoming_value.astype(jnp.float32)
    key_grad_raw = (
        rotate_back(key_grad, cosine_table, sine_table)
        .astype(jnp.bfloat16)
        .reshape(tok_rows, key_width)
    )
    value_low = value_grad.astype(jnp.bfloat16).reshape(tok_rows, key_width)
    grads_cat = jnp.concatenate([key_grad_raw, value_low], axis=1)

    def block_term(place):
        term = jnp.einsum(
            "td,tk->dk", normed_blocks[place], grads_cat, preferred_element_type=jnp.float32
        )
        return (term * grad_scale).astype(jnp.bfloat16).astype(jnp.float32)

    ahead = [(ring[i], ring[(i + 1) % n_blocks]) for i in range(n_blocks)]
    behind = [(ring[i], ring[(i - 1) % n_blocks]) for i in range(n_blocks)]
    n_ahead = n_blocks // 2
    carried = block_term(n_ahead)
    for step in range(2, n_ahead + 1):
        arrived = lax.ppermute(carried.astype(jnp.bfloat16), ("ctx", "dp"), ahead)
        carried = arrived.astype(jnp.float32) + block_term(n_ahead + 1 - step)
    from_left = lax.ppermute(carried.astype(jnp.bfloat16), ("ctx", "dp"), ahead)
    n_behind = n_blocks - 1 - n_ahead
    carried = block_term(n_blocks - n_behind)
    for step in range(2, n_behind + 1):
        arrived = lax.ppermute(carried.astype(jnp.bfloat16), ("ctx", "dp"), behind)
        carried = arrived.astype(jnp.float32) + block_term(n_blocks - n_behind - 1 + step)
    from_right = lax.ppermute(carried.astype(jnp.bfloat16), ("ctx", "dp"), behind)
    stacked = block_term(0) + from_left.astype(jnp.float32) + from_right.astype(jnp.float32)
    key_weight_grad = stacked[:, :key_width]
    value_weight_grad = stacked[:, key_width:]
    normed_grad = jnp.stack(
        [
            jnp.einsum("tk,rk->tr", grads_cat, piece, preferred_element_type=jnp.float32)
            for piece in weights
        ],
        axis=1,
    )
    normed_grad = jnp.take(normed_grad, offset_of, axis=1).reshape(tok_rows, -1)
    scaled = normed_grad * norm_gain
    cubed = inverse * inverse * inverse
    hidden_grad = (
        inverse * scaled - inputs * cubed * jnp.mean(scaled * inputs, axis=-1, keepdims=True)
    ).astype(jnp.bfloat16)
    gain_term = jnp.sum(normed_grad * inputs * inverse, axis=0) * grad_scale
    gain_pieces = lax.all_to_all(
        gain_term.reshape(n_blocks, shard_rows), ("ctx", "dp"), 0, 0, tiled=True
    )
    gain_grad = jnp.sum(gain_pieces, axis=0)
    return (hidden_grad[None], query_gradient[None], key_weight_grad, value_weight_grad, gain_grad)


def solution(mesh):
    return jax.shard_map(
        body,
        mesh=mesh,
        in_specs=(
            P(("groups", "dp"), "ctx", None),
            P(),
            P(("ctx", "dp"), None),
            P(("ctx", "dp"), None),
            P(("groups", "dp"), "ctx", None),
            P(("groups", "dp"), "ctx", None),
        ),
        out_specs=(
            P(("groups", "dp"), "ctx", None),
            P(("groups", "dp"), "ctx", None),
            P(("groups", "ctx", "dp"), None),
            P(("groups", "ctx", "dp"), None),
            P(("groups", "ctx", "dp")),
        ),
        check_vma=False,
    )
```
